32 devices in a mesh: lat: 8 (over y, x, core), wave: 4 (over z).
Axes of the slice: x: 2, y: 2, z: 4, core: 2. Of those that a mesh axis runs over, the one named last changes fastest.
Arguments:
- arnoldi_block: float32 [32, 4, 18, 2048], P(('lat', 'wave')), may hold values from -6 to 6
- legendre: bfloat16 [32, 2048, 2048], P(('lat', 'wave')), may hold values from -0.125 to 0.125
- wave_index: int32 [32], replicated, may hold values from 0 to 2047, as said below
- lat_index: int32 [2048], replicated, may hold values from 0 to 2047, each once
- quad_weight: float32 [2048], replicated, may hold values from 0.5 to 2
- zonal_flow: float32 [3, 2048], replicated, may hold values from -1 to 1
- layer_depth: float32 [3, 2048], replicated, may hold values from 0.3 to 3
- tide_height: float32 [2048, 4096], P(('lat', 'wave')), may hold values from -6 to 6
- mode_to_layer: float32 [3, 3], replicated, as said below
- layer_to_mode: float32 [3, 3], replicated, as said below
- mode_speed: float32 [3], replicated, may hold values from 0.3 to 3
Outputs:
- new_block: float32 [32, 4, 18, 2048], P(('lat', 'wave'))
- hessenberg: float32 [4, 4], replicated
- subdiagonal: float32 [4], replicated
The draws below stay inside these ranges and needn't reach their ends.
Inputs may be any that keep to these rules, and one draw needn't show every extreme that they name: `wave_index`: 32 distinct wavenumbers, 0 and 2047 among them. `lat_index`: each row number once. `mode_to_layer`: diagonal entries 0.8 to 1.2, others within 0.35; drawn independently of layer_to_mode. `layer_to_mode`: diagonal entries 0.8 to 1.2, others within 0.35; drawn independently of mode_to_layer.
All inputs are finite; a program needn't handle non-finite values.
Results may differ from the reference program's by a relative error of at most 0.0065.
Values may be sent and summed in bfloat16 or wider, within the bound.
No kernel may reach another device: no remote copies, remote signals or barrier semaphores. Data moves between devices by JAX's collectives and lax.ppermute only.
A program may use at most 64 MiB of HBM per device.

```python
import math
import jax
import jax.numpy as jnp
from jax import lax

NLAT = 2048
NDEG = 2048
NLON = 4096
LAYERS = 3
VEC = 4
STEPS = 3
MW = 32
NTRUNC = 2047
CHAN = 18


def draw_wave_index(key, part):
    shuffled = jax.random.permutation(key, NTRUNC - 1).astype(jnp.int32) + 1
    chosen = jnp.concatenate([jnp.array([0, NTRUNC], dtype=jnp.int32), shuffled[:MW - 2]])
    order = jax.random.permutation(jax.random.fold_in(key, 7), MW)
    return chosen[order]


def mode_matrix(key):
    diagonal_part = jax.random.uniform(jax.random.fold_in(key, 1), (LAYERS,), jnp.float32, 0.8, 1.2)
    others = jax.random.uniform(jax.random.fold_in(key, 2), (LAYERS, LAYERS), jnp.float32, -0.35, 0.35)
    identity = jnp.eye(LAYERS, dtype=jnp.float32)
    return identity * diagonal_part[:, None] + others * (1.0 - identity)


def draw_mode_to_layer(key, part):
    return mode_matrix(jax.random.fold_in(key, 11))


def draw_layer_to_mode(key, part):
    return mode_matrix(jax.random.fold_in(key, 23))


def block_levels(own_key, extent, cuts, low, top_value):
    gain, own = 1.0, jax.random.fold_in(own_key, 6)
    for dim, shards_of in cuts:
        steps = jnp.exp(jax.random.uniform(jax.random.fold_in(own, dim), (shards_of,), jnp.float32, low / len(cuts), top_value / len(cuts)))
        gain = gain * jnp.repeat(steps, extent[dim] // shards_of).reshape([-1 if axis == dim else 1 for axis in range(len(extent))])
    return gain


def centred(stream_key, dims, width, reach, cuts=(), held_as=jnp.bfloat16):
    values = width * jax.random.normal(stream_key, dims, jnp.float32)
    if cuts:
        values = values * block_levels(stream_key, dims, cuts, -0.22, 0.18)
    return jnp.clip(values, -reach, reach).astype(held_as)


def setup_inputs(seed: int = 0) -> dict:
    keys = jax.random.split(jax.random.key(seed), 12)
    arnoldi_block = centred(keys[0], (MW, VEC, CHAN, NDEG), 1.0, 6.0, ((0, 32),), jnp.float32)
    legendre = centred(keys[1], (MW, NLAT, NDEG), NDEG ** -0.5, 0.125, ((0, 32),))
    wave_index = draw_wave_index(jax.random.fold_in(keys[11], 71), 0)
    lat_index = jax.random.permutation(keys[3], NLAT).astype(jnp.int32)
    quad_weight = jnp.clip(jnp.exp(jax.random.uniform(keys[4], (NLAT,), jnp.float32, math.log(0.5), math.log(2.0))), 0.5, 2.0)
    zonal_flow = jnp.clip(jax.random.uniform(keys[5], (LAYERS, NLAT), jnp.float32, -1.0, 1.0), -1.0, 1.0)
    layer_depth = jnp.clip(jnp.exp(jax.random.uniform(keys[6], (LAYERS, NLAT), jnp.float32, math.log(0.3), math.log(3.0))), 0.3, 3.0)
    tide_height = centred(keys[7], (NLAT, NLON), 1.0, 6.0, ((0, 32),), jnp.float32)
    mode_to_layer = draw_mode_to_layer(jax.random.fold_in(keys[11], 71), 0)
    layer_to_mode = draw_layer_to_mode(jax.random.fold_in(keys[11], 71), 0)
    mode_speed = jnp.clip(jnp.exp(jax.random.uniform(keys[10], (LAYERS,), jnp.float32, math.log(0.3), math.log(3.0))), 0.3, 3.0)
    return {"arnoldi_block": arnoldi_block, "legendre": legendre, "wave_index": wave_index, "lat_index": lat_index, "quad_weight": quad_weight, "zonal_flow": zonal_flow, "layer_depth": layer_depth, "tide_height": tide_height, "mode_to_layer": mode_to_layer, "layer_to_mode": layer_to_mode, "mode_speed": mode_speed}


HIGHEST_PRECISION = lax.Precision.HIGHEST

def angle_tables(wave_ids, nlon):
    lon_steps = jnp.arange(nlon, dtype=jnp.int32)
    phase = wave_ids[:, None] * lon_steps[None, :] % nlon
    theta = phase.astype(jnp.float32) * (2.0 * math.pi / nlon)
    return jnp.concatenate([jnp.cos(theta), jnp.sin(theta)], axis=0)

def tide_term(div_real, div_imag, tide_rows, tables):
    stacked = jnp.concatenate([div_real, -div_imag], axis=0)
    field = jnp.einsum('sikb,sl->ikbl', stacked, tables, precision=HIGHEST_PRECISION)
    product = field * tide_rows[None, None, :, :]
    folded = jnp.einsum('ikbl,sl->sikb', product, tables, precision=HIGHEST_PRECISION) * (2.0 / tables.shape[1])
    slots = div_real.shape[0]
    return (folded[:slots], -folded[slots:])

def tendency(grid_values, advect, coriolis, depth_rows, tide_real, tide_imag):
    vort_re = grid_values[:, :, :, 0, :]
    vort_im = grid_values[:, :, :, 1, :]
    div_re = grid_values[:, :, :, 2, :]
    div_im = grid_values[:, :, :, 3, :]
    height_re = grid_values[:, :, :, 4, :]
    height_im = grid_values[:, :, :, 5, :]
    depth_b = depth_rows[None, None, :, :]
    parts = [advect * vort_im - coriolis * div_re, -advect * vort_re - coriolis * div_im, advect * div_im + coriolis * vort_re, -advect * div_re + coriolis * vort_im, advect * height_im - depth_b * div_re - tide_real, -advect * height_re - depth_b * div_im - tide_imag]
    return jnp.stack(parts, axis=3)

def implicit_step(explicit, wave_ids, mode_to_layer, layer_to_mode, mode_speed, ntrunc):
    degrees = wave_ids[:, None] + jnp.arange(explicit.shape[-1], dtype=jnp.int32)[None, :]
    degree_f = degrees.astype(jnp.float32)
    laplace = (degree_f * (degree_f + 1.0) / float(ntrunc * ntrunc))[:, None, None, None, :]
    speeds = mode_speed[None, None, :, None, None]
    div_modes = jnp.einsum('pk,svkrj->svprj', layer_to_mode, explicit[:, :, :, 2:4, :], precision=HIGHEST_PRECISION)
    height_modes = jnp.einsum('pk,svkrj->svprj', layer_to_mode, explicit[:, :, :, 4:6, :], precision=HIGHEST_PRECISION)
    div_new = (div_modes + laplace * speeds * height_modes) / (1.0 + laplace * speeds * speeds)
    height_new = height_modes - speeds * div_new
    div_layers = jnp.einsum('kp,svprj->svkrj', mode_to_layer, div_new, precision=HIGHEST_PRECISION)
    height_layers = jnp.einsum('kp,svprj->svkrj', mode_to_layer, height_new, precision=HIGHEST_PRECISION)
    return jnp.concatenate([explicit[:, :, :, 0:2, :], div_layers, height_layers], axis=3)

def reference(arnoldi_block, legendre, wave_index, lat_index, quad_weight, zonal_flow, layer_depth, tide_height, mode_to_layer, layer_to_mode, mode_speed):
    degrees = wave_index[:, None] + jnp.arange(NDEG, dtype=jnp.int32)[None, :]
    truncation = (degrees <= NTRUNC).astype(jnp.float32)[:, None, None, :]
    basis = arnoldi_block * truncation
    tables = angle_tables(wave_index, NLON)
    wave_float = wave_index.astype(jnp.float32)
    advect = wave_float[:, None, None, None] * zonal_flow[None, None, :, :] / NTRUNC
    coriolis = (2 * lat_index + 1).astype(jnp.float32) / NLAT - 1.0
    block_count = NLAT // 16
    tide_blocks = tide_height.reshape(block_count, 16, NLON)

    def synthesize(slot_pair):
        spectral_b, table = slot_pair
        return jnp.einsum('vcj,lj->vcl', spectral_b.astype(jnp.float32), table.astype(jnp.float32)).astype(jnp.bfloat16)

    def analyse(slot_pair):
        weighted_b, table = slot_pair
        return jnp.einsum('vcl,lj->vcj', weighted_b.astype(jnp.float32), table.astype(jnp.float32))

    def tide_block(block_pair):
        divergence, tide_rows = block_pair
        real_part, imag_part = tide_term(divergence[:, :, :, 0, :], divergence[:, :, :, 1, :], tide_rows, tables)
        return jnp.stack([real_part, imag_part], axis=3)
    spectral = basis
    for step_index in range(STEPS):
        spectral_b = spectral.astype(jnp.bfloat16)
        grid_b = lax.map(synthesize, (spectral_b, legendre))
        grid_values = grid_b.astype(jnp.float32).reshape(MW, VEC, LAYERS, 6, NLAT)
        divergence = grid_values[:, :, :, 2:4, :].reshape(MW, VEC, LAYERS, 2, block_count, 16)
        divergence = jnp.moveaxis(divergence, 4, 0)
        tide_parts = lax.map(tide_block, (divergence, tide_blocks))
        tide_parts = jnp.moveaxis(tide_parts, 0, 4).reshape(MW, VEC, LAYERS, 2, NLAT)
        tendencies = tendency(grid_values, advect, coriolis, layer_depth, tide_parts[:, :, :, 0, :], tide_parts[:, :, :, 1, :])
        weighted = (quad_weight * tendencies).astype(jnp.bfloat16).reshape(MW, VEC, CHAN, NLAT)
        analysed = lax.map(analyse, (weighted, legendre)) * truncation
        explicit = (spectral + analysed).reshape(MW, VEC, LAYERS, 6, NDEG)
        spectral = implicit_step(explicit, wave_index, mode_to_layer, layer_to_mode, mode_speed, NTRUNC).reshape(MW, VEC, CHAN, NDEG) * truncation
    entries = float(MW * CHAN * NDEG)
    hessenberg = jnp.einsum('skcj,svcj->kv', basis, spectral, precision=HIGHEST_PRECISION) / entries
    residual = spectral - jnp.einsum('skcj,kv->svcj', basis, hessenberg, precision=HIGHEST_PRECISION)
    norm_sq = lax.optimization_barrier(jnp.sum(residual * residual, axis=(0, 2, 3))) / entries
    subdiagonal = jnp.sqrt(norm_sq + 1e-06)
    return (residual / subdiagonal[None, :, None, None], hessenberg, subdiagonal)
```

```python
import math

import jax
import jax.numpy as jnp
from jax import lax
from jax.sharding import PartitionSpec as P

STEPS = 3


HIGHEST_PRECISION = lax.Precision.HIGHEST


def angle_tables(wave_ids, nlon):
    lon_steps = jnp.arange(nlon, dtype=jnp.int32)
    phase = wave_ids[:, None] * lon_steps[None, :] % nlon
    theta = phase.astype(jnp.float32) * (2.0 * math.pi / nlon)
    return jnp.concatenate([jnp.cos(theta), jnp.sin(theta)], axis=0)


def tide_term(div_real, div_imag, tide_rows, tables, tables_upper, tables_lower):
    slots, items, lays, rows = div_real.shape
    nlon = tables.shape[1]
    stacked = jnp.concatenate([div_real, -div_imag], axis=0).reshape(2 * slots, items * lays * rows)
    lead_dims = (((0,), (0,)), ((), ()))
    field = lax.dot_general(stacked, tables_upper, lead_dims, preferred_element_type=jnp.float32)
    field = field + lax.dot_general(
        stacked, tables_lower, lead_dims, preferred_element_type=jnp.float32
    )
    product = field.reshape(items * lays, rows, nlon) * tide_rows[None, :, :]
    product = product.reshape(items * lays * rows, nlon)
    last_dims = (((1,), (1,)), ((), ()))
    folded = lax.dot_general(
        tables, product, last_dims, precision=lax.Precision.HIGH, preferred_element_type=jnp.float32
    ) * (2.0 / nlon)
    folded = folded.reshape(2 * slots, items, lays, rows)
    return (folded[:slots], -folded[slots:])


def tendency(grid_values, advect, coriolis, depth_rows, tide_real, tide_imag):
    vort_re = grid_values[:, :, :, 0, :]
    vort_im = grid_values[:, :, :, 1, :]
    div_re = grid_values[:, :, :, 2, :]
    div_im = grid_values[:, :, :, 3, :]
    height_re = grid_values[:, :, :, 4, :]
    height_im = grid_values[:, :, :, 5, :]
    depth_b = depth_rows[None, None, :, :]
    parts = [
        advect * vort_im - coriolis * div_re,
        -advect * vort_re - coriolis * div_im,
        advect * div_im + coriolis * vort_re,
        -advect * div_re + coriolis * vort_im,
        advect * height_im - depth_b * div_re - tide_real,
        -advect * height_re - depth_b * div_im - tide_imag,
    ]
    return jnp.stack(parts, axis=3)


def implicit_step(explicit, wave_ids, mode_to_layer, layer_to_mode, mode_speed, ntrunc):
    degrees = wave_ids[:, None] + jnp.arange(explicit.shape[-1], dtype=jnp.int32)[None, :]
    degree_f = degrees.astype(jnp.float32)
    laplace = (degree_f * (degree_f + 1.0) / float(ntrunc * ntrunc))[:, None, None, None, :]
    speeds = mode_speed[None, None, :, None, None]
    div_modes = jnp.einsum(
        "pk,svkrj->svprj", layer_to_mode, explicit[:, :, :, 2:4, :], precision=HIGHEST_PRECISION
    )
    height_modes = jnp.einsum(
        "pk,svkrj->svprj", layer_to_mode, explicit[:, :, :, 4:6, :], precision=HIGHEST_PRECISION
    )
    div_new = (div_modes + laplace * speeds * height_modes) / (1.0 + laplace * speeds * speeds)
    height_new = height_modes - speeds * div_new
    div_layers = jnp.einsum("kp,svprj->svkrj", mode_to_layer, div_new, precision=HIGHEST_PRECISION)
    height_layers = jnp.einsum(
        "kp,svprj->svkrj", mode_to_layer, height_new, precision=HIGHEST_PRECISION
    )
    return jnp.concatenate([explicit[:, :, :, 0:2, :], div_layers, height_layers], axis=3)


def exchange_sum(parts, device_count):
    flat = jnp.concatenate([p.reshape(-1) for p in parts])
    rows = jnp.broadcast_to(flat[None, :], (device_count, flat.shape[0]))
    gathered = lax.all_to_all(rows, ("lat", "wave"), 0, 0, tiled=True)
    total = jnp.sum(gathered, axis=0)
    out, start = [], 0
    for p in parts:
        out.append(total[start:start + p.size].reshape(p.shape))
        start += p.size
    return tuple(out)


def on_device(
    arnoldi_block,
    legendre,
    wave_index,
    lat_index,
    quad_weight,
    zonal_flow,
    layer_depth,
    tide_height,
    mode_to_layer,
    layer_to_mode,
    mode_speed,
):
    local_slots = arnoldi_block.shape[0]
    vectors = arnoldi_block.shape[1]
    channels = arnoldi_block.shape[2]
    nlat = legendre.shape[1]
    ndeg = legendre.shape[2]
    ntrunc = ndeg - 1
    layers = mode_speed.shape[0]
    band_rows = tide_height.shape[0]
    device_count = lax.axis_size("lat") * lax.axis_size("wave")
    device_rank = lax.axis_index("lat") * lax.axis_size("wave") + lax.axis_index("wave")
    all_slots = wave_index.shape[0]
    local_waves = lax.dynamic_slice_in_dim(wave_index, device_rank * local_slots, local_slots)
    degrees = local_waves[:, None] + jnp.arange(ndeg, dtype=jnp.int32)[None, :]
    truncation = (degrees <= ntrunc).astype(jnp.float32)[:, None, None, :]
    basis = arnoldi_block * truncation
    tables = angle_tables(wave_index, tide_height.shape[1])
    tables_upper = tables.astype(jnp.bfloat16)
    tables_lower = (tables - tables_upper.astype(jnp.float32)).astype(jnp.bfloat16)
    coriolis_all = (2 * lat_index + 1).astype(jnp.float32) / nlat - 1.0
    band_start = device_rank * band_rows
    band_flow = lax.dynamic_slice_in_dim(zonal_flow, band_start, band_rows, 1)
    band_depth = lax.dynamic_slice_in_dim(layer_depth, band_start, band_rows, 1)
    band_coriolis = lax.dynamic_slice_in_dim(coriolis_all, band_start, band_rows)
    band_weight = lax.dynamic_slice_in_dim(quad_weight, band_start, band_rows)
    band_advect = (
        wave_index.astype(jnp.float32)[:, None, None, None] * band_flow[None, None, :, :] / ntrunc
    )
    spectral = basis
    for step_index in range(STEPS):
        spectral_b = spectral.astype(jnp.bfloat16)
        grid_b = jnp.einsum(
            "svcj,slj->svcl", spectral_b, legendre, preferred_element_type=jnp.float32
        ).astype(jnp.bfloat16)
        received = lax.all_to_all(grid_b, ("lat", "wave"), split_axis=3, concat_axis=0, tiled=True)
        items = received.shape[1]
        grid_split = received.reshape(all_slots, items, layers, 6, band_rows)
        grid_values = grid_split.astype(jnp.float32)
        tide_real, tide_imag = tide_term(
            grid_split[:, :, :, 2, :],
            grid_split[:, :, :, 3, :],
            tide_height,
            tables,
            tables_upper,
            tables_lower,
        )
        tendencies = tendency(
            grid_values, band_advect, band_coriolis, band_depth, tide_real, tide_imag
        )
        weighted = (
            (band_weight * tendencies)
            .astype(jnp.bfloat16)
            .reshape(all_slots, items, channels, band_rows)
        )
        returned = lax.all_to_all(
            weighted, ("lat", "wave"), split_axis=0, concat_axis=3, tiled=True
        )
        analysed = jnp.einsum(
            "svcl,slj->svcj", returned, legendre, preferred_element_type=jnp.float32
        )
        analysed = analysed * truncation
        explicit = (spectral + analysed).reshape(local_slots, vectors, layers, 6, ndeg)
        spectral = (
            implicit_step(
                explicit, local_waves, mode_to_layer, layer_to_mode, mode_speed, ntrunc
            ).reshape(local_slots, vectors, channels, ndeg)
            * truncation
        )
    entries = float(local_slots * device_count * channels * ndeg)
    local_proj = jnp.einsum("skcj,svcj->kv", basis, spectral, precision=HIGHEST_PRECISION)
    local_self = jnp.sum(spectral * spectral, axis=(0, 2, 3))
    local_gram = jnp.einsum("skcj,sqcj->kq", basis, basis, precision=HIGHEST_PRECISION)
    projection, self_sum, gram = exchange_sum((local_proj, local_self, local_gram), device_count)
    hessenberg = projection / entries
    residual = spectral - jnp.einsum(
        "skcj,kv->svcj", basis, hessenberg, precision=HIGHEST_PRECISION
    )
    quadratic = jnp.einsum("kv,kq,qv->v", hessenberg, gram, hessenberg, precision=HIGHEST_PRECISION)
    norm_sq = (self_sum - 2.0 * jnp.sum(hessenberg * projection, axis=0) + quadratic) / entries
    subdiagonal = jnp.sqrt(norm_sq + 1e-06)
    return (residual / subdiagonal[None, :, None, None], hessenberg, subdiagonal)


def solution(mesh):
    return jax.shard_map(
        on_device,
        mesh=mesh,
        in_specs=(
            P(("lat", "wave"), None, None, None),
            P(("lat", "wave"), None, None),
            P(),
            P(),
            P(),
            P(),
            P(),
            P(("lat", "wave"), None),
            P(),
            P(),
            P(),
        ),
        out_specs=(P(("lat", "wave"), None, None, None), P(), P()),
        check_vma=False,
    )
```

```python
import math

import jax
import jax.numpy as jnp
from jax import lax
from jax.sharding import PartitionSpec as P

STEPS = 3


HIGHEST_PRECISION = lax.Precision.HIGHEST


def angle_tables(wave_ids, nlon):
    lon_steps = jnp.arange(nlon, dtype=jnp.int32)
    phase = wave_ids[:, None] * lon_steps[None, :] % nlon
    theta = phase.astype(jnp.float32) * (2.0 * math.pi / nlon)
    return jnp.concatenate([jnp.cos(theta), jnp.sin(theta)], axis=0)


def tide_term(div_real, div_imag, tide_rows, tables, tables_upper, tables_lower):
    slots, items, lays, rows = div_real.shape
    nlon = tables.shape[1]
    stacked = jnp.concatenate([div_real, -div_imag], axis=0).reshape(2 * slots, items * lays * rows)
    lead_dims = (((0,), (0,)), ((), ()))
    field = lax.dot_general(stacked, tables_upper, lead_dims, preferred_element_type=jnp.float32)
    field = field + lax.dot_general(
        stacked, tables_lower, lead_dims, preferred_element_type=jnp.float32
    )
    product = field.reshape(items * lays, rows, nlon) * tide_rows[None, :, :]
    product = product.reshape(items * lays * rows, nlon)
    last_dims = (((1,), (1,)), ((), ()))
    folded = lax.dot_general(
        tables, product, last_dims, precision=lax.Precision.HIGH, preferred_element_type=jnp.float32
    ) * (2.0 / nlon)
    folded = folded.reshape(2 * slots, items, lays, rows)
    return (folded[:slots], -folded[slots:])


def tendency(grid_values, advect, coriolis, depth_rows, tide_real, tide_imag):
    vort_re = grid_values[:, :, :, 0, :]
    vort_im = grid_values[:, :, :, 1, :]
    div_re = grid_values[:, :, :, 2, :]
    div_im = grid_values[:, :, :, 3, :]
    height_re = grid_values[:, :, :, 4, :]
    height_im = grid_values[:, :, :, 5, :]
    depth_b = depth_rows[None, None, :, :]
    parts = [
        advect * vort_im - coriolis * div_re,
        -advect * vort_re - coriolis * div_im,
        advect * div_im + coriolis * vort_re,
        -advect * div_re + coriolis * vort_im,
        advect * height_im - depth_b * div_re - tide_real,
        -advect * height_re - depth_b * div_im - tide_imag,
    ]
    return jnp.stack(parts, axis=3)


def implicit_step(explicit, wave_ids, mode_to_layer, layer_to_mode, mode_speed, ntrunc):
    degrees = wave_ids[:, None] + jnp.arange(explicit.shape[-1], dtype=jnp.int32)[None, :]
    degree_f = degrees.astype(jnp.float32)
    laplace = (degree_f * (degree_f + 1.0) / float(ntrunc * ntrunc))[:, None, None, None, :]
    speeds = mode_speed[None, None, :, None, None]
    div_modes = jnp.einsum(
        "pk,svkrj->svprj", layer_to_mode, explicit[:, :, :, 2:4, :], precision=HIGHEST_PRECISION
    )
    height_modes = jnp.einsum(
        "pk,svkrj->svprj", layer_to_mode, explicit[:, :, :, 4:6, :], precision=HIGHEST_PRECISION
    )
    div_new = (div_modes + laplace * speeds * height_modes) / (1.0 + laplace * speeds * speeds)
    height_new = height_modes - speeds * div_new
    div_layers = jnp.einsum("kp,svprj->svkrj", mode_to_layer, div_new, precision=HIGHEST_PRECISION)
    height_layers = jnp.einsum(
        "kp,svprj->svkrj", mode_to_layer, height_new, precision=HIGHEST_PRECISION
    )
    return jnp.concatenate([explicit[:, :, :, 0:2, :], div_layers, height_layers], axis=3)


def exchange_sum(parts, device_count):
    flat = jnp.concatenate([p.reshape(-1) for p in parts])
    rows = jnp.broadcast_to(flat[None, :], (device_count, flat.shape[0]))
    gathered = lax.all_to_all(rows, ("lat", "wave"), 0, 0, tiled=True)
    total = jnp.sum(gathered, axis=0)
    out, start = [], 0
    for p in parts:
        out.append(total[start:start + p.size].reshape(p.shape))
        start += p.size
    return tuple(out)


def to_bands(values, device_count, lanes=128):
    ls, vecs, lays, parts, nlat = values.shape
    band = nlat // device_count
    split = values.reshape(ls, vecs, lays, parts, device_count, band)
    split = jnp.transpose(split, (4, 0, 1, 2, 3, 5))
    return split.reshape(device_count, ls * vecs * lays * parts * band // lanes, lanes)


def on_device(
    arnoldi_block,
    legendre,
    wave_index,
    lat_index,
    quad_weight,
    zonal_flow,
    layer_depth,
    tide_height,
    mode_to_layer,
    layer_to_mode,
    mode_speed,
):
    local_slots = arnoldi_block.shape[0]
    vectors = arnoldi_block.shape[1]
    channels = arnoldi_block.shape[2]
    nlat = legendre.shape[1]
    ndeg = legendre.shape[2]
    ntrunc = ndeg - 1
    layers = mode_speed.shape[0]
    band_rows = tide_height.shape[0]
    device_count = lax.axis_size("lat") * lax.axis_size("wave")
    device_rank = lax.axis_index("lat") * lax.axis_size("wave") + lax.axis_index("wave")
    all_slots = wave_index.shape[0]
    axes = ("lat", "wave")
    local_waves = lax.dynamic_slice_in_dim(wave_index, device_rank * local_slots, local_slots)
    degrees = local_waves[:, None] + jnp.arange(ndeg, dtype=jnp.int32)[None, :]
    truncation = (degrees <= ntrunc).astype(jnp.float32)[:, None, None, :]
    basis = arnoldi_block * truncation
    tables = angle_tables(wave_index, tide_height.shape[1])
    tables_upper = tables.astype(jnp.bfloat16)
    tables_lower = (tables - tables_upper.astype(jnp.float32)).astype(jnp.bfloat16)
    coriolis = (2 * lat_index + 1).astype(jnp.float32) / nlat - 1.0
    advect = (
        local_waves.astype(jnp.float32)[:, None, None, None] * zonal_flow[None, None, :, :] / ntrunc
    )
    spectral = basis
    for step_index in range(STEPS):
        spectral_b = spectral.astype(jnp.bfloat16)
        grid_b = jnp.einsum(
            "svcj,slj->svcl", spectral_b, legendre, preferred_element_type=jnp.float32
        ).astype(jnp.bfloat16)
        grid_split = grid_b.reshape(local_slots, vectors, layers, 6, nlat)
        sent = to_bands(grid_split[:, :, :, 2:4, :], device_count)
        received = lax.all_to_all(sent, axes, 0, 0, tiled=True)
        band_div = received.reshape(all_slots, vectors, layers, 2, band_rows)
        tide_real, tide_imag = tide_term(
            band_div[:, :, :, 0, :],
            band_div[:, :, :, 1, :],
            tide_height,
            tables,
            tables_upper,
            tables_lower,
        )
        tide_parts = jnp.stack([tide_real, tide_imag], axis=3)
        back = tide_parts.reshape(device_count, -1, 128)
        returned = lax.all_to_all(back, axes, 0, 0, tiled=True)
        returned = returned.reshape(device_count, local_slots, vectors, layers, 2, band_rows)
        tide_rows = jnp.transpose(returned, (1, 2, 3, 4, 0, 5)).reshape(
            local_slots, vectors, layers, 2, nlat
        )
        tendencies = tendency(
            grid_split.astype(jnp.float32),
            advect,
            coriolis,
            layer_depth,
            tide_rows[:, :, :, 0, :],
            tide_rows[:, :, :, 1, :],
        )
        weighted = (
            (quad_weight * tendencies)
            .astype(jnp.bfloat16)
            .reshape(local_slots, vectors, channels, nlat)
        )
        analysed = jnp.einsum(
            "svcl,slj->svcj", weighted, legendre, preferred_element_type=jnp.float32
        )
        analysed = analysed * truncation
        explicit = (spectral + analysed).reshape(local_slots, vectors, layers, 6, ndeg)
        spectral = (
            implicit_step(
                explicit, local_waves, mode_to_layer, layer_to_mode, mode_speed, ntrunc
            ).reshape(local_slots, vectors, channels, ndeg)
            * truncation
        )
    entries = float(local_slots * device_count * channels * ndeg)
    local_proj = jnp.einsum("skcj,svcj->kv", basis, spectral, precision=HIGHEST_PRECISION)
    local_self = jnp.sum(spectral * spectral, axis=(0, 2, 3))
    local_gram = jnp.einsum("skcj,sqcj->kq", basis, basis, precision=HIGHEST_PRECISION)
    projection, self_sum, gram = exchange_sum((local_proj, local_self, local_gram), device_count)
    hessenberg = projection / entries
    residual = spectral - jnp.einsum(
        "skcj,kv->svcj", basis, hessenberg, precision=HIGHEST_PRECISION
    )
    quadratic = jnp.einsum("kv,kq,qv->v", hessenberg, gram, hessenberg, precision=HIGHEST_PRECISION)
    norm_sq = (self_sum - 2.0 * jnp.sum(hessenberg * projection, axis=0) + quadratic) / entries
    subdiagonal = jnp.sqrt(norm_sq + 1e-06)
    return (residual / subdiagonal[None, :, None, None], hessenberg, subdiagonal)


def solution(mesh):
    return jax.shard_map(
        on_device,
        mesh=mesh,
        in_specs=(
            P(("lat", "wave"), None, None, None),
            P(("lat", "wave"), None, None),
            P(),
            P(),
            P(),
            P(),
            P(),
            P(("lat", "wave"), None),
            P(),
            P(),
            P(),
        ),
        out_specs=(P(("lat", "wave"), None, None, None), P(), P()),
        check_vma=False,
    )
```

```python
import functools
import math

import jax
import jax.numpy as jnp
from jax import lax
from jax.sharding import PartitionSpec as P
from jax.experimental import pallas as pl
from jax.experimental.pallas import tpu as pltpu

STEPS = 3


HIGHEST_PRECISION = lax.Precision.HIGHEST


def angle_tables(wave_ids, nlon):
    lon_steps = jnp.arange(nlon, dtype=jnp.int32)
    phase = wave_ids[:, None] * lon_steps[None, :] % nlon
    theta = phase.astype(jnp.float32) * (2.0 * math.pi / nlon)
    return jnp.concatenate([jnp.cos(theta), jnp.sin(theta)], axis=0)


def tide_kernel(items, rows, lhs_ref, tab_ref, tide_ref, out_ref):
    step = pl.program_id(0)

    @pl.when(step == 0)
    def _():
        out_ref[...] = jnp.zeros_like(out_ref)

    pairs = out_ref.shape[0]
    field = jnp.dot(lhs_ref[...], tab_ref[...], preferred_element_type=jnp.float32)
    width = field.shape[1]
    product = (field.reshape(items, rows, width) * tide_ref[...][None, :, :]).reshape(
        items * rows, width
    )
    product_hi = product.astype(jnp.bfloat16)
    product_lo = (product - product_hi.astype(jnp.float32)).astype(jnp.bfloat16)
    upper = tab_ref[0:pairs, :]
    lower = tab_ref[pairs:2 * pairs, :]
    last_dims = (((1,), (1,)), ((), ()))
    folded = lax.dot_general(upper, product_hi, last_dims, preferred_element_type=jnp.float32)
    folded = folded + lax.dot_general(
        lower, product_hi, last_dims, preferred_element_type=jnp.float32
    )
    folded = folded + lax.dot_general(
        upper, product_lo, last_dims, preferred_element_type=jnp.float32
    )
    out_ref[...] += folded


def tide_term(div_real, div_imag, tide_rows, tables_upper, tables_lower):
    slots, items, lays, rows = div_real.shape
    nlon = tables_upper.shape[1]
    pairs = 2 * slots
    stacked = jnp.concatenate([div_real, -div_imag], axis=0).reshape(pairs, items * lays * rows)
    lhs = jnp.concatenate([stacked, stacked], axis=0).T
    tabs = jnp.concatenate([tables_upper, tables_lower], axis=0)
    block = 512
    mixed = items * lays * rows
    folded = pl.pallas_call(
        functools.partial(tide_kernel, items * lays, rows),
        out_shape=jax.ShapeDtypeStruct((pairs, mixed), jnp.float32),
        grid=(nlon // block,),
        in_specs=[
            pl.BlockSpec((mixed, 2 * pairs), lambda k: (0, 0)),
            pl.BlockSpec((2 * pairs, block), lambda k: (0, k)),
            pl.BlockSpec((rows, block), lambda k: (0, k)),
        ],
        out_specs=pl.BlockSpec((pairs, mixed), lambda k: (0, 0)),
        compiler_params=pltpu.CompilerParams(dimension_semantics=("arbitrary",)),
        cost_estimate=pl.CostEstimate(
            flops=2 * mixed * nlon * (2 * pairs + 3 * pairs),
            transcendentals=0,
            bytes_accessed=2 * pairs * nlon * 2 + rows * nlon * 4 + mixed * 4 * pairs * 2,
        ),
    )(lhs, tabs, tide_rows)
    folded = (folded * (2.0 / nlon)).reshape(pairs, items, lays, rows)
    return (folded[:slots], -folded[slots:])


def tendency(grid_values, advect, coriolis, depth_rows, tide_real, tide_imag):
    vort_re = grid_values[:, :, :, 0, :]
    vort_im = grid_values[:, :, :, 1, :]
    div_re = grid_values[:, :, :, 2, :]
    div_im = grid_values[:, :, :, 3, :]
    height_re = grid_values[:, :, :, 4, :]
    height_im = grid_values[:, :, :, 5, :]
    depth_b = depth_rows[None, None, :, :]
    parts = [
        advect * vort_im - coriolis * div_re,
        -advect * vort_re - coriolis * div_im,
        advect * div_im + coriolis * vort_re,
        -advect * div_re + coriolis * vort_im,
        advect * height_im - depth_b * div_re - tide_real,
        -advect * height_re - depth_b * div_im - tide_imag,
    ]
    return jnp.stack(parts, axis=3)


def implicit_step(explicit, wave_ids, mode_to_layer, layer_to_mode, mode_speed, ntrunc):
    degrees = wave_ids[:, None] + jnp.arange(explicit.shape[-1], dtype=jnp.int32)[None, :]
    degree_f = degrees.astype(jnp.float32)
    laplace = (degree_f * (degree_f + 1.0) / float(ntrunc * ntrunc))[:, None, None, None, :]
    speeds = mode_speed[None, None, :, None, None]
    div_modes = jnp.einsum(
        "pk,svkrj->svprj", layer_to_mode, explicit[:, :, :, 2:4, :], precision=HIGHEST_PRECISION
    )
    height_modes = jnp.einsum(
        "pk,svkrj->svprj", layer_to_mode, explicit[:, :, :, 4:6, :], precision=HIGHEST_PRECISION
    )
    div_new = (div_modes + laplace * speeds * height_modes) / (1.0 + laplace * speeds * speeds)
    height_new = height_modes - speeds * div_new
    div_layers = jnp.einsum("kp,svprj->svkrj", mode_to_layer, div_new, precision=HIGHEST_PRECISION)
    height_layers = jnp.einsum(
        "kp,svprj->svkrj", mode_to_layer, height_new, precision=HIGHEST_PRECISION
    )
    return jnp.concatenate([explicit[:, :, :, 0:2, :], div_layers, height_layers], axis=3)


def exchange_sum(parts, device_count):
    flat = jnp.concatenate([p.reshape(-1) for p in parts])
    rows = jnp.broadcast_to(flat[None, :], (device_count, flat.shape[0]))
    gathered = lax.all_to_all(rows, ("lat", "wave"), 0, 0, tiled=True)
    total = jnp.sum(gathered, axis=0)
    out, start = [], 0
    for p in parts:
        out.append(total[start:start + p.size].reshape(p.shape))
        start += p.size
    return tuple(out)


def to_bands(values, device_count, lanes=128):
    ls, vecs, lays, parts, nlat = values.shape
    band = nlat // device_count
    split = values.reshape(ls, vecs, lays, parts, device_count, band)
    split = jnp.transpose(split, (4, 0, 1, 2, 3, 5))
    return split.reshape(device_count, ls * vecs * lays * parts * band // lanes, lanes)


def on_device(
    arnoldi_block,
    legendre,
    wave_index,
    lat_index,
    quad_weight,
    zonal_flow,
    layer_depth,
    tide_height,
    mode_to_layer,
    layer_to_mode,
    mode_speed,
):
    local_slots = arnoldi_block.shape[0]
    vectors = arnoldi_block.shape[1]
    channels = arnoldi_block.shape[2]
    nlat = legendre.shape[1]
    ndeg = legendre.shape[2]
    ntrunc = ndeg - 1
    layers = mode_speed.shape[0]
    band_rows = tide_height.shape[0]
    device_count = lax.axis_size("lat") * lax.axis_size("wave")
    device_rank = lax.axis_index("lat") * lax.axis_size("wave") + lax.axis_index("wave")
    all_slots = wave_index.shape[0]
    axes = ("lat", "wave")
    local_waves = lax.dynamic_slice_in_dim(wave_index, device_rank * local_slots, local_slots)
    degrees = local_waves[:, None] + jnp.arange(ndeg, dtype=jnp.int32)[None, :]
    truncation = (degrees <= ntrunc).astype(jnp.float32)[:, None, None, :]
    basis = arnoldi_block * truncation
    tables = angle_tables(wave_index, tide_height.shape[1])
    tables_upper = tables.astype(jnp.bfloat16)
    tables_lower = (tables - tables_upper.astype(jnp.float32)).astype(jnp.bfloat16)
    coriolis = (2 * lat_index + 1).astype(jnp.float32) / nlat - 1.0
    advect = (
        local_waves.astype(jnp.float32)[:, None, None, None] * zonal_flow[None, None, :, :] / ntrunc
    )
    spectral = basis
    for step_index in range(STEPS):
        spectral_b = spectral.astype(jnp.bfloat16)
        grid_b = jnp.einsum(
            "svcj,slj->svcl", spectral_b, legendre, preferred_element_type=jnp.float32
        ).astype(jnp.bfloat16)
        grid_split = grid_b.reshape(local_slots, vectors, layers, 6, nlat)
        sent = to_bands(grid_split[:, :, :, 2:4, :], device_count)
        received = lax.all_to_all(sent, axes, 0, 0, tiled=True)
        band_div = received.reshape(all_slots, vectors, layers, 2, band_rows)
        tide_real, tide_imag = tide_term(
            band_div[:, :, :, 0, :],
            band_div[:, :, :, 1, :],
            tide_height,
            tables_upper,
            tables_lower,
        )
        tide_parts = jnp.stack([tide_real, tide_imag], axis=3)
        back = tide_parts.reshape(device_count, -1, 128)
        returned = lax.all_to_all(back, axes, 0, 0, tiled=True)
        returned = returned.reshape(device_count, local_slots, vectors, layers, 2, band_rows)
        tide_rows = jnp.transpose(returned, (1, 2, 3, 4, 0, 5)).reshape(
            local_slots, vectors, layers, 2, nlat
        )
        tendencies = tendency(
            grid_split.astype(jnp.float32),
            advect,
            coriolis,
            layer_depth,
            tide_rows[:, :, :, 0, :],
            tide_rows[:, :, :, 1, :],
        )
        weighted = (
            (quad_weight * tendencies)
            .astype(jnp.bfloat16)
            .reshape(local_slots, vectors, channels, nlat)
        )
        analysed = jnp.einsum(
            "svcl,slj->svcj", weighted, legendre, preferred_element_type=jnp.float32
        )
        analysed = analysed * truncation
        explicit = (spectral + analysed).reshape(local_slots, vectors, layers, 6, ndeg)
        spectral = (
            implicit_step(
                explicit, local_waves, mode_to_layer, layer_to_mode, mode_speed, ntrunc
            ).reshape(local_slots, vectors, channels, ndeg)
            * truncation
        )
    entries = float(local_slots * device_count * channels * ndeg)
    local_proj = jnp.einsum("skcj,svcj->kv", basis, spectral, precision=HIGHEST_PRECISION)
    local_self = jnp.sum(spectral * spectral, axis=(0, 2, 3))
    local_gram = jnp.einsum("skcj,sqcj->kq", basis, basis, precision=HIGHEST_PRECISION)
    projection, self_sum, gram = exchange_sum((local_proj, local_self, local_gram), device_count)
    hessenberg = projection / entries
    residual = spectral - jnp.einsum(
        "skcj,kv->svcj", basis, hessenberg, precision=HIGHEST_PRECISION
    )
    quadratic = jnp.einsum("kv,kq,qv->v", hessenberg, gram, hessenberg, precision=HIGHEST_PRECISION)
    norm_sq = (self_sum - 2.0 * jnp.sum(hessenberg * projection, axis=0) + quadratic) / entries
    subdiagonal = jnp.sqrt(norm_sq + 1e-06)
    return (residual / subdiagonal[None, :, None, None], hessenberg, subdiagonal)


def solution(mesh):
    return jax.shard_map(
        on_device,
        mesh=mesh,
        in_specs=(
            P(("lat", "wave"), None, None, None),
            P(("lat", "wave"), None, None),
            P(),
            P(),
            P(),
            P(),
            P(),
            P(("lat", "wave"), None),
            P(),
            P(),
            P(),
        ),
        out_specs=(P(("lat", "wave"), None, None, None), P(), P()),
        check_vma=False,
    )
```

```python
import functools
import math

import jax
import jax.numpy as jnp
from jax import lax
from jax.sharding import PartitionSpec as P
from jax.experimental import pallas as pl
from jax.experimental.pallas import tpu as pltpu

STEPS = 3


HIGHEST_PRECISION = lax.Precision.HIGHEST


def angle_tables(wave_ids, nlon):
    lon_steps = jnp.arange(nlon, dtype=jnp.int32)
    phase = wave_ids[:, None] * lon_steps[None, :] % nlon
    theta = phase.astype(jnp.float32) * (2.0 * math.pi / nlon)
    return jnp.concatenate([jnp.cos(theta), jnp.sin(theta)], axis=0)


def tide_kernel(items, rows, lhs_ref, tab_ref, both_ref, upper_ref, tide_ref, hi_ref, lo_ref):
    step = pl.program_id(0)

    @pl.when(step == 0)
    def _():
        hi_ref[...] = jnp.zeros_like(hi_ref)
        lo_ref[...] = jnp.zeros_like(lo_ref)

    field = jnp.dot(lhs_ref[...], tab_ref[...], preferred_element_type=jnp.float32)
    width = field.shape[1]
    product = (field.reshape(items, rows, width) * tide_ref[...][None, :, :]).reshape(
        items * rows, width
    )
    product_hi = product.astype(jnp.bfloat16)
    product_lo = (product - product_hi.astype(jnp.float32)).astype(jnp.bfloat16)
    hi_ref[...] += jnp.dot(product_hi, both_ref[...], preferred_element_type=jnp.float32)
    lo_ref[...] += jnp.dot(product_lo, upper_ref[...], preferred_element_type=jnp.float32)


def tide_term(div_real, div_imag, tide_rows, tables_upper, tables_lower):
    slots, items, lays, rows = div_real.shape
    nlon = tables_upper.shape[1]
    pairs = 2 * slots
    stacked = jnp.concatenate([div_real, -div_imag], axis=0).reshape(pairs, items * lays * rows)
    lhs = jnp.concatenate([stacked, stacked], axis=0).T
    tabs = jnp.concatenate([tables_upper, tables_lower], axis=0)
    upper_t = tables_upper.T
    both_t = jnp.concatenate([upper_t, tables_lower.T], axis=1)
    block = 1024
    mixed = items * lays * rows
    hi_part, lo_part = pl.pallas_call(
        functools.partial(tide_kernel, items * lays, rows),
        out_shape=(
            jax.ShapeDtypeStruct((mixed, 2 * pairs), jnp.float32),
            jax.ShapeDtypeStruct((mixed, pairs), jnp.float32),
        ),
        grid=(nlon // block,),
        in_specs=[
            pl.BlockSpec((mixed, 2 * pairs), lambda k: (0, 0)),
            pl.BlockSpec((2 * pairs, block), lambda k: (0, k)),
            pl.BlockSpec((block, 2 * pairs), lambda k: (k, 0)),
            pl.BlockSpec((block, pairs), lambda k: (k, 0)),
            pl.BlockSpec((rows, block), lambda k: (0, k)),
        ],
        out_specs=(
            pl.BlockSpec((mixed, 2 * pairs), lambda k: (0, 0)),
            pl.BlockSpec((mixed, pairs), lambda k: (0, 0)),
        ),
        compiler_params=pltpu.CompilerParams(dimension_semantics=("arbitrary",)),
        cost_estimate=pl.CostEstimate(
            flops=2 * mixed * nlon * (2 * pairs + 3 * pairs),
            transcendentals=0,
            bytes_accessed=5 * pairs * nlon * 2 + rows * nlon * 4 + mixed * 4 * pairs * 3,
        ),
    )(lhs, tabs, both_t, upper_t, tide_rows)
    folded = (hi_part[:, :pairs] + hi_part[:, pairs:] + lo_part) * (2.0 / nlon)
    folded = folded.T.reshape(pairs, items, lays, rows)
    return (folded[:slots], -folded[slots:])


def tendency(grid_values, advect, coriolis, depth_rows, tide_real, tide_imag):
    vort_re = grid_values[:, :, :, 0, :]
    vort_im = grid_values[:, :, :, 1, :]
    div_re = grid_values[:, :, :, 2, :]
    div_im = grid_values[:, :, :, 3, :]
    height_re = grid_values[:, :, :, 4, :]
    height_im = grid_values[:, :, :, 5, :]
    depth_b = depth_rows[None, None, :, :]
    parts = [
        advect * vort_im - coriolis * div_re,
        -advect * vort_re - coriolis * div_im,
        advect * div_im + coriolis * vort_re,
        -advect * div_re + coriolis * vort_im,
        advect * height_im - depth_b * div_re - tide_real,
        -advect * height_re - depth_b * div_im - tide_imag,
    ]
    return jnp.stack(parts, axis=3)


def implicit_step(explicit, wave_ids, mode_to_layer, layer_to_mode, mode_speed, ntrunc):
    degrees = wave_ids[:, None] + jnp.arange(explicit.shape[-1], dtype=jnp.int32)[None, :]
    degree_f = degrees.astype(jnp.float32)
    laplace = (degree_f * (degree_f + 1.0) / float(ntrunc * ntrunc))[:, None, None, None, :]
    speeds = mode_speed[None, None, :, None, None]
    div_modes = jnp.einsum(
        "pk,svkrj->svprj", layer_to_mode, explicit[:, :, :, 2:4, :], precision=HIGHEST_PRECISION
    )
    height_modes = jnp.einsum(
        "pk,svkrj->svprj", layer_to_mode, explicit[:, :, :, 4:6, :], precision=HIGHEST_PRECISION
    )
    div_new = (div_modes + laplace * speeds * height_modes) / (1.0 + laplace * speeds * speeds)
    height_new = height_modes - speeds * div_new
    div_layers = jnp.einsum("kp,svprj->svkrj", mode_to_layer, div_new, precision=HIGHEST_PRECISION)
    height_layers = jnp.einsum(
        "kp,svprj->svkrj", mode_to_layer, height_new, precision=HIGHEST_PRECISION
    )
    return jnp.concatenate([explicit[:, :, :, 0:2, :], div_layers, height_layers], axis=3)


def exchange_sum(parts, device_count):
    flat = jnp.concatenate([p.reshape(-1) for p in parts])
    rows = jnp.broadcast_to(flat[None, :], (device_count, flat.shape[0]))
    gathered = lax.all_to_all(rows, ("lat", "wave"), 0, 0, tiled=True)
    total = jnp.sum(gathered, axis=0)
    out, start = [], 0
    for p in parts:
        out.append(total[start:start + p.size].reshape(p.shape))
        start += p.size
    return tuple(out)


def to_bands(values, device_count, lanes=128):
    ls, vecs, lays, parts, nlat = values.shape
    band = nlat // device_count
    split = values.reshape(ls, vecs, lays, parts, device_count, band)
    split = jnp.transpose(split, (4, 0, 1, 2, 3, 5))
    return split.reshape(device_count, ls * vecs * lays * parts * band // lanes, lanes)


def on_device(
    arnoldi_block,
    legendre,
    wave_index,
    lat_index,
    quad_weight,
    zonal_flow,
    layer_depth,
    tide_height,
    mode_to_layer,
    layer_to_mode,
    mode_speed,
):
    local_slots = arnoldi_block.shape[0]
    vectors = arnoldi_block.shape[1]
    channels = arnoldi_block.shape[2]
    nlat = legendre.shape[1]
    ndeg = legendre.shape[2]
    ntrunc = ndeg - 1
    layers = mode_speed.shape[0]
    band_rows = tide_height.shape[0]
    device_count = lax.axis_size("lat") * lax.axis_size("wave")
    device_rank = lax.axis_index("lat") * lax.axis_size("wave") + lax.axis_index("wave")
    all_slots = wave_index.shape[0]
    axes = ("lat", "wave")
    local_waves = lax.dynamic_slice_in_dim(wave_index, device_rank * local_slots, local_slots)
    degrees = local_waves[:, None] + jnp.arange(ndeg, dtype=jnp.int32)[None, :]
    truncation = (degrees <= ntrunc).astype(jnp.float32)[:, None, None, :]
    basis = arnoldi_block * truncation
    tables = angle_tables(wave_index, tide_height.shape[1])
    tables_upper = tables.astype(jnp.bfloat16)
    tables_lower = (tables - tables_upper.astype(jnp.float32)).astype(jnp.bfloat16)
    coriolis = (2 * lat_index + 1).astype(jnp.float32) / nlat - 1.0
    advect = (
        local_waves.astype(jnp.float32)[:, None, None, None] * zonal_flow[None, None, :, :] / ntrunc
    )
    spectral = basis
    for step_index in range(STEPS):
        spectral_b = spectral.astype(jnp.bfloat16)
        grid_b = jnp.einsum(
            "svcj,slj->svcl", spectral_b, legendre, preferred_element_type=jnp.float32
        ).astype(jnp.bfloat16)
        grid_split = grid_b.reshape(local_slots, vectors, layers, 6, nlat)
        sent = to_bands(grid_split[:, :, :, 2:4, :], device_count)
        received = lax.all_to_all(sent, axes, 0, 0, tiled=True)
        band_div = received.reshape(all_slots, vectors, layers, 2, band_rows)
        tide_real, tide_imag = tide_term(
            band_div[:, :, :, 0, :],
            band_div[:, :, :, 1, :],
            tide_height,
            tables_upper,
            tables_lower,
        )
        tide_parts = jnp.stack([tide_real, tide_imag], axis=3)
        back = tide_parts.reshape(device_count, -1, 128)
        returned = lax.all_to_all(back, axes, 0, 0, tiled=True)
        returned = returned.reshape(device_count, local_slots, vectors, layers, 2, band_rows)
        tide_rows = jnp.transpose(returned, (1, 2, 3, 4, 0, 5)).reshape(
            local_slots, vectors, layers, 2, nlat
        )
        tendencies = tendency(
            grid_split.astype(jnp.float32),
            advect,
            coriolis,
            layer_depth,
            tide_rows[:, :, :, 0, :],
            tide_rows[:, :, :, 1, :],
        )
        weighted = (
            (quad_weight * tendencies)
            .astype(jnp.bfloat16)
            .reshape(local_slots, vectors, channels, nlat)
        )
        analysed = jnp.einsum(
            "svcl,slj->svcj", weighted, legendre, preferred_element_type=jnp.float32
        )
        analysed = analysed * truncation
        explicit = (spectral + analysed).reshape(local_slots, vectors, layers, 6, ndeg)
        spectral = (
            implicit_step(
                explicit, local_waves, mode_to_layer, layer_to_mode, mode_speed, ntrunc
            ).reshape(local_slots, vectors, channels, ndeg)
            * truncation
        )
    entries = float(local_slots * device_count * channels * ndeg)
    local_proj = jnp.einsum("skcj,svcj->kv", basis, spectral, precision=HIGHEST_PRECISION)
    local_self = jnp.sum(spectral * spectral, axis=(0, 2, 3))
    local_gram = jnp.einsum("skcj,sqcj->kq", basis, basis, precision=HIGHEST_PRECISION)
    projection, self_sum, gram = exchange_sum((local_proj, local_self, local_gram), device_count)
    hessenberg = projection / entries
    residual = spectral - jnp.einsum(
        "skcj,kv->svcj", basis, hessenberg, precision=HIGHEST_PRECISION
    )
    quadratic = jnp.einsum("kv,kq,qv->v", hessenberg, gram, hessenberg, precision=HIGHEST_PRECISION)
    norm_sq = (self_sum - 2.0 * jnp.sum(hessenberg * projection, axis=0) + quadratic) / entries
    subdiagonal = jnp.sqrt(norm_sq + 1e-06)
    return (residual / subdiagonal[None, :, None, None], hessenberg, subdiagonal)


def solution(mesh):
    return jax.shard_map(
        on_device,
        mesh=mesh,
        in_specs=(
            P(("lat", "wave"), None, None, None),
            P(("lat", "wave"), None, None),
            P(),
            P(),
            P(),
            P(),
            P(),
            P(("lat", "wave"), None),
            P(),
            P(),
            P(),
        ),
        out_specs=(P(("lat", "wave"), None, None, None), P(), P()),
        check_vma=False,
    )
```

```python
import functools
import math

import jax
import jax.numpy as jnp
from jax import lax
from jax.sharding import PartitionSpec as P
from jax.experimental import pallas as pl
from jax.experimental.pallas import tpu as pltpu

STEPS = 3


HIGHEST_PRECISION = lax.Precision.HIGHEST


def angle_tables(wave_ids, nlon):
    lon_steps = jnp.arange(nlon, dtype=jnp.int32)
    phase = wave_ids[:, None] * lon_steps[None, :] % nlon
    theta = phase.astype(jnp.float32) * (2.0 * math.pi / nlon)
    return jnp.concatenate([jnp.cos(theta), jnp.sin(theta)], axis=0)


def tide_kernel(items, pairs, rows, lhs_ref, tab_ref, tide_ref, hi_ref, lo_ref):
    step = pl.program_id(0)

    @pl.when(step == 0)
    def _():
        hi_ref[...] = jnp.zeros_like(hi_ref)
        lo_ref[...] = jnp.zeros_like(lo_ref)

    field = jnp.dot(lhs_ref[...], tab_ref[...], preferred_element_type=jnp.float32)
    width = field.shape[1]
    product = (field.reshape(items, rows, width) * tide_ref[...][None, :, :]).reshape(
        items * rows, width
    )
    product_hi = product.astype(jnp.bfloat16)
    product_lo = (product - product_hi.astype(jnp.float32)).astype(jnp.bfloat16)
    last_dims = (((1,), (1,)), ((), ()))
    hi_ref[...] += lax.dot_general(
        product_hi, tab_ref[...], last_dims, preferred_element_type=jnp.float32
    )
    lo_ref[...] += lax.dot_general(
        product_lo, tab_ref[0:pairs, :], last_dims, preferred_element_type=jnp.float32
    )


def tide_term(div_real, div_imag, tide_rows, tables_upper, tables_lower):
    slots, items, lays, rows = div_real.shape
    nlon = tables_upper.shape[1]
    pairs = 2 * slots
    stacked = jnp.concatenate([div_real, -div_imag], axis=0).reshape(pairs, items * lays * rows)
    lhs = jnp.concatenate([stacked, stacked], axis=0).T
    tabs = jnp.concatenate([tables_upper, tables_lower], axis=0)
    block = 1024
    mixed = items * lays * rows
    hi_part, lo_part = pl.pallas_call(
        functools.partial(tide_kernel, items * lays, pairs, rows),
        out_shape=(
            jax.ShapeDtypeStruct((mixed, 2 * pairs), jnp.float32),
            jax.ShapeDtypeStruct((mixed, pairs), jnp.float32),
        ),
        grid=(nlon // block,),
        in_specs=[
            pl.BlockSpec((mixed, 2 * pairs), lambda k: (0, 0)),
            pl.BlockSpec((2 * pairs, block), lambda k: (0, k)),
            pl.BlockSpec((rows, block), lambda k: (0, k)),
        ],
        out_specs=(
            pl.BlockSpec((mixed, 2 * pairs), lambda k: (0, 0)),
            pl.BlockSpec((mixed, pairs), lambda k: (0, 0)),
        ),
        compiler_params=pltpu.CompilerParams(dimension_semantics=("arbitrary",)),
        cost_estimate=pl.CostEstimate(
            flops=2 * mixed * nlon * (2 * pairs + 3 * pairs),
            transcendentals=0,
            bytes_accessed=2 * pairs * nlon * 2 + rows * nlon * 4 + mixed * 4 * pairs * 3,
        ),
    )(lhs, tabs, tide_rows)
    folded = (hi_part[:, :pairs] + hi_part[:, pairs:] + lo_part) * (2.0 / nlon)
    folded = folded.T.reshape(pairs, items, lays, rows)
    return (folded[:slots], -folded[slots:])


def tendency(grid_values, advect, coriolis, depth_rows, tide_real, tide_imag):
    vort_re = grid_values[:, :, :, 0, :]
    vort_im = grid_values[:, :, :, 1, :]
    div_re = grid_values[:, :, :, 2, :]
    div_im = grid_values[:, :, :, 3, :]
    height_re = grid_values[:, :, :, 4, :]
    height_im = grid_values[:, :, :, 5, :]
    depth_b = depth_rows[None, None, :, :]
    parts = [
        advect * vort_im - coriolis * div_re,
        -advect * vort_re - coriolis * div_im,
        advect * div_im + coriolis * vort_re,
        -advect * div_re + coriolis * vort_im,
        advect * height_im - depth_b * div_re - tide_real,
        -advect * height_re - depth_b * div_im - tide_imag,
    ]
    return jnp.stack(parts, axis=3)


def implicit_step(explicit, wave_ids, mode_to_layer, layer_to_mode, mode_speed, ntrunc):
    degrees = wave_ids[:, None] + jnp.arange(explicit.shape[-1], dtype=jnp.int32)[None, :]
    degree_f = degrees.astype(jnp.float32)
    laplace = (degree_f * (degree_f + 1.0) / float(ntrunc * ntrunc))[:, None, None, None, :]
    speeds = mode_speed[None, None, :, None, None]
    div_modes = jnp.einsum(
        "pk,svkrj->svprj", layer_to_mode, explicit[:, :, :, 2:4, :], precision=HIGHEST_PRECISION
    )
    height_modes = jnp.einsum(
        "pk,svkrj->svprj", layer_to_mode, explicit[:, :, :, 4:6, :], precision=HIGHEST_PRECISION
    )
    div_new = (div_modes + laplace * speeds * height_modes) / (1.0 + laplace * speeds * speeds)
    height_new = height_modes - speeds * div_new
    div_layers = jnp.einsum("kp,svprj->svkrj", mode_to_layer, div_new, precision=HIGHEST_PRECISION)
    height_layers = jnp.einsum(
        "kp,svprj->svkrj", mode_to_layer, height_new, precision=HIGHEST_PRECISION
    )
    return jnp.concatenate([explicit[:, :, :, 0:2, :], div_layers, height_layers], axis=3)


def exchange_sum(parts, device_count):
    flat = jnp.concatenate([p.reshape(-1) for p in parts])
    rows = jnp.broadcast_to(flat[None, :], (device_count, flat.shape[0]))
    gathered = lax.all_to_all(rows, ("lat", "wave"), 0, 0, tiled=True)
    total = jnp.sum(gathered, axis=0)
    out, start = [], 0
    for p in parts:
        out.append(total[start:start + p.size].reshape(p.shape))
        start += p.size
    return tuple(out)


def to_bands(values, device_count, lanes=128):
    ls, vecs, lays, parts, nlat = values.shape
    band = nlat // device_count
    split = values.reshape(ls, vecs, lays, parts, device_count, band)
    split = jnp.transpose(split, (4, 0, 1, 2, 3, 5))
    return split.reshape(device_count, ls * vecs * lays * parts * band // lanes, lanes)


def on_device(
    arnoldi_block,
    legendre,
    wave_index,
    lat_index,
    quad_weight,
    zonal_flow,
    layer_depth,
    tide_height,
    mode_to_layer,
    layer_to_mode,
    mode_speed,
):
    local_slots = arnoldi_block.shape[0]
    vectors = arnoldi_block.shape[1]
    channels = arnoldi_block.shape[2]
    nlat = legendre.shape[1]
    ndeg = legendre.shape[2]
    ntrunc = ndeg - 1
    layers = mode_speed.shape[0]
    band_rows = tide_height.shape[0]
    device_count = lax.axis_size("lat") * lax.axis_size("wave")
    device_rank = lax.axis_index("lat") * lax.axis_size("wave") + lax.axis_index("wave")
    all_slots = wave_index.shape[0]
    axes = ("lat", "wave")
    local_waves = lax.dynamic_slice_in_dim(wave_index, device_rank * local_slots, local_slots)
    degrees = local_waves[:, None] + jnp.arange(ndeg, dtype=jnp.int32)[None, :]
    truncation = (degrees <= ntrunc).astype(jnp.float32)[:, None, None, :]
    basis = arnoldi_block * truncation
    tables = angle_tables(wave_index, tide_height.shape[1])
    tables_upper = tables.astype(jnp.bfloat16)
    tables_lower = (tables - tables_upper.astype(jnp.float32)).astype(jnp.bfloat16)
    coriolis = (2 * lat_index + 1).astype(jnp.float32) / nlat - 1.0
    advect = (
        local_waves.astype(jnp.float32)[:, None, None, None] * zonal_flow[None, None, :, :] / ntrunc
    )
    spectral = basis
    for step_index in range(STEPS):
        spectral_b = spectral.astype(jnp.bfloat16)
        grid_b = jnp.einsum(
            "svcj,slj->svcl", spectral_b, legendre, preferred_element_type=jnp.float32
        ).astype(jnp.bfloat16)
        grid_split = grid_b.reshape(local_slots, vectors, layers, 6, nlat)
        sent = to_bands(grid_split[:, :, :, 2:4, :], device_count)
        received = lax.all_to_all(sent, axes, 0, 0, tiled=True)
        band_div = received.reshape(all_slots, vectors, layers, 2, band_rows)
        tide_real, tide_imag = tide_term(
            band_div[:, :, :, 0, :],
            band_div[:, :, :, 1, :],
            tide_height,
            tables_upper,
            tables_lower,
        )
        tide_parts = jnp.stack([tide_real, tide_imag], axis=3)
        back = tide_parts.reshape(device_count, -1, 128)
        returned = lax.all_to_all(back, axes, 0, 0, tiled=True)
        returned = returned.reshape(device_count, local_slots, vectors, layers, 2, band_rows)
        tide_rows = jnp.transpose(returned, (1, 2, 3, 4, 0, 5)).reshape(
            local_slots, vectors, layers, 2, nlat
        )
        tendencies = tendency(
            grid_split.astype(jnp.float32),
            advect,
            coriolis,
            layer_depth,
            tide_rows[:, :, :, 0, :],
            tide_rows[:, :, :, 1, :],
        )
        weighted = (
            (quad_weight * tendencies)
            .astype(jnp.bfloat16)
            .reshape(local_slots, vectors, channels, nlat)
        )
        analysed = jnp.einsum(
            "svcl,slj->svcj", weighted, legendre, preferred_element_type=jnp.float32
        )
        analysed = analysed * truncation
        explicit = (spectral + analysed).reshape(local_slots, vectors, layers, 6, ndeg)
        spectral = (
            implicit_step(
                explicit, local_waves, mode_to_layer, layer_to_mode, mode_speed, ntrunc
            ).reshape(local_slots, vectors, channels, ndeg)
            * truncation
        )
    entries = float(local_slots * device_count * channels * ndeg)
    local_proj = jnp.einsum("skcj,svcj->kv", basis, spectral, precision=HIGHEST_PRECISION)
    local_self = jnp.sum(spectral * spectral, axis=(0, 2, 3))
    local_gram = jnp.einsum("skcj,sqcj->kq", basis, basis, precision=HIGHEST_PRECISION)
    projection, self_sum, gram = exchange_sum((local_proj, local_self, local_gram), device_count)
    hessenberg = projection / entries
    residual = spectral - jnp.einsum(
        "skcj,kv->svcj", basis, hessenberg, precision=HIGHEST_PRECISION
    )
    quadratic = jnp.einsum("kv,kq,qv->v", hessenberg, gram, hessenberg, precision=HIGHEST_PRECISION)
    norm_sq = (self_sum - 2.0 * jnp.sum(hessenberg * projection, axis=0) + quadratic) / entries
    subdiagonal = jnp.sqrt(norm_sq + 1e-06)
    return (residual / subdiagonal[None, :, None, None], hessenberg, subdiagonal)


def solution(mesh):
    return jax.shard_map(
        on_device,
        mesh=mesh,
        in_specs=(
            P(("lat", "wave"), None, None, None),
            P(("lat", "wave"), None, None),
            P(),
            P(),
            P(),
            P(),
            P(),
            P(("lat", "wave"), None),
            P(),
            P(),
            P(),
        ),
        out_specs=(P(("lat", "wave"), None, None, None), P(), P()),
        check_vma=False,
    )
```

```python
import functools
import math

import jax
import jax.numpy as jnp
from jax import lax
from jax.sharding import PartitionSpec as P
from jax.experimental import pallas as pl
from jax.experimental.pallas import tpu as pltpu

STEPS = 3


HIGHEST_PRECISION = lax.Precision.HIGHEST


def angle_tables(wave_ids, nlon):
    lon_steps = jnp.arange(nlon, dtype=jnp.int32)
    phase = wave_ids[:, None] * lon_steps[None, :] % nlon
    theta = phase.astype(jnp.float32) * (2.0 * math.pi / nlon)
    return jnp.concatenate([jnp.cos(theta), jnp.sin(theta)], axis=0)


def tide_kernel(items, pairs, rows, lhs_ref, tab_ref, tide_ref, hi_ref, lo_ref):
    step = pl.program_id(0)

    @pl.when(step == 0)
    def _():
        hi_ref[...] = jnp.zeros_like(hi_ref)
        lo_ref[...] = jnp.zeros_like(lo_ref)

    field = jnp.dot(lhs_ref[...], tab_ref[...], preferred_element_type=jnp.float32)
    width = field.shape[1]
    product = (field.reshape(items, rows, width) * tide_ref[...][None, :, :]).reshape(
        items * rows, width
    )
    product_hi = product.astype(jnp.bfloat16)
    product_lo = (product - product_hi.astype(jnp.float32)).astype(jnp.bfloat16)
    last_dims = (((1,), (1,)), ((), ()))
    hi_ref[...] += lax.dot_general(
        product_hi, tab_ref[...], last_dims, preferred_element_type=jnp.float32
    )
    lo_ref[...] += lax.dot_general(
        product_lo, tab_ref[0:pairs, :], last_dims, preferred_element_type=jnp.float32
    )


def tide_term(div_real, div_imag, tide_rows, tables_upper, tables_lower):
    slots, items, lays, rows = div_real.shape
    nlon = tables_upper.shape[1]
    pairs = 2 * slots
    stacked = jnp.concatenate([div_real, -div_imag], axis=0).reshape(pairs, items * lays * rows)
    lhs = jnp.concatenate([stacked, stacked], axis=0).T
    tabs = jnp.concatenate([tables_upper, tables_lower], axis=0)
    block = 1024
    mixed = items * lays * rows
    hi_part, lo_part = pl.pallas_call(
        functools.partial(tide_kernel, items * lays, pairs, rows),
        out_shape=(
            jax.ShapeDtypeStruct((mixed, 2 * pairs), jnp.float32),
            jax.ShapeDtypeStruct((mixed, pairs), jnp.float32),
        ),
        grid=(nlon // block,),
        in_specs=[
            pl.BlockSpec((mixed, 2 * pairs), lambda k: (0, 0)),
            pl.BlockSpec((2 * pairs, block), lambda k: (0, k)),
            pl.BlockSpec((rows, block), lambda k: (0, k)),
        ],
        out_specs=(
            pl.BlockSpec((mixed, 2 * pairs), lambda k: (0, 0)),
            pl.BlockSpec((mixed, pairs), lambda k: (0, 0)),
        ),
        compiler_params=pltpu.CompilerParams(dimension_semantics=("arbitrary",)),
        cost_estimate=pl.CostEstimate(
            flops=2 * mixed * nlon * (2 * pairs + 3 * pairs),
            transcendentals=0,
            bytes_accessed=2 * pairs * nlon * 2 + rows * nlon * 4 + mixed * 4 * pairs * 3,
        ),
    )(lhs, tabs, tide_rows)
    folded = (hi_part[:, :pairs] + hi_part[:, pairs:] + lo_part) * (2.0 / nlon)
    folded = folded.T.reshape(pairs, items, lays, rows)
    return (folded[:slots], -folded[slots:])


def tendency(grid_values, advect, coriolis, depth_rows, tide_real, tide_imag):
    vort_re = grid_values[:, :, :, 0, :]
    vort_im = grid_values[:, :, :, 1, :]
    div_re = grid_values[:, :, :, 2, :]
    div_im = grid_values[:, :, :, 3, :]
    height_re = grid_values[:, :, :, 4, :]
    height_im = grid_values[:, :, :, 5, :]
    depth_b = depth_rows[None, None, :, :]
    parts = [
        advect * vort_im - coriolis * div_re,
        -advect * vort_re - coriolis * div_im,
        advect * div_im + coriolis * vort_re,
        -advect * div_re + coriolis * vort_im,
        advect * height_im - depth_b * div_re - tide_real,
        -advect * height_re - depth_b * div_im - tide_imag,
    ]
    return jnp.stack(parts, axis=3)


def implicit_step(explicit, wave_ids, mode_to_layer, layer_to_mode, mode_speed, ntrunc):
    degrees = wave_ids[:, None] + jnp.arange(explicit.shape[-1], dtype=jnp.int32)[None, :]
    degree_f = degrees.astype(jnp.float32)
    laplace = (degree_f * (degree_f + 1.0) / float(ntrunc * ntrunc))[:, None, None, None, :]
    speeds = mode_speed[None, None, :, None, None]
    div_modes = jnp.einsum(
        "pk,svkrj->svprj", layer_to_mode, explicit[:, :, :, 2:4, :], precision=HIGHEST_PRECISION
    )
    height_modes = jnp.einsum(
        "pk,svkrj->svprj", layer_to_mode, explicit[:, :, :, 4:6, :], precision=HIGHEST_PRECISION
    )
    div_new = (div_modes + laplace * speeds * height_modes) / (1.0 + laplace * speeds * speeds)
    height_new = height_modes - speeds * div_new
    div_layers = jnp.einsum("kp,svprj->svkrj", mode_to_layer, div_new, precision=HIGHEST_PRECISION)
    height_layers = jnp.einsum(
        "kp,svprj->svkrj", mode_to_layer, height_new, precision=HIGHEST_PRECISION
    )
    return jnp.concatenate([explicit[:, :, :, 0:2, :], div_layers, height_layers], axis=3)


def exchange_sum(parts, device_count):
    flat = jnp.concatenate([p.reshape(-1) for p in parts])
    rows = jnp.broadcast_to(flat[None, :], (device_count, flat.shape[0]))
    gathered = lax.all_to_all(rows, ("lat", "wave"), 0, 0, tiled=True)
    total = jnp.sum(gathered, axis=0)
    out, start = [], 0
    for p in parts:
        out.append(total[start:start + p.size].reshape(p.shape))
        start += p.size
    return tuple(out)


def to_bands(values, device_count, lanes=128):
    ls, vecs, lays, parts, nlat = values.shape
    band = nlat // device_count
    split = values.reshape(ls, vecs, lays, parts, device_count, band)
    split = jnp.transpose(split, (4, 0, 1, 2, 3, 5))
    return split.reshape(device_count, ls * vecs * lays * parts * band // lanes, lanes)


def on_device(
    arnoldi_block,
    legendre,
    wave_index,
    lat_index,
    quad_weight,
    zonal_flow,
    layer_depth,
    tide_height,
    mode_to_layer,
    layer_to_mode,
    mode_speed,
):
    local_slots = arnoldi_block.shape[0]
    vectors = arnoldi_block.shape[1]
    channels = arnoldi_block.shape[2]
    nlat = legendre.shape[1]
    ndeg = legendre.shape[2]
    ntrunc = ndeg - 1
    layers = mode_speed.shape[0]
    band_rows = tide_height.shape[0]
    device_count = lax.axis_size("lat") * lax.axis_size("wave")
    device_rank = lax.axis_index("lat") * lax.axis_size("wave") + lax.axis_index("wave")
    all_slots = wave_index.shape[0]
    axes = ("lat", "wave")
    local_waves = lax.dynamic_slice_in_dim(wave_index, device_rank * local_slots, local_slots)
    degrees = local_waves[:, None] + jnp.arange(ndeg, dtype=jnp.int32)[None, :]
    truncation = (degrees <= ntrunc).astype(jnp.float32)[:, None, None, :]
    basis = arnoldi_block * truncation
    tables = angle_tables(wave_index, tide_height.shape[1])
    tables_upper = tables.astype(jnp.bfloat16)
    tables_lower = (tables - tables_upper.astype(jnp.float32)).astype(jnp.bfloat16)
    coriolis = (2 * lat_index + 1).astype(jnp.float32) / nlat - 1.0
    advect = (
        local_waves.astype(jnp.float32)[:, None, None, None] * zonal_flow[None, None, :, :] / ntrunc
    )
    spectral = basis
    for step_index in range(STEPS):
        spectral_b = spectral.astype(jnp.bfloat16).reshape(local_slots, vectors, layers, 6, ndeg)
        grid_div = jnp.einsum(
            "svaqj,slj->svaql", spectral_b[:, :, :, 2:4, :], legendre,
            preferred_element_type=jnp.float32,
        ).astype(jnp.bfloat16)
        sent = to_bands(grid_div, device_count)
        received = lax.all_to_all(sent, axes, 0, 0, tiled=True)
        other_b = jnp.concatenate([spectral_b[:, :, :, 0:2, :], spectral_b[:, :, :, 4:6, :]], axis=3)
        grid_other = jnp.einsum(
            "svaqj,slj->svaql", other_b, legendre, preferred_element_type=jnp.float32
        ).astype(jnp.bfloat16)
        vort_re = grid_other[:, :, :, 0, :].astype(jnp.float32)
        vort_im = grid_other[:, :, :, 1, :].astype(jnp.float32)
        height_re = grid_other[:, :, :, 2, :].astype(jnp.float32)
        height_im = grid_other[:, :, :, 3, :].astype(jnp.float32)
        div_re = grid_div[:, :, :, 0, :].astype(jnp.float32)
        div_im = grid_div[:, :, :, 1, :].astype(jnp.float32)
        free_parts = jnp.stack(
            [
                advect * vort_im - coriolis * div_re,
                -advect * vort_re - coriolis * div_im,
                advect * div_im + coriolis * vort_re,
                -advect * div_re + coriolis * vort_im,
            ],
            axis=3,
        )
        free_weighted = (quad_weight * free_parts).astype(jnp.bfloat16)
        free_analysed = jnp.einsum(
            "svaql,slj->svaqj", free_weighted, legendre, preferred_element_type=jnp.float32
        )
        band_div = received.reshape(all_slots, vectors, layers, 2, band_rows)
        tide_real, tide_imag = tide_term(
            band_div[:, :, :, 0, :],
            band_div[:, :, :, 1, :],
            tide_height,
            tables_upper,
            tables_lower,
        )
        tide_parts = jnp.stack([tide_real, tide_imag], axis=3)
        back = tide_parts.reshape(device_count, -1, 128)
        returned = lax.all_to_all(back, axes, 0, 0, tiled=True)
        returned = returned.reshape(device_count, local_slots, vectors, layers, 2, band_rows)
        tide_rows = jnp.transpose(returned, (1, 2, 3, 4, 0, 5)).reshape(
            local_slots, vectors, layers, 2, nlat
        )
        depth_b = layer_depth[None, None, :, :]
        height_parts = jnp.stack(
            [
                advect * height_im - depth_b * div_re - tide_rows[:, :, :, 0, :],
                -advect * height_re - depth_b * div_im - tide_rows[:, :, :, 1, :],
            ],
            axis=3,
        )
        height_weighted = (quad_weight * height_parts).astype(jnp.bfloat16)
        height_analysed = jnp.einsum(
            "svaql,slj->svaqj", height_weighted, legendre, preferred_element_type=jnp.float32
        )
        analysed = jnp.concatenate([free_analysed, height_analysed], axis=3)
        analysed = analysed.reshape(local_slots, vectors, channels, ndeg) * truncation
        explicit = (spectral + analysed).reshape(local_slots, vectors, layers, 6, ndeg)
        spectral = (
            implicit_step(
                explicit, local_waves, mode_to_layer, layer_to_mode, mode_speed, ntrunc
            ).reshape(local_slots, vectors, channels, ndeg)
            * truncation
        )
    entries = float(local_slots * device_count * channels * ndeg)
    local_proj = jnp.einsum("skcj,svcj->kv", basis, spectral, precision=HIGHEST_PRECISION)
    local_self = jnp.sum(spectral * spectral, axis=(0, 2, 3))
    local_gram = jnp.einsum("skcj,sqcj->kq", basis, basis, precision=HIGHEST_PRECISION)
    projection, self_sum, gram = exchange_sum((local_proj, local_self, local_gram), device_count)
    hessenberg = projection / entries
    residual = spectral - jnp.einsum(
        "skcj,kv->svcj", basis, hessenberg, precision=HIGHEST_PRECISION
    )
    quadratic = jnp.einsum("kv,kq,qv->v", hessenberg, gram, hessenberg, precision=HIGHEST_PRECISION)
    norm_sq = (self_sum - 2.0 * jnp.sum(hessenberg * projection, axis=0) + quadratic) / entries
    subdiagonal = jnp.sqrt(norm_sq + 1e-06)
    return (residual / subdiagonal[None, :, None, None], hessenberg, subdiagonal)


def solution(mesh):
    return jax.shard_map(
        on_device,
        mesh=mesh,
        in_specs=(
            P(("lat", "wave"), None, None, None),
            P(("lat", "wave"), None, None),
            P(),
            P(),
            P(),
            P(),
            P(),
            P(("lat", "wave"), None),
            P(),
            P(),
            P(),
        ),
        out_specs=(P(("lat", "wave"), None, None, None), P(), P()),
        check_vma=False,
    )
```

```python
import functools
import math

import jax
import jax.numpy as jnp
from jax import lax
from jax.sharding import PartitionSpec as P
from jax.experimental import pallas as pl
from jax.experimental.pallas import tpu as pltpu

STEPS = 3


HIGHEST_PRECISION = lax.Precision.HIGHEST


def angle_tables(wave_ids, nlon):
    lon_steps = jnp.arange(nlon, dtype=jnp.int32)
    phase = wave_ids[:, None] * lon_steps[None, :] % nlon
    theta = phase.astype(jnp.float32) * (2.0 * math.pi / nlon)
    return jnp.concatenate([jnp.cos(theta), jnp.sin(theta)], axis=0)


def tide_kernel(items, pairs, rows, lhs_ref, tab_ref, tide_ref, hi_ref, lo_ref):
    step = pl.program_id(0)

    @pl.when(step == 0)
    def _():
        hi_ref[...] = jnp.zeros_like(hi_ref)
        lo_ref[...] = jnp.zeros_like(lo_ref)

    field = jnp.dot(lhs_ref[...], tab_ref[...], preferred_element_type=jnp.float32)
    width = field.shape[1]
    product = (field.reshape(items, rows, width) * tide_ref[...][None, :, :]).reshape(
        items * rows, width
    )
    product_hi = product.astype(jnp.bfloat16)
    product_lo = (product - product_hi.astype(jnp.float32)).astype(jnp.bfloat16)
    last_dims = (((1,), (1,)), ((), ()))
    hi_ref[...] += lax.dot_general(
        product_hi, tab_ref[...], last_dims, preferred_element_type=jnp.float32
    )
    lo_ref[...] += lax.dot_general(
        product_lo, tab_ref[0:pairs, :], last_dims, preferred_element_type=jnp.float32
    )


def tide_term(div_real, div_imag, tide_rows, tables_upper, tables_lower):
    slots, items, lays, rows = div_real.shape
    nlon = tables_upper.shape[1]
    pairs = 2 * slots
    stacked = jnp.concatenate([div_real, -div_imag], axis=0).reshape(pairs, items * lays * rows)
    lhs = jnp.concatenate([stacked, stacked], axis=0).T
    tabs = jnp.concatenate([tables_upper, tables_lower], axis=0)
    block = 1024
    mixed = items * lays * rows
    hi_part, lo_part = pl.pallas_call(
        functools.partial(tide_kernel, items * lays, pairs, rows),
        out_shape=(
            jax.ShapeDtypeStruct((mixed, 2 * pairs), jnp.float32),
            jax.ShapeDtypeStruct((mixed, pairs), jnp.float32),
        ),
        grid=(nlon // block,),
        in_specs=[
            pl.BlockSpec((mixed, 2 * pairs), lambda k: (0, 0)),
            pl.BlockSpec((2 * pairs, block), lambda k: (0, k)),
            pl.BlockSpec((rows, block), lambda k: (0, k)),
        ],
        out_specs=(
            pl.BlockSpec((mixed, 2 * pairs), lambda k: (0, 0)),
            pl.BlockSpec((mixed, pairs), lambda k: (0, 0)),
        ),
        compiler_params=pltpu.CompilerParams(dimension_semantics=("arbitrary",)),
        cost_estimate=pl.CostEstimate(
            flops=2 * mixed * nlon * (2 * pairs + 3 * pairs),
            transcendentals=0,
            bytes_accessed=2 * pairs * nlon * 2 + rows * nlon * 4 + mixed * 4 * pairs * 3,
        ),
    )(lhs, tabs, tide_rows)
    folded = (hi_part[:, :pairs] + hi_part[:, pairs:] + lo_part) * (2.0 / nlon)
    folded = folded.T.reshape(pairs, items, lays, rows)
    return (folded[:slots], -folded[slots:])


def tendency(grid_values, advect, coriolis, depth_rows, tide_real, tide_imag):
    vort_re = grid_values[:, :, :, 0, :]
    vort_im = grid_values[:, :, :, 1, :]
    div_re = grid_values[:, :, :, 2, :]
    div_im = grid_values[:, :, :, 3, :]
    height_re = grid_values[:, :, :, 4, :]
    height_im = grid_values[:, :, :, 5, :]
    depth_b = depth_rows[None, None, :, :]
    parts = [
        advect * vort_im - coriolis * div_re,
        -advect * vort_re - coriolis * div_im,
        advect * div_im + coriolis * vort_re,
        -advect * div_re + coriolis * vort_im,
        advect * height_im - depth_b * div_re - tide_real,
        -advect * height_re - depth_b * div_im - tide_imag,
    ]
    return jnp.stack(parts, axis=3)


def implicit_step(explicit, wave_ids, mode_to_layer, layer_to_mode, mode_speed, ntrunc):
    degrees = wave_ids[:, None] + jnp.arange(explicit.shape[-1], dtype=jnp.int32)[None, :]
    degree_f = degrees.astype(jnp.float32)
    laplace = (degree_f * (degree_f + 1.0) / float(ntrunc * ntrunc))[:, None, None, None, :]
    speeds = mode_speed[None, None, :, None, None]
    div_modes = jnp.einsum(
        "pk,svkrj->svprj", layer_to_mode, explicit[:, :, :, 2:4, :], precision=HIGHEST_PRECISION
    )
    height_modes = jnp.einsum(
        "pk,svkrj->svprj", layer_to_mode, explicit[:, :, :, 4:6, :], precision=HIGHEST_PRECISION
    )
    div_new = (div_modes + laplace * speeds * height_modes) / (1.0 + laplace * speeds * speeds)
    height_new = height_modes - speeds * div_new
    div_layers = jnp.einsum("kp,svprj->svkrj", mode_to_layer, div_new, precision=HIGHEST_PRECISION)
    height_layers = jnp.einsum(
        "kp,svprj->svkrj", mode_to_layer, height_new, precision=HIGHEST_PRECISION
    )
    return jnp.concatenate([explicit[:, :, :, 0:2, :], div_layers, height_layers], axis=3)


def exchange_sum(parts, device_count):
    flat = jnp.concatenate([p.reshape(-1) for p in parts])
    rows = jnp.broadcast_to(flat[None, :], (device_count, flat.shape[0]))
    gathered = lax.all_to_all(rows, ("lat", "wave"), 0, 0, tiled=True)
    total = jnp.sum(gathered, axis=0)
    out, start = [], 0
    for p in parts:
        out.append(total[start:start + p.size].reshape(p.shape))
        start += p.size
    return tuple(out)


def transpose_kernel(in_ref, out_ref):
    out_ref[0] = in_ref[0].T


def transpose_tables(tables):
    slots, rows, cols = tables.shape
    tile = 512
    return pl.pallas_call(
        transpose_kernel,
        out_shape=jax.ShapeDtypeStruct((slots, cols, rows), tables.dtype),
        grid=(slots, rows // tile, cols // tile),
        in_specs=[pl.BlockSpec((1, tile, tile), lambda s, i, j: (s, i, j))],
        out_specs=pl.BlockSpec((1, tile, tile), lambda s, i, j: (s, j, i)),
        cost_estimate=pl.CostEstimate(
            flops=0, transcendentals=0, bytes_accessed=2 * tables.size * tables.dtype.itemsize
        ),
    )(tables)


def to_bands(values, device_count, lanes=128):
    ls, vecs, lays, parts, nlat = values.shape
    band = nlat // device_count
    split = values.reshape(ls, vecs, lays, parts, device_count, band)
    split = jnp.transpose(split, (4, 0, 1, 2, 3, 5))
    return split.reshape(device_count, ls * vecs * lays * parts * band // lanes, lanes)


def on_device(
    arnoldi_block,
    legendre,
    wave_index,
    lat_index,
    quad_weight,
    zonal_flow,
    layer_depth,
    tide_height,
    mode_to_layer,
    layer_to_mode,
    mode_speed,
):
    local_slots = arnoldi_block.shape[0]
    vectors = arnoldi_block.shape[1]
    channels = arnoldi_block.shape[2]
    nlat = legendre.shape[1]
    ndeg = legendre.shape[2]
    ntrunc = ndeg - 1
    layers = mode_speed.shape[0]
    band_rows = tide_height.shape[0]
    device_count = lax.axis_size("lat") * lax.axis_size("wave")
    device_rank = lax.axis_index("lat") * lax.axis_size("wave") + lax.axis_index("wave")
    all_slots = wave_index.shape[0]
    axes = ("lat", "wave")
    local_waves = lax.dynamic_slice_in_dim(wave_index, device_rank * local_slots, local_slots)
    degrees = local_waves[:, None] + jnp.arange(ndeg, dtype=jnp.int32)[None, :]
    truncation = (degrees <= ntrunc).astype(jnp.float32)[:, None, None, :]
    basis = arnoldi_block * truncation
    tables = angle_tables(wave_index, tide_height.shape[1])
    tables_upper = tables.astype(jnp.bfloat16)
    tables_lower = (tables - tables_upper.astype(jnp.float32)).astype(jnp.bfloat16)
    coriolis = (2 * lat_index + 1).astype(jnp.float32) / nlat - 1.0
    advect = (
        local_waves.astype(jnp.float32)[:, None, None, None] * zonal_flow[None, None, :, :] / ntrunc
    )
    legendre_t = transpose_tables(legendre)
    spectral = basis
    for step_index in range(STEPS):
        spectral_b = spectral.astype(jnp.bfloat16)
        grid_b = jnp.einsum(
            "svcj,slj->svcl", spectral_b, legendre, preferred_element_type=jnp.float32
        ).astype(jnp.bfloat16)
        grid_split = grid_b.reshape(local_slots, vectors, layers, 6, nlat)
        sent = to_bands(grid_split[:, :, :, 2:4, :], device_count)
        received = lax.all_to_all(sent, axes, 0, 0, tiled=True)
        band_div = received.reshape(all_slots, vectors, layers, 2, band_rows)
        tide_real, tide_imag = tide_term(
            band_div[:, :, :, 0, :],
            band_div[:, :, :, 1, :],
            tide_height,
            tables_upper,
            tables_lower,
        )
        tide_parts = jnp.stack([tide_real, tide_imag], axis=3)
        back = tide_parts.reshape(device_count, -1, 128)
        returned = lax.all_to_all(back, axes, 0, 0, tiled=True)
        returned = returned.reshape(device_count, local_slots, vectors, layers, 2, band_rows)
        tide_rows = jnp.transpose(returned, (1, 2, 3, 4, 0, 5)).reshape(
            local_slots, vectors, layers, 2, nlat
        )
        tendencies = tendency(
            grid_split.astype(jnp.float32),
            advect,
            coriolis,
            layer_depth,
            tide_rows[:, :, :, 0, :],
            tide_rows[:, :, :, 1, :],
        )
        weighted = (
            (quad_weight * tendencies)
            .astype(jnp.bfloat16)
            .reshape(local_slots, vectors, channels, nlat)
        )
        analysed = jnp.einsum(
            "svcl,sjl->svcj", weighted, legendre_t, preferred_element_type=jnp.float32
        )
        analysed = analysed * truncation
        explicit = (spectral + analysed).reshape(local_slots, vectors, layers, 6, ndeg)
        spectral = (
            implicit_step(
                explicit, local_waves, mode_to_layer, layer_to_mode, mode_speed, ntrunc
            ).reshape(local_slots, vectors, channels, ndeg)
            * truncation
        )
    entries = float(local_slots * device_count * channels * ndeg)
    local_proj = jnp.einsum("skcj,svcj->kv", basis, spectral, precision=HIGHEST_PRECISION)
    local_self = jnp.sum(spectral * spectral, axis=(0, 2, 3))
    local_gram = jnp.einsum("skcj,sqcj->kq", basis, basis, precision=HIGHEST_PRECISION)
    projection, self_sum, gram = exchange_sum((local_proj, local_self, local_gram), device_count)
    hessenberg = projection / entries
    residual = spectral - jnp.einsum(
        "skcj,kv->svcj", basis, hessenberg, precision=HIGHEST_PRECISION
    )
    quadratic = jnp.einsum("kv,kq,qv->v", hessenberg, gram, hessenberg, precision=HIGHEST_PRECISION)
    norm_sq = (self_sum - 2.0 * jnp.sum(hessenberg * projection, axis=0) + quadratic) / entries
    subdiagonal = jnp.sqrt(norm_sq + 1e-06)
    return (residual / subdiagonal[None, :, None, None], hessenberg, subdiagonal)


def solution(mesh):
    return jax.shard_map(
        on_device,
        mesh=mesh,
        in_specs=(
            P(("lat", "wave"), None, None, None),
            P(("lat", "wave"), None, None),
            P(),
            P(),
            P(),
            P(),
            P(),
            P(("lat", "wave"), None),
            P(),
            P(),
            P(),
        ),
        out_specs=(P(("lat", "wave"), None, None, None), P(), P()),
        check_vma=False,
    )
```

```python
import functools
import math

import jax
import jax.numpy as jnp
from jax import lax
from jax.sharding import PartitionSpec as P
from jax.experimental import pallas as pl
from jax.experimental.pallas import tpu as pltpu

STEPS = 3


HIGHEST_PRECISION = lax.Precision.HIGHEST


def angle_tables(wave_ids, nlon):
    lon_steps = jnp.arange(nlon, dtype=jnp.int32)
    phase = wave_ids[:, None] * lon_steps[None, :] % nlon
    theta = phase.astype(jnp.float32) * (2.0 * math.pi / nlon)
    return jnp.concatenate([jnp.cos(theta), jnp.sin(theta)], axis=0)


def tide_kernel(items, pairs, rows, lhs_ref, tab_ref, tide_ref, hi_ref, lo_ref):
    step = pl.program_id(0)

    @pl.when(step == 0)
    def _():
        hi_ref[...] = jnp.zeros_like(hi_ref)
        lo_ref[...] = jnp.zeros_like(lo_ref)

    field = jnp.dot(lhs_ref[...], tab_ref[...], preferred_element_type=jnp.float32)
    width = field.shape[1]
    product = (field.reshape(items, rows, width) * tide_ref[...][None, :, :]).reshape(
        items * rows, width
    )
    product_hi = product.astype(jnp.bfloat16)
    product_lo = (product - product_hi.astype(jnp.float32)).astype(jnp.bfloat16)
    last_dims = (((1,), (1,)), ((), ()))
    hi_ref[...] += lax.dot_general(
        product_hi, tab_ref[...], last_dims, preferred_element_type=jnp.float32
    )
    lo_ref[...] += lax.dot_general(
        product_lo, tab_ref[0:pairs, :], last_dims, preferred_element_type=jnp.float32
    )


def tide_term(div_real, div_imag, tide_rows, tables_upper, tables_lower):
    slots, items, lays, rows = div_real.shape
    nlon = tables_upper.shape[1]
    pairs = 2 * slots
    stacked = jnp.concatenate([div_real, -div_imag], axis=0).reshape(pairs, items * lays * rows)
    lhs = jnp.concatenate([stacked, stacked], axis=0).T
    tabs = jnp.concatenate([tables_upper, tables_lower], axis=0)
    block = 1024
    mixed = items * lays * rows
    hi_part, lo_part = pl.pallas_call(
        functools.partial(tide_kernel, items * lays, pairs, rows),
        out_shape=(
            jax.ShapeDtypeStruct((mixed, 2 * pairs), jnp.float32),
            jax.ShapeDtypeStruct((mixed, pairs), jnp.float32),
        ),
        grid=(nlon // block,),
        in_specs=[
            pl.BlockSpec((mixed, 2 * pairs), lambda k: (0, 0)),
            pl.BlockSpec((2 * pairs, block), lambda k: (0, k)),
            pl.BlockSpec((rows, block), lambda k: (0, k)),
        ],
        out_specs=(
            pl.BlockSpec((mixed, 2 * pairs), lambda k: (0, 0)),
            pl.BlockSpec((mixed, pairs), lambda k: (0, 0)),
        ),
        compiler_params=pltpu.CompilerParams(dimension_semantics=("arbitrary",)),
        cost_estimate=pl.CostEstimate(
            flops=2 * mixed * nlon * (2 * pairs + 3 * pairs),
            transcendentals=0,
            bytes_accessed=2 * pairs * nlon * 2 + rows * nlon * 4 + mixed * 4 * pairs * 3,
        ),
    )(lhs, tabs, tide_rows)
    folded = (hi_part[:, :pairs] + hi_part[:, pairs:] + lo_part) * (2.0 / nlon)
    folded = folded.T.reshape(pairs, items, lays, rows)
    return (folded[:slots], -folded[slots:])


def tendency(grid_values, advect, coriolis, depth_rows, tide_real, tide_imag):
    vort_re = grid_values[:, :, :, 0, :]
    vort_im = grid_values[:, :, :, 1, :]
    div_re = grid_values[:, :, :, 2, :]
    div_im = grid_values[:, :, :, 3, :]
    height_re = grid_values[:, :, :, 4, :]
    height_im = grid_values[:, :, :, 5, :]
    depth_b = depth_rows[None, None, :, :]
    parts = [
        advect * vort_im - coriolis * div_re,
        -advect * vort_re - coriolis * div_im,
        advect * div_im + coriolis * vort_re,
        -advect * div_re + coriolis * vort_im,
        advect * height_im - depth_b * div_re - tide_real,
        -advect * height_re - depth_b * div_im - tide_imag,
    ]
    return jnp.stack(parts, axis=3)


def implicit_step(explicit, wave_ids, mode_to_layer, layer_to_mode, mode_speed, ntrunc):
    degrees = wave_ids[:, None] + jnp.arange(explicit.shape[-1], dtype=jnp.int32)[None, :]
    degree_f = degrees.astype(jnp.float32)
    laplace = (degree_f * (degree_f + 1.0) / float(ntrunc * ntrunc))[:, None, None, None, :]
    speeds = mode_speed[None, None, :, None, None]
    div_modes = jnp.einsum(
        "pk,svkrj->svprj", layer_to_mode, explicit[:, :, :, 2:4, :], precision=HIGHEST_PRECISION
    )
    height_modes = jnp.einsum(
        "pk,svkrj->svprj", layer_to_mode, explicit[:, :, :, 4:6, :], precision=HIGHEST_PRECISION
    )
    div_new = (div_modes + laplace * speeds * height_modes) / (1.0 + laplace * speeds * speeds)
    height_new = height_modes - speeds * div_new
    div_layers = jnp.einsum("kp,svprj->svkrj", mode_to_layer, div_new, precision=HIGHEST_PRECISION)
    height_layers = jnp.einsum(
        "kp,svprj->svkrj", mode_to_layer, height_new, precision=HIGHEST_PRECISION
    )
    return jnp.concatenate([explicit[:, :, :, 0:2, :], div_layers, height_layers], axis=3)


def exchange_sum(parts, device_count):
    flat = jnp.concatenate([p.reshape(-1) for p in parts])
    rows = jnp.broadcast_to(flat[None, :], (device_count, flat.shape[0]))
    gathered = lax.all_to_all(rows, ("lat", "wave"), 0, 0, tiled=True)
    total = jnp.sum(gathered, axis=0)
    out, start = [], 0
    for p in parts:
        out.append(total[start:start + p.size].reshape(p.shape))
        start += p.size
    return tuple(out)


def to_bands(values, device_count, lanes=128):
    ls, vecs, lays, parts, nlat = values.shape
    band = nlat // device_count
    split = values.reshape(ls, vecs, lays, parts, device_count, band)
    split = jnp.transpose(split, (4, 0, 1, 2, 3, 5))
    return split.reshape(device_count, ls * vecs * lays * parts * band // lanes, lanes)


def on_device(
    arnoldi_block,
    legendre,
    wave_index,
    lat_index,
    quad_weight,
    zonal_flow,
    layer_depth,
    tide_height,
    mode_to_layer,
    layer_to_mode,
    mode_speed,
):
    local_slots = arnoldi_block.shape[0]
    vectors = arnoldi_block.shape[1]
    channels = arnoldi_block.shape[2]
    nlat = legendre.shape[1]
    ndeg = legendre.shape[2]
    ntrunc = ndeg - 1
    layers = mode_speed.shape[0]
    band_rows = tide_height.shape[0]
    device_count = lax.axis_size("lat") * lax.axis_size("wave")
    device_rank = lax.axis_index("lat") * lax.axis_size("wave") + lax.axis_index("wave")
    all_slots = wave_index.shape[0]
    axes = ("lat", "wave")
    local_waves = lax.dynamic_slice_in_dim(wave_index, device_rank * local_slots, local_slots)
    degrees = local_waves[:, None] + jnp.arange(ndeg, dtype=jnp.int32)[None, :]
    truncation = (degrees <= ntrunc).astype(jnp.float32)[:, None, None, :]
    basis = arnoldi_block * truncation
    tables = angle_tables(wave_index, tide_height.shape[1])
    tables_upper = tables.astype(jnp.bfloat16)
    tables_lower = (tables - tables_upper.astype(jnp.float32)).astype(jnp.bfloat16)
    coriolis = (2 * lat_index + 1).astype(jnp.float32) / nlat - 1.0
    advect = (
        local_waves.astype(jnp.float32)[:, None, None, None] * zonal_flow[None, None, :, :] / ntrunc
    )
    def one_step(step_index, spectral):
        spectral_b = spectral.astype(jnp.bfloat16)
        grid_b = jnp.einsum(
            "svcj,slj->svcl", spectral_b, legendre, preferred_element_type=jnp.float32
        ).astype(jnp.bfloat16)
        grid_split = grid_b.reshape(local_slots, vectors, layers, 6, nlat)
        sent = to_bands(grid_split[:, :, :, 2:4, :], device_count)
        received = lax.all_to_all(sent, axes, 0, 0, tiled=True)
        band_div = received.reshape(all_slots, vectors, layers, 2, band_rows)
        tide_real, tide_imag = tide_term(
            band_div[:, :, :, 0, :],
            band_div[:, :, :, 1, :],
            tide_height,
            tables_upper,
            tables_lower,
        )
        tide_parts = jnp.stack([tide_real, tide_imag], axis=3)
        back = tide_parts.reshape(device_count, -1, 128)
        returned = lax.all_to_all(back, axes, 0, 0, tiled=True)
        returned = returned.reshape(device_count, local_slots, vectors, layers, 2, band_rows)
        tide_rows = jnp.transpose(returned, (1, 2, 3, 4, 0, 5)).reshape(
            local_slots, vectors, layers, 2, nlat
        )
        tendencies = tendency(
            grid_split.astype(jnp.float32),
            advect,
            coriolis,
            layer_depth,
            tide_rows[:, :, :, 0, :],
            tide_rows[:, :, :, 1, :],
        )
        weighted = (
            (quad_weight * tendencies)
            .astype(jnp.bfloat16)
            .reshape(local_slots, vectors, channels, nlat)
        )
        analysed = jnp.einsum(
            "svcl,slj->svcj", weighted, legendre, preferred_element_type=jnp.float32
        )
        analysed = analysed * truncation
        explicit = (spectral + analysed).reshape(local_slots, vectors, layers, 6, ndeg)
        spectral = (
            implicit_step(
                explicit, local_waves, mode_to_layer, layer_to_mode, mode_speed, ntrunc
            ).reshape(local_slots, vectors, channels, ndeg)
            * truncation
        )
        return spectral

    spectral = lax.fori_loop(0, STEPS, one_step, basis)
    entries = float(local_slots * device_count * channels * ndeg)
    local_proj = jnp.einsum("skcj,svcj->kv", basis, spectral, precision=HIGHEST_PRECISION)
    local_self = jnp.sum(spectral * spectral, axis=(0, 2, 3))
    local_gram = jnp.einsum("skcj,sqcj->kq", basis, basis, precision=HIGHEST_PRECISION)
    projection, self_sum, gram = exchange_sum((local_proj, local_self, local_gram), device_count)
    hessenberg = projection / entries
    residual = spectral - jnp.einsum(
        "skcj,kv->svcj", basis, hessenberg, precision=HIGHEST_PRECISION
    )
    quadratic = jnp.einsum("kv,kq,qv->v", hessenberg, gram, hessenberg, precision=HIGHEST_PRECISION)
    norm_sq = (self_sum - 2.0 * jnp.sum(hessenberg * projection, axis=0) + quadratic) / entries
    subdiagonal = jnp.sqrt(norm_sq + 1e-06)
    return (residual / subdiagonal[None, :, None, None], hessenberg, subdiagonal)


def solution(mesh):
    return jax.shard_map(
        on_device,
        mesh=mesh,
        in_specs=(
            P(("lat", "wave"), None, None, None),
            P(("lat", "wave"), None, None),
            P(),
            P(),
            P(),
            P(),
            P(),
            P(("lat", "wave"), None),
            P(),
            P(),
            P(),
        ),
        out_specs=(P(("lat", "wave"), None, None, None), P(), P()),
        check_vma=False,
    )
```

```python
import functools
import math

import jax
import jax.numpy as jnp
from jax import lax
from jax.sharding import PartitionSpec as P
from jax.experimental import pallas as pl
from jax.experimental.pallas import tpu as pltpu

STEPS = 3


HIGHEST_PRECISION = lax.Precision.HIGHEST


def angle_tables(wave_ids, nlon):
    lon_steps = jnp.arange(nlon, dtype=jnp.int32)
    phase = wave_ids[:, None] * lon_steps[None, :] % nlon
    theta = phase.astype(jnp.float32) * (2.0 * math.pi / nlon)
    return jnp.concatenate([jnp.cos(theta), jnp.sin(theta)], axis=0)


def tide_kernel(items, pairs, rows, lhs_ref, tab_ref, tide_ref, hi_ref, lo_ref):
    step = pl.program_id(0)

    @pl.when(step == 0)
    def _():
        hi_ref[...] = jnp.zeros_like(hi_ref)
        lo_ref[...] = jnp.zeros_like(lo_ref)

    field = jnp.dot(lhs_ref[...], tab_ref[...], preferred_element_type=jnp.float32)
    width = field.shape[1]
    product = (field.reshape(items, rows, width) * tide_ref[...][None, :, :]).reshape(
        items * rows, width
    )
    product_hi = product.astype(jnp.bfloat16)
    product_lo = (product - product_hi.astype(jnp.float32)).astype(jnp.bfloat16)
    last_dims = (((1,), (1,)), ((), ()))
    hi_ref[...] += lax.dot_general(
        product_hi, tab_ref[...], last_dims, preferred_element_type=jnp.float32
    )
    lo_ref[...] += lax.dot_general(
        product_lo, tab_ref[0:pairs, :], last_dims, preferred_element_type=jnp.float32
    )


def tide_term(div_real, div_imag, tide_rows, tables_upper, tables_lower):
    slots, items, lays, rows = div_real.shape
    nlon = tables_upper.shape[1]
    pairs = 2 * slots
    stacked = jnp.concatenate([div_real, -div_imag], axis=0).reshape(pairs, items * lays * rows)
    lhs = jnp.concatenate([stacked, stacked], axis=0).T
    tabs = jnp.concatenate([tables_upper, tables_lower], axis=0)
    block = 1024
    mixed = items * lays * rows
    hi_part, lo_part = pl.pallas_call(
        functools.partial(tide_kernel, items * lays, pairs, rows),
        out_shape=(
            jax.ShapeDtypeStruct((mixed, 2 * pairs), jnp.float32),
            jax.ShapeDtypeStruct((mixed, pairs), jnp.float32),
        ),
        grid=(nlon // block,),
        in_specs=[
            pl.BlockSpec((mixed, 2 * pairs), lambda k: (0, 0)),
            pl.BlockSpec((2 * pairs, block), lambda k: (0, k)),
            pl.BlockSpec((rows, block), lambda k: (0, k)),
        ],
        out_specs=(
            pl.BlockSpec((mixed, 2 * pairs), lambda k: (0, 0)),
            pl.BlockSpec((mixed, pairs), lambda k: (0, 0)),
        ),
        compiler_params=pltpu.CompilerParams(dimension_semantics=("arbitrary",)),
        cost_estimate=pl.CostEstimate(
            flops=2 * mixed * nlon * (2 * pairs + 3 * pairs),
            transcendentals=0,
            bytes_accessed=2 * pairs * nlon * 2 + rows * nlon * 4 + mixed * 4 * pairs * 3,
        ),
    )(lhs, tabs, tide_rows)
    folded = (hi_part[:, :pairs] + hi_part[:, pairs:] + lo_part) * (2.0 / nlon)
    folded = folded.T.reshape(pairs, items, lays, rows)
    return (folded[:slots], -folded[slots:])


def tendency(grid_values, advect, coriolis, depth_rows, tide_real, tide_imag):
    vort_re = grid_values[:, :, :, 0, :]
    vort_im = grid_values[:, :, :, 1, :]
    div_re = grid_values[:, :, :, 2, :]
    div_im = grid_values[:, :, :, 3, :]
    height_re = grid_values[:, :, :, 4, :]
    height_im = grid_values[:, :, :, 5, :]
    depth_b = depth_rows[None, None, :, :]
    parts = [
        advect * vort_im - coriolis * div_re,
        -advect * vort_re - coriolis * div_im,
        advect * div_im + coriolis * vort_re,
        -advect * div_re + coriolis * vort_im,
        advect * height_im - depth_b * div_re - tide_real,
        -advect * height_re - depth_b * div_im - tide_imag,
    ]
    return jnp.stack(parts, axis=3)


def implicit_step(explicit, wave_ids, mode_to_layer, layer_to_mode, mode_speed, ntrunc):
    degrees = wave_ids[:, None] + jnp.arange(explicit.shape[-1], dtype=jnp.int32)[None, :]
    degree_f = degrees.astype(jnp.float32)
    laplace = (degree_f * (degree_f + 1.0) / float(ntrunc * ntrunc))[:, None, None, None, :]
    speeds = mode_speed[None, None, :, None, None]
    div_modes = jnp.einsum(
        "pk,svkrj->svprj", layer_to_mode, explicit[:, :, :, 2:4, :], precision=HIGHEST_PRECISION
    )
    height_modes = jnp.einsum(
        "pk,svkrj->svprj", layer_to_mode, explicit[:, :, :, 4:6, :], precision=HIGHEST_PRECISION
    )
    div_new = (div_modes + laplace * speeds * height_modes) / (1.0 + laplace * speeds * speeds)
    height_new = height_modes - speeds * div_new
    div_layers = jnp.einsum("kp,svprj->svkrj", mode_to_layer, div_new, precision=HIGHEST_PRECISION)
    height_layers = jnp.einsum(
        "kp,svprj->svkrj", mode_to_layer, height_new, precision=HIGHEST_PRECISION
    )
    return jnp.concatenate([explicit[:, :, :, 0:2, :], div_layers, height_layers], axis=3)


def exchange_sum(parts, device_count):
    flat = jnp.concatenate([p.reshape(-1) for p in parts])
    rows = jnp.broadcast_to(flat[None, :], (device_count, flat.shape[0]))
    gathered = lax.all_to_all(rows, ("lat", "wave"), 0, 0, tiled=True)
    total = jnp.sum(gathered, axis=0)
    out, start = [], 0
    for p in parts:
        out.append(total[start:start + p.size].reshape(p.shape))
        start += p.size
    return tuple(out)


def synthesis_kernel(table_ref, coeff_ref, out_ref):
    out_ref[0] = jnp.dot(
        table_ref[0], coeff_ref[0], preferred_element_type=jnp.float32
    ).astype(out_ref.dtype)


def synthesize(coeffs, tables):
    slots, rows, ndeg = coeffs.shape
    nlat = tables.shape[1]
    block = 256
    coeffs_t = jnp.swapaxes(coeffs, 1, 2)
    return pl.pallas_call(
        synthesis_kernel,
        out_shape=jax.ShapeDtypeStruct((slots, nlat, rows), jnp.bfloat16),
        grid=(slots, nlat // block),
        in_specs=[
            pl.BlockSpec((1, block, ndeg), lambda s, i: (s, i, 0)),
            pl.BlockSpec((1, ndeg, rows), lambda s, i: (s, 0, 0)),
        ],
        out_specs=pl.BlockSpec((1, block, rows), lambda s, i: (s, i, 0)),
        cost_estimate=pl.CostEstimate(
            flops=2 * slots * nlat * ndeg * rows,
            transcendentals=0,
            bytes_accessed=slots * (nlat * ndeg + ndeg * rows + nlat * rows) * 2,
        ),
    )(tables, coeffs_t)


def to_bands(values, device_count, lanes=128):
    ls, vecs, lays, parts, nlat = values.shape
    band = nlat // device_count
    split = values.reshape(ls, vecs, lays, parts, device_count, band)
    split = jnp.transpose(split, (4, 0, 1, 2, 3, 5))
    return split.reshape(device_count, ls * vecs * lays * parts * band // lanes, lanes)


def on_device(
    arnoldi_block,
    legendre,
    wave_index,
    lat_index,
    quad_weight,
    zonal_flow,
    layer_depth,
    tide_height,
    mode_to_layer,
    layer_to_mode,
    mode_speed,
):
    local_slots = arnoldi_block.shape[0]
    vectors = arnoldi_block.shape[1]
    channels = arnoldi_block.shape[2]
    nlat = legendre.shape[1]
    ndeg = legendre.shape[2]
    ntrunc = ndeg - 1
    layers = mode_speed.shape[0]
    band_rows = tide_height.shape[0]
    device_count = lax.axis_size("lat") * lax.axis_size("wave")
    device_rank = lax.axis_index("lat") * lax.axis_size("wave") + lax.axis_index("wave")
    all_slots = wave_index.shape[0]
    axes = ("lat", "wave")
    local_waves = lax.dynamic_slice_in_dim(wave_index, device_rank * local_slots, local_slots)
    degrees = local_waves[:, None] + jnp.arange(ndeg, dtype=jnp.int32)[None, :]
    truncation = (degrees <= ntrunc).astype(jnp.float32)[:, None, None, :]
    basis = arnoldi_block * truncation
    tables = angle_tables(wave_index, tide_height.shape[1])
    tables_upper = tables.astype(jnp.bfloat16)
    tables_lower = (tables - tables_upper.astype(jnp.float32)).astype(jnp.bfloat16)
    coriolis = (2 * lat_index + 1).astype(jnp.float32) / nlat - 1.0
    advect = (
        local_waves.astype(jnp.float32)[:, None, None, None] * zonal_flow[None, None, :, :] / ntrunc
    )
    def one_step(step_index, spectral):
        spectral_b = spectral.astype(jnp.bfloat16)
        grid_t = synthesize(
            spectral_b.reshape(local_slots, vectors * channels, ndeg), legendre
        )
        grid_b = jnp.swapaxes(grid_t, 1, 2).reshape(local_slots, vectors, channels, nlat)
        grid_split = grid_b.reshape(local_slots, vectors, layers, 6, nlat)
        sent = to_bands(grid_split[:, :, :, 2:4, :], device_count)
        received = lax.all_to_all(sent, axes, 0, 0, tiled=True)
        band_div = received.reshape(all_slots, vectors, layers, 2, band_rows)
        tide_real, tide_imag = tide_term(
            band_div[:, :, :, 0, :],
            band_div[:, :, :, 1, :],
            tide_height,
            tables_upper,
            tables_lower,
        )
        tide_parts = jnp.stack([tide_real, tide_imag], axis=3)
        back = tide_parts.reshape(device_count, -1, 128)
        returned = lax.all_to_all(back, axes, 0, 0, tiled=True)
        returned = returned.reshape(device_count, local_slots, vectors, layers, 2, band_rows)
        tide_rows = jnp.transpose(returned, (1, 2, 3, 4, 0, 5)).reshape(
            local_slots, vectors, layers, 2, nlat
        )
        tendencies = tendency(
            grid_split.astype(jnp.float32),
            advect,
            coriolis,
            layer_depth,
            tide_rows[:, :, :, 0, :],
            tide_rows[:, :, :, 1, :],
        )
        weighted = (
            (quad_weight * tendencies)
            .astype(jnp.bfloat16)
            .reshape(local_slots, vectors, channels, nlat)
        )
        analysed = jnp.einsum(
            "svcl,slj->svcj", weighted, legendre, preferred_element_type=jnp.float32
        )
        analysed = analysed * truncation
        explicit = (spectral + analysed).reshape(local_slots, vectors, layers, 6, ndeg)
        spectral = (
            implicit_step(
                explicit, local_waves, mode_to_layer, layer_to_mode, mode_speed, ntrunc
            ).reshape(local_slots, vectors, channels, ndeg)
            * truncation
        )
        return spectral

    spectral = lax.fori_loop(0, STEPS, one_step, basis)
    entries = float(local_slots * device_count * channels * ndeg)
    local_proj = jnp.einsum("skcj,svcj->kv", basis, spectral, precision=HIGHEST_PRECISION)
    local_self = jnp.sum(spectral * spectral, axis=(0, 2, 3))
    local_gram = jnp.einsum("skcj,sqcj->kq", basis, basis, precision=HIGHEST_PRECISION)
    projection, self_sum, gram = exchange_sum((local_proj, local_self, local_gram), device_count)
    hessenberg = projection / entries
    residual = spectral - jnp.einsum(
        "skcj,kv->svcj", basis, hessenberg, precision=HIGHEST_PRECISION
    )
    quadratic = jnp.einsum("kv,kq,qv->v", hessenberg, gram, hessenberg, precision=HIGHEST_PRECISION)
    norm_sq = (self_sum - 2.0 * jnp.sum(hessenberg * projection, axis=0) + quadratic) / entries
    subdiagonal = jnp.sqrt(norm_sq + 1e-06)
    return (residual / subdiagonal[None, :, None, None], hessenberg, subdiagonal)


def solution(mesh):
    return jax.shard_map(
        on_device,
        mesh=mesh,
        in_specs=(
            P(("lat", "wave"), None, None, None),
            P(("lat", "wave"), None, None),
            P(),
            P(),
            P(),
            P(),
            P(),
            P(("lat", "wave"), None),
            P(),
            P(),
            P(),
        ),
        out_specs=(P(("lat", "wave"), None, None, None), P(), P()),
        check_vma=False,
    )
```

```python
import functools
import math

import jax
import jax.numpy as jnp
from jax import lax
from jax.sharding import PartitionSpec as P
from jax.experimental import pallas as pl
from jax.experimental.pallas import tpu as pltpu

STEPS = 3


HIGHEST_PRECISION = lax.Precision.HIGHEST


def angle_tables(wave_ids, nlon):
    lon_steps = jnp.arange(nlon, dtype=jnp.int32)
    phase = wave_ids[:, None] * lon_steps[None, :] % nlon
    theta = phase.astype(jnp.float32) * (2.0 * math.pi / nlon)
    return jnp.concatenate([jnp.cos(theta), jnp.sin(theta)], axis=0)


def tide_kernel(items, pairs, rows, lhs_ref, tab_ref, tide_ref, hi_ref, lo_ref):
    step = pl.program_id(0)

    @pl.when(step == 0)
    def _():
        hi_ref[...] = jnp.zeros_like(hi_ref)
        lo_ref[...] = jnp.zeros_like(lo_ref)

    field = jnp.dot(lhs_ref[...], tab_ref[...], preferred_element_type=jnp.float32)
    width = field.shape[1]
    product = (field.reshape(items, rows, width) * tide_ref[...][None, :, :]).reshape(
        items * rows, width
    )
    product_hi = product.astype(jnp.bfloat16)
    product_lo = (product - product_hi.astype(jnp.float32)).astype(jnp.bfloat16)
    last_dims = (((1,), (1,)), ((), ()))
    hi_ref[...] += lax.dot_general(
        product_hi, tab_ref[...], last_dims, preferred_element_type=jnp.float32
    )
    lo_ref[...] += lax.dot_general(
        product_lo, tab_ref[0:pairs, :], last_dims, preferred_element_type=jnp.float32
    )


def tide_term(div_real, div_imag, tide_rows, tables_upper, tables_lower):
    slots, items, lays, rows = div_real.shape
    nlon = tables_upper.shape[1]
    pairs = 2 * slots
    stacked = jnp.concatenate([div_real, -div_imag], axis=0).reshape(pairs, items * lays * rows)
    lhs = jnp.concatenate([stacked, stacked], axis=0).T
    tabs = jnp.concatenate([tables_upper, tables_lower], axis=0)
    block = 2048
    mixed = items * lays * rows
    hi_part, lo_part = pl.pallas_call(
        functools.partial(tide_kernel, items * lays, pairs, rows),
        out_shape=(
            jax.ShapeDtypeStruct((mixed, 2 * pairs), jnp.float32),
            jax.ShapeDtypeStruct((mixed, pairs), jnp.float32),
        ),
        grid=(nlon // block,),
        in_specs=[
            pl.BlockSpec((mixed, 2 * pairs), lambda k: (0, 0)),
            pl.BlockSpec((2 * pairs, block), lambda k: (0, k)),
            pl.BlockSpec((rows, block), lambda k: (0, k)),
        ],
        out_specs=(
            pl.BlockSpec((mixed, 2 * pairs), lambda k: (0, 0)),
            pl.BlockSpec((mixed, pairs), lambda k: (0, 0)),
        ),
        compiler_params=pltpu.CompilerParams(dimension_semantics=("arbitrary",)),
        cost_estimate=pl.CostEstimate(
            flops=2 * mixed * nlon * (2 * pairs + 3 * pairs),
            transcendentals=0,
            bytes_accessed=2 * pairs * nlon * 2 + rows * nlon * 4 + mixed * 4 * pairs * 3,
        ),
    )(lhs, tabs, tide_rows)
    folded = (hi_part[:, :pairs] + hi_part[:, pairs:] + lo_part) * (2.0 / nlon)
    folded = folded.T.reshape(pairs, items, lays, rows)
    return (folded[:slots], -folded[slots:])


def tendency(grid_values, advect, coriolis, depth_rows, tide_real, tide_imag):
    vort_re = grid_values[:, :, :, 0, :]
    vort_im = grid_values[:, :, :, 1, :]
    div_re = grid_values[:, :, :, 2, :]
    div_im = grid_values[:, :, :, 3, :]
    height_re = grid_values[:, :, :, 4, :]
    height_im = grid_values[:, :, :, 5, :]
    depth_b = depth_rows[None, None, :, :]
    parts = [
        advect * vort_im - coriolis * div_re,
        -advect * vort_re - coriolis * div_im,
        advect * div_im + coriolis * vort_re,
        -advect * div_re + coriolis * vort_im,
        advect * height_im - depth_b * div_re - tide_real,
        -advect * height_re - depth_b * div_im - tide_imag,
    ]
    return jnp.stack(parts, axis=3)


def implicit_step(explicit, wave_ids, mode_to_layer, layer_to_mode, mode_speed, ntrunc):
    degrees = wave_ids[:, None] + jnp.arange(explicit.shape[-1], dtype=jnp.int32)[None, :]
    degree_f = degrees.astype(jnp.float32)
    laplace = (degree_f * (degree_f + 1.0) / float(ntrunc * ntrunc))[:, None, None, None, :]
    speeds = mode_speed[None, None, :, None, None]
    div_modes = jnp.einsum(
        "pk,svkrj->svprj", layer_to_mode, explicit[:, :, :, 2:4, :], precision=HIGHEST_PRECISION
    )
    height_modes = jnp.einsum(
        "pk,svkrj->svprj", layer_to_mode, explicit[:, :, :, 4:6, :], precision=HIGHEST_PRECISION
    )
    div_new = (div_modes + laplace * speeds * height_modes) / (1.0 + laplace * speeds * speeds)
    height_new = height_modes - speeds * div_new
    div_layers = jnp.einsum("kp,svprj->svkrj", mode_to_layer, div_new, precision=HIGHEST_PRECISION)
    height_layers = jnp.einsum(
        "kp,svprj->svkrj", mode_to_layer, height_new, precision=HIGHEST_PRECISION
    )
    return jnp.concatenate([explicit[:, :, :, 0:2, :], div_layers, height_layers], axis=3)


def exchange_sum(parts, device_count):
    flat = jnp.concatenate([p.reshape(-1) for p in parts])
    rows = jnp.broadcast_to(flat[None, :], (device_count, flat.shape[0]))
    gathered = lax.all_to_all(rows, ("lat", "wave"), 0, 0, tiled=True)
    total = jnp.sum(gathered, axis=0)
    out, start = [], 0
    for p in parts:
        out.append(total[start:start + p.size].reshape(p.shape))
        start += p.size
    return tuple(out)


def to_bands(values, device_count, lanes=128):
    ls, vecs, lays, parts, nlat = values.shape
    band = nlat // device_count
    split = values.reshape(ls, vecs, lays, parts, device_count, band)
    split = jnp.transpose(split, (4, 0, 1, 2, 3, 5))
    return split.reshape(device_count, ls * vecs * lays * parts * band // lanes, lanes)


def on_device(
    arnoldi_block,
    legendre,
    wave_index,
    lat_index,
    quad_weight,
    zonal_flow,
    layer_depth,
    tide_height,
    mode_to_layer,
    layer_to_mode,
    mode_speed,
):
    local_slots = arnoldi_block.shape[0]
    vectors = arnoldi_block.shape[1]
    channels = arnoldi_block.shape[2]
    nlat = legendre.shape[1]
    ndeg = legendre.shape[2]
    ntrunc = ndeg - 1
    layers = mode_speed.shape[0]
    band_rows = tide_height.shape[0]
    device_count = lax.axis_size("lat") * lax.axis_size("wave")
    device_rank = lax.axis_index("lat") * lax.axis_size("wave") + lax.axis_index("wave")
    all_slots = wave_index.shape[0]
    axes = ("lat", "wave")
    local_waves = lax.dynamic_slice_in_dim(wave_index, device_rank * local_slots, local_slots)
    degrees = local_waves[:, None] + jnp.arange(ndeg, dtype=jnp.int32)[None, :]
    truncation = (degrees <= ntrunc).astype(jnp.float32)[:, None, None, :]
    basis = arnoldi_block * truncation
    tables = angle_tables(wave_index, tide_height.shape[1])
    tables_upper = tables.astype(jnp.bfloat16)
    tables_lower = (tables - tables_upper.astype(jnp.float32)).astype(jnp.bfloat16)
    coriolis = (2 * lat_index + 1).astype(jnp.float32) / nlat - 1.0
    advect = (
        local_waves.astype(jnp.float32)[:, None, None, None] * zonal_flow[None, None, :, :] / ntrunc
    )
    def one_step(step_index, spectral):
        spectral_b = spectral.astype(jnp.bfloat16)
        grid_b = jnp.einsum(
            "svcj,slj->svcl", spectral_b, legendre, preferred_element_type=jnp.float32
        ).astype(jnp.bfloat16)
        grid_split = grid_b.reshape(local_slots, vectors, layers, 6, nlat)
        sent = to_bands(grid_split[:, :, :, 2:4, :], device_count)
        received = lax.all_to_all(sent, axes, 0, 0, tiled=True)
        band_div = received.reshape(all_slots, vectors, layers, 2, band_rows)
        tide_real, tide_imag = tide_term(
            band_div[:, :, :, 0, :],
            band_div[:, :, :, 1, :],
            tide_height,
            tables_upper,
            tables_lower,
        )
        tide_parts = jnp.stack([tide_real, tide_imag], axis=3)
        back = tide_parts.reshape(device_count, -1, 128)
        returned = lax.all_to_all(back, axes, 0, 0, tiled=True)
        returned = returned.reshape(device_count, local_slots, vectors, layers, 2, band_rows)
        tide_rows = jnp.transpose(returned, (1, 2, 3, 4, 0, 5)).reshape(
            local_slots, vectors, layers, 2, nlat
        )
        tendencies = tendency(
            grid_split.astype(jnp.float32),
            advect,
            coriolis,
            layer_depth,
            tide_rows[:, :, :, 0, :],
            tide_rows[:, :, :, 1, :],
        )
        weighted = (
            (quad_weight * tendencies)
            .astype(jnp.bfloat16)
            .reshape(local_slots, vectors, channels, nlat)
        )
        analysed = jnp.einsum(
            "svcl,slj->svcj", weighted, legendre, preferred_element_type=jnp.float32
        )
        analysed = analysed * truncation
        explicit = (spectral + analysed).reshape(local_slots, vectors, layers, 6, ndeg)
        spectral = (
            implicit_step(
                explicit, local_waves, mode_to_layer, layer_to_mode, mode_speed, ntrunc
            ).reshape(local_slots, vectors, channels, ndeg)
            * truncation
        )
        return spectral

    spectral = lax.fori_loop(0, STEPS, one_step, basis)
    entries = float(local_slots * device_count * channels * ndeg)
    local_proj = jnp.einsum("skcj,svcj->kv", basis, spectral, precision=HIGHEST_PRECISION)
    local_self = jnp.sum(spectral * spectral, axis=(0, 2, 3))
    local_gram = jnp.einsum("skcj,sqcj->kq", basis, basis, precision=HIGHEST_PRECISION)
    projection, self_sum, gram = exchange_sum((local_proj, local_self, local_gram), device_count)
    hessenberg = projection / entries
    residual = spectral - jnp.einsum(
        "skcj,kv->svcj", basis, hessenberg, precision=HIGHEST_PRECISION
    )
    quadratic = jnp.einsum("kv,kq,qv->v", hessenberg, gram, hessenberg, precision=HIGHEST_PRECISION)
    norm_sq = (self_sum - 2.0 * jnp.sum(hessenberg * projection, axis=0) + quadratic) / entries
    subdiagonal = jnp.sqrt(norm_sq + 1e-06)
    return (residual / subdiagonal[None, :, None, None], hessenberg, subdiagonal)


def solution(mesh):
    return jax.shard_map(
        on_device,
        mesh=mesh,
        in_specs=(
            P(("lat", "wave"), None, None, None),
            P(("lat", "wave"), None, None),
            P(),
            P(),
            P(),
            P(),
            P(),
            P(("lat", "wave"), None),
            P(),
            P(),
            P(),
        ),
        out_specs=(P(("lat", "wave"), None, None, None), P(), P()),
        check_vma=False,
    )
```

```python
import functools
import math

import jax
import jax.numpy as jnp
from jax import lax
from jax.sharding import PartitionSpec as P
from jax.experimental import pallas as pl
from jax.experimental.pallas import tpu as pltpu

STEPS = 3


HIGHEST_PRECISION = lax.Precision.HIGHEST


def angle_tables(wave_ids, nlon):
    lon_steps = jnp.arange(nlon, dtype=jnp.int32)
    phase = wave_ids[:, None] * lon_steps[None, :] % nlon
    theta = phase.astype(jnp.float32) * (2.0 * math.pi / nlon)
    return jnp.concatenate([jnp.cos(theta), jnp.sin(theta)], axis=0)


def tide_kernel(items, pairs, rows, lhs_ref, tab_ref, tide_ref, hi_ref, lo_ref):
    step = pl.program_id(0)

    @pl.when(step == 0)
    def _():
        hi_ref[...] = jnp.zeros_like(hi_ref)
        lo_ref[...] = jnp.zeros_like(lo_ref)

    field = jnp.dot(lhs_ref[...], tab_ref[...], preferred_element_type=jnp.float32)
    width = field.shape[1]
    product = (field.reshape(items, rows, width) * tide_ref[...][None, :, :]).reshape(
        items * rows, width
    )
    product_hi = product.astype(jnp.bfloat16)
    product_lo = (product - product_hi.astype(jnp.float32)).astype(jnp.bfloat16)
    last_dims = (((1,), (1,)), ((), ()))
    hi_ref[...] += lax.dot_general(
        product_hi, tab_ref[...], last_dims, preferred_element_type=jnp.float32
    )
    lo_ref[...] += lax.dot_general(
        product_lo, tab_ref[0:pairs, :], last_dims, preferred_element_type=jnp.float32
    )


def tide_term(div_real, div_imag, tide_rows, tables_upper, tables_lower):
    slots, items, lays, rows = div_real.shape
    nlon = tables_upper.shape[1]
    pairs = 2 * slots
    stacked = jnp.concatenate([div_real, -div_imag], axis=0).reshape(pairs, items * lays * rows)
    lhs = jnp.concatenate([stacked, stacked], axis=0).T
    tabs = jnp.concatenate([tables_upper, tables_lower], axis=0)
    block = 2048
    mixed = items * lays * rows
    hi_part, lo_part = pl.pallas_call(
        functools.partial(tide_kernel, items * lays, pairs, rows),
        out_shape=(
            jax.ShapeDtypeStruct((mixed, 2 * pairs), jnp.float32),
            jax.ShapeDtypeStruct((mixed, pairs), jnp.float32),
        ),
        grid=(nlon // block,),
        in_specs=[
            pl.BlockSpec((mixed, 2 * pairs), lambda k: (0, 0)),
            pl.BlockSpec((2 * pairs, block), lambda k: (0, k)),
            pl.BlockSpec((rows, block), lambda k: (0, k)),
        ],
        out_specs=(
            pl.BlockSpec((mixed, 2 * pairs), lambda k: (0, 0)),
            pl.BlockSpec((mixed, pairs), lambda k: (0, 0)),
        ),
        compiler_params=pltpu.CompilerParams(dimension_semantics=("arbitrary",)),
        cost_estimate=pl.CostEstimate(
            flops=2 * mixed * nlon * (2 * pairs + 3 * pairs),
            transcendentals=0,
            bytes_accessed=2 * pairs * nlon * 2 + rows * nlon * 4 + mixed * 4 * pairs * 3,
        ),
    )(lhs, tabs, tide_rows)
    folded = (hi_part[:, :pairs] + hi_part[:, pairs:] + lo_part) * (2.0 / nlon)
    folded = folded.T.reshape(pairs, items, lays, rows)
    return (folded[:slots], -folded[slots:])


def tendency(grid_values, advect, coriolis, depth_rows, tide_real, tide_imag):
    vort_re = grid_values[:, :, :, 0, :]
    vort_im = grid_values[:, :, :, 1, :]
    div_re = grid_values[:, :, :, 2, :]
    div_im = grid_values[:, :, :, 3, :]
    height_re = grid_values[:, :, :, 4, :]
    height_im = grid_values[:, :, :, 5, :]
    depth_b = depth_rows[None, None, :, :]
    parts = [
        advect * vort_im - coriolis * div_re,
        -advect * vort_re - coriolis * div_im,
        advect * div_im + coriolis * vort_re,
        -advect * div_re + coriolis * vort_im,
        advect * height_im - depth_b * div_re - tide_real,
        -advect * height_re - depth_b * div_im - tide_imag,
    ]
    return jnp.stack(parts, axis=3)


def mix(matrix, parts):
    return [
        sum(matrix[row, col] * parts[col] for col in range(len(parts)))
        for row in range(matrix.shape[0])
    ]


def implicit_step(explicit, wave_ids, mode_to_layer, layer_to_mode, mode_speed, ntrunc):
    degrees = wave_ids[:, None] + jnp.arange(explicit.shape[-1], dtype=jnp.int32)[None, :]
    degree_f = degrees.astype(jnp.float32)
    laplace = (degree_f * (degree_f + 1.0) / float(ntrunc * ntrunc))[:, None, None, :]
    layers = mode_speed.shape[0]
    div_in = [explicit[:, :, k, 2:4, :] for k in range(layers)]
    height_in = [explicit[:, :, k, 4:6, :] for k in range(layers)]
    div_modes = mix(layer_to_mode, div_in)
    height_modes = mix(layer_to_mode, height_in)
    div_new, height_new = [], []
    for p in range(layers):
        speed = mode_speed[p]
        div_p = (div_modes[p] + laplace * speed * height_modes[p]) / (1.0 + laplace * speed * speed)
        div_new.append(div_p)
        height_new.append(height_modes[p] - speed * div_p)
    div_layers = mix(mode_to_layer, div_new)
    height_layers = mix(mode_to_layer, height_new)
    out = [
        jnp.concatenate([explicit[:, :, k, 0:2, :], div_layers[k], height_layers[k]], axis=2)
        for k in range(layers)
    ]
    return jnp.stack(out, axis=2)


def exchange_sum(parts, device_count):
    flat = jnp.concatenate([p.reshape(-1) for p in parts])
    rows = jnp.broadcast_to(flat[None, :], (device_count, flat.shape[0]))
    gathered = lax.all_to_all(rows, ("lat", "wave"), 0, 0, tiled=True)
    total = jnp.sum(gathered, axis=0)
    out, start = [], 0
    for p in parts:
        out.append(total[start:start + p.size].reshape(p.shape))
        start += p.size
    return tuple(out)


def to_bands(values, device_count, lanes=128):
    ls, vecs, lays, parts, nlat = values.shape
    band = nlat // device_count
    split = values.reshape(ls, vecs, lays, parts, device_count, band)
    split = jnp.transpose(split, (4, 0, 1, 2, 3, 5))
    return split.reshape(device_count, ls * vecs * lays * parts * band // lanes, lanes)


def on_device(
    arnoldi_block,
    legendre,
    wave_index,
    lat_index,
    quad_weight,
    zonal_flow,
    layer_depth,
    tide_height,
    mode_to_layer,
    layer_to_mode,
    mode_speed,
):
    local_slots = arnoldi_block.shape[0]
    vectors = arnoldi_block.shape[1]
    channels = arnoldi_block.shape[2]
    nlat = legendre.shape[1]
    ndeg = legendre.shape[2]
    ntrunc = ndeg - 1
    layers = mode_speed.shape[0]
    band_rows = tide_height.shape[0]
    device_count = lax.axis_size("lat") * lax.axis_size("wave")
    device_rank = lax.axis_index("lat") * lax.axis_size("wave") + lax.axis_index("wave")
    all_slots = wave_index.shape[0]
    axes = ("lat", "wave")
    local_waves = lax.dynamic_slice_in_dim(wave_index, device_rank * local_slots, local_slots)
    degrees = local_waves[:, None] + jnp.arange(ndeg, dtype=jnp.int32)[None, :]
    truncation = (degrees <= ntrunc).astype(jnp.float32)[:, None, None, :]
    basis = arnoldi_block * truncation
    tables = angle_tables(wave_index, tide_height.shape[1])
    tables_upper = tables.astype(jnp.bfloat16)
    tables_lower = (tables - tables_upper.astype(jnp.float32)).astype(jnp.bfloat16)
    coriolis = (2 * lat_index + 1).astype(jnp.float32) / nlat - 1.0
    advect = (
        local_waves.astype(jnp.float32)[:, None, None, None] * zonal_flow[None, None, :, :] / ntrunc
    )
    def one_step(step_index, spectral):
        spectral_b = spectral.astype(jnp.bfloat16)
        grid_b = jnp.einsum(
            "svcj,slj->svcl", spectral_b, legendre, preferred_element_type=jnp.float32
        ).astype(jnp.bfloat16)
        grid_split = grid_b.reshape(local_slots, vectors, layers, 6, nlat)
        sent = to_bands(grid_split[:, :, :, 2:4, :], device_count)
        received = lax.all_to_all(sent, axes, 0, 0, tiled=True)
        band_div = received.reshape(all_slots, vectors, layers, 2, band_rows)
        tide_real, tide_imag = tide_term(
            band_div[:, :, :, 0, :],
            band_div[:, :, :, 1, :],
            tide_height,
            tables_upper,
            tables_lower,
        )
        tide_parts = jnp.stack([tide_real, tide_imag], axis=3)
        back = tide_parts.reshape(device_count, -1, 128)
        returned = lax.all_to_all(back, axes, 0, 0, tiled=True)
        returned = returned.reshape(device_count, local_slots, vectors, layers, 2, band_rows)
        tide_rows = jnp.transpose(returned, (1, 2, 3, 4, 0, 5)).reshape(
            local_slots, vectors, layers, 2, nlat
        )
        tendencies = tendency(
            grid_split.astype(jnp.float32),
            advect,
            coriolis,
            layer_depth,
            tide_rows[:, :, :, 0, :],
            tide_rows[:, :, :, 1, :],
        )
        weighted = (
            (quad_weight * tendencies)
            .astype(jnp.bfloat16)
            .reshape(local_slots, vectors, channels, nlat)
        )
        analysed = jnp.einsum(
            "svcl,slj->svcj", weighted, legendre, preferred_element_type=jnp.float32
        )
        analysed = analysed * truncation
        explicit = (spectral + analysed).reshape(local_slots, vectors, layers, 6, ndeg)
        spectral = (
            implicit_step(
                explicit, local_waves, mode_to_layer, layer_to_mode, mode_speed, ntrunc
            ).reshape(local_slots, vectors, channels, ndeg)
            * truncation
        )
        return spectral

    spectral = lax.fori_loop(0, STEPS, one_step, basis)
    entries = float(local_slots * device_count * channels * ndeg)
    local_proj = jnp.einsum("skcj,svcj->kv", basis, spectral, precision=HIGHEST_PRECISION)
    local_self = jnp.sum(spectral * spectral, axis=(0, 2, 3))
    local_gram = jnp.einsum("skcj,sqcj->kq", basis, basis, precision=HIGHEST_PRECISION)
    projection, self_sum, gram = exchange_sum((local_proj, local_self, local_gram), device_count)
    hessenberg = projection / entries
    residual = spectral - jnp.einsum(
        "skcj,kv->svcj", basis, hessenberg, precision=HIGHEST_PRECISION
    )
    quadratic = jnp.einsum("kv,kq,qv->v", hessenberg, gram, hessenberg, precision=HIGHEST_PRECISION)
    norm_sq = (self_sum - 2.0 * jnp.sum(hessenberg * projection, axis=0) + quadratic) / entries
    subdiagonal = jnp.sqrt(norm_sq + 1e-06)
    return (residual / subdiagonal[None, :, None, None], hessenberg, subdiagonal)


def solution(mesh):
    return jax.shard_map(
        on_device,
        mesh=mesh,
        in_specs=(
            P(("lat", "wave"), None, None, None),
            P(("lat", "wave"), None, None),
            P(),
            P(),
            P(),
            P(),
            P(),
            P(("lat", "wave"), None),
            P(),
            P(),
            P(),
        ),
        out_specs=(P(("lat", "wave"), None, None, None), P(), P()),
        check_vma=False,
    )
```

```python
import functools
import math

import jax
import jax.numpy as jnp
from jax import lax
from jax.sharding import PartitionSpec as P
from jax.experimental import pallas as pl
from jax.experimental.pallas import tpu as pltpu

STEPS = 3


HIGHEST_PRECISION = lax.Precision.HIGHEST


def angle_tables(wave_ids, nlon):
    lon_steps = jnp.arange(nlon, dtype=jnp.int32)
    phase = wave_ids[:, None] * lon_steps[None, :] % nlon
    theta = phase.astype(jnp.float32) * (2.0 * math.pi / nlon)
    return jnp.concatenate([jnp.cos(theta), jnp.sin(theta)], axis=0)


def tide_kernel(items, pairs, rows, lhs_ref, tab_ref, tide_ref, hi_ref, lo_ref):
    step = pl.program_id(0)

    @pl.when(step == 0)
    def _():
        hi_ref[...] = jnp.zeros_like(hi_ref)
        lo_ref[...] = jnp.zeros_like(lo_ref)

    field = jnp.dot(lhs_ref[...], tab_ref[...], preferred_element_type=jnp.float32)
    width = field.shape[1]
    product = (field.reshape(items, rows, width) * tide_ref[...][None, :, :]).reshape(
        items * rows, width
    )
    product_hi = product.astype(jnp.bfloat16)
    product_lo = (product - product_hi.astype(jnp.float32)).astype(jnp.bfloat16)
    last_dims = (((1,), (1,)), ((), ()))
    hi_ref[...] += lax.dot_general(
        product_hi, tab_ref[...], last_dims, preferred_element_type=jnp.float32
    )
    lo_ref[...] += lax.dot_general(
        product_lo, tab_ref[0:pairs, :], last_dims, preferred_element_type=jnp.float32
    )


def tide_term(div_real, div_imag, tide_rows, tables_upper, tables_lower):
    slots, items, lays, rows = div_real.shape
    nlon = tables_upper.shape[1]
    pairs = 2 * slots
    stacked = jnp.concatenate([div_real, -div_imag], axis=0).reshape(pairs, items * lays * rows)
    lhs = jnp.concatenate([stacked, stacked], axis=0).T
    tabs = jnp.concatenate([tables_upper, tables_lower], axis=0)
    block = 2048
    mixed = items * lays * rows
    hi_part, lo_part = pl.pallas_call(
        functools.partial(tide_kernel, items * lays, pairs, rows),
        out_shape=(
            jax.ShapeDtypeStruct((mixed, 2 * pairs), jnp.float32),
            jax.ShapeDtypeStruct((mixed, pairs), jnp.float32),
        ),
        grid=(nlon // block,),
        in_specs=[
            pl.BlockSpec((mixed, 2 * pairs), lambda k: (0, 0)),
            pl.BlockSpec((2 * pairs, block), lambda k: (0, k)),
            pl.BlockSpec((rows, block), lambda k: (0, k)),
        ],
        out_specs=(
            pl.BlockSpec((mixed, 2 * pairs), lambda k: (0, 0)),
            pl.BlockSpec((mixed, pairs), lambda k: (0, 0)),
        ),
        compiler_params=pltpu.CompilerParams(dimension_semantics=("arbitrary",)),
        cost_estimate=pl.CostEstimate(
            flops=2 * mixed * nlon * (2 * pairs + 3 * pairs),
            transcendentals=0,
            bytes_accessed=2 * pairs * nlon * 2 + rows * nlon * 4 + mixed * 4 * pairs * 3,
        ),
    )(lhs, tabs, tide_rows)
    folded = (hi_part[:, :pairs] + hi_part[:, pairs:] + lo_part) * (2.0 / nlon)
    folded = folded.T.reshape(pairs, items, lays, rows)
    return (folded[:slots], -folded[slots:])


def tendency(grid_values, advect, coriolis, depth_rows, tide_real, tide_imag):
    vort_re = grid_values[:, :, :, 0, :]
    vort_im = grid_values[:, :, :, 1, :]
    div_re = grid_values[:, :, :, 2, :]
    div_im = grid_values[:, :, :, 3, :]
    height_re = grid_values[:, :, :, 4, :]
    height_im = grid_values[:, :, :, 5, :]
    depth_b = depth_rows[None, None, :, :]
    parts = [
        advect * vort_im - coriolis * div_re,
        -advect * vort_re - coriolis * div_im,
        advect * div_im + coriolis * vort_re,
        -advect * div_re + coriolis * vort_im,
        advect * height_im - depth_b * div_re - tide_real,
        -advect * height_re - depth_b * div_im - tide_imag,
    ]
    return jnp.stack(parts, axis=3)


def implicit_step(explicit, wave_ids, mode_to_layer, layer_to_mode, mode_speed, ntrunc):
    degrees = wave_ids[:, None] + jnp.arange(explicit.shape[-1], dtype=jnp.int32)[None, :]
    degree_f = degrees.astype(jnp.float32)
    laplace = (degree_f * (degree_f + 1.0) / float(ntrunc * ntrunc))[:, None, None, None, :]
    speeds = mode_speed[None, None, :, None, None]
    div_modes = jnp.einsum(
        "pk,svkrj->svprj", layer_to_mode, explicit[:, :, :, 2:4, :], precision=HIGHEST_PRECISION
    )
    height_modes = jnp.einsum(
        "pk,svkrj->svprj", layer_to_mode, explicit[:, :, :, 4:6, :], precision=HIGHEST_PRECISION
    )
    div_new = (div_modes + laplace * speeds * height_modes) / (1.0 + laplace * speeds * speeds)
    height_new = height_modes - speeds * div_new
    div_layers = jnp.einsum("kp,svprj->svkrj", mode_to_layer, div_new, precision=HIGHEST_PRECISION)
    height_layers = jnp.einsum(
        "kp,svprj->svkrj", mode_to_layer, height_new, precision=HIGHEST_PRECISION
    )
    return jnp.concatenate([explicit[:, :, :, 0:2, :], div_layers, height_layers], axis=3)


def exchange_sum(parts, device_count):
    flat = jnp.concatenate([p.reshape(-1) for p in parts])
    rows = jnp.broadcast_to(flat[None, :], (device_count, flat.shape[0]))
    gathered = lax.all_to_all(rows, ("lat", "wave"), 0, 0, tiled=True)
    total = jnp.sum(gathered, axis=0)
    out, start = [], 0
    for p in parts:
        out.append(total[start:start + p.size].reshape(p.shape))
        start += p.size
    return tuple(out)


def to_bands(values, device_count, lanes=128):
    ls, vecs, lays, parts, nlat = values.shape
    band = nlat // device_count
    split = values.reshape(ls, vecs, lays, parts, device_count, band)
    split = jnp.transpose(split, (4, 0, 1, 2, 3, 5))
    return split.reshape(device_count, ls * vecs * lays * parts * band // lanes, lanes)


def on_device(
    arnoldi_block,
    legendre,
    wave_index,
    lat_index,
    quad_weight,
    zonal_flow,
    layer_depth,
    tide_height,
    mode_to_layer,
    layer_to_mode,
    mode_speed,
):
    local_slots = arnoldi_block.shape[0]
    vectors = arnoldi_block.shape[1]
    channels = arnoldi_block.shape[2]
    nlat = legendre.shape[1]
    ndeg = legendre.shape[2]
    ntrunc = ndeg - 1
    layers = mode_speed.shape[0]
    band_rows = tide_height.shape[0]
    device_count = lax.axis_size("lat") * lax.axis_size("wave")
    device_rank = lax.axis_index("lat") * lax.axis_size("wave") + lax.axis_index("wave")
    all_slots = wave_index.shape[0]
    axes = ("lat", "wave")
    local_waves = lax.dynamic_slice_in_dim(wave_index, device_rank * local_slots, local_slots)
    degrees = local_waves[:, None] + jnp.arange(ndeg, dtype=jnp.int32)[None, :]
    truncation = (degrees <= ntrunc).astype(jnp.float32)[:, None, None, :]
    basis = arnoldi_block * truncation
    tables = angle_tables(wave_index, tide_height.shape[1])
    tables_upper = tables.astype(jnp.bfloat16)
    tables_lower = (tables - tables_upper.astype(jnp.float32)).astype(jnp.bfloat16)
    coriolis = (2 * lat_index + 1).astype(jnp.float32) / nlat - 1.0
    advect = (
        local_waves.astype(jnp.float32)[:, None, None, None] * zonal_flow[None, None, :, :] / ntrunc
    )
    def one_step(step_index, spectral):
        spectral_b = spectral.astype(jnp.bfloat16)
        grid_b = jnp.einsum(
            "svcj,slj->svcl", spectral_b, legendre, preferred_element_type=jnp.float32
        ).astype(jnp.bfloat16)
        grid_split = grid_b.reshape(local_slots, vectors, layers, 6, nlat)
        sent = to_bands(grid_split[:, :, :, 2:4, :], device_count)
        received = lax.all_to_all(sent, axes, 0, 0, tiled=True)
        band_div = received.reshape(all_slots, vectors, layers, 2, band_rows)
        tide_real, tide_imag = tide_term(
            band_div[:, :, :, 0, :],
            band_div[:, :, :, 1, :],
            tide_height,
            tables_upper,
            tables_lower,
        )
        tide_parts = jnp.stack([tide_real, tide_imag], axis=3)
        back = tide_parts.reshape(device_count, -1, 128)
        returned = lax.all_to_all(back, axes, 0, 0, tiled=True)
        returned = returned.reshape(device_count, local_slots, vectors, layers, 2, band_rows)
        tide_rows = jnp.transpose(returned, (1, 2, 3, 4, 0, 5)).reshape(
            local_slots, vectors, layers, 2, nlat
        )
        tendencies = tendency(
            grid_split.astype(jnp.float32),
            advect,
            coriolis,
            layer_depth,
            tide_rows[:, :, :, 0, :],
            tide_rows[:, :, :, 1, :],
        )
        weighted = (
            (quad_weight * tendencies)
            .astype(jnp.bfloat16)
            .reshape(local_slots, vectors, channels, nlat)
        )
        analysed = jnp.einsum(
            "svcl,slj->svcj", weighted, legendre, preferred_element_type=jnp.float32
        )
        analysed = analysed * truncation
        explicit = (spectral + analysed).reshape(local_slots, vectors, layers, 6, ndeg)
        spectral = (
            implicit_step(
                explicit, local_waves, mode_to_layer, layer_to_mode, mode_speed, ntrunc
            ).reshape(local_slots, vectors, channels, ndeg)
            * truncation
        )
        return spectral

    spectral = lax.fori_loop(0, STEPS, one_step, basis)
    entries = float(local_slots * device_count * channels * ndeg)
    local_proj = jnp.sum(basis[:, :, None] * spectral[:, None, :], axis=(0, 3, 4))
    local_self = jnp.sum(spectral * spectral, axis=(0, 2, 3))
    local_gram = jnp.sum(basis[:, :, None] * basis[:, None, :], axis=(0, 3, 4))
    projection, self_sum, gram = exchange_sum((local_proj, local_self, local_gram), device_count)
    hessenberg = projection / entries
    residual = spectral - jnp.einsum(
        "skcj,kv->svcj", basis, hessenberg, precision=HIGHEST_PRECISION
    )
    quadratic = jnp.einsum("kv,kq,qv->v", hessenberg, gram, hessenberg, precision=HIGHEST_PRECISION)
    norm_sq = (self_sum - 2.0 * jnp.sum(hessenberg * projection, axis=0) + quadratic) / entries
    subdiagonal = jnp.sqrt(norm_sq + 1e-06)
    return (residual / subdiagonal[None, :, None, None], hessenberg, subdiagonal)


def solution(mesh):
    return jax.shard_map(
        on_device,
        mesh=mesh,
        in_specs=(
            P(("lat", "wave"), None, None, None),
            P(("lat", "wave"), None, None),
            P(),
            P(),
            P(),
            P(),
            P(),
            P(("lat", "wave"), None),
            P(),
            P(),
            P(),
        ),
        out_specs=(P(("lat", "wave"), None, None, None), P(), P()),
        check_vma=False,
    )
```

```python
import functools
import math

import jax
import jax.numpy as jnp
from jax import lax
from jax.sharding import PartitionSpec as P
from jax.experimental import pallas as pl
from jax.experimental.pallas import tpu as pltpu

STEPS = 3


HIGHEST_PRECISION = lax.Precision.HIGHEST


def angle_tables(wave_ids, nlon):
    lon_steps = jnp.arange(nlon, dtype=jnp.int32)
    phase = wave_ids[:, None] * lon_steps[None, :] % nlon
    theta = phase.astype(jnp.float32) * (2.0 * math.pi / nlon)
    return jnp.concatenate([jnp.cos(theta), jnp.sin(theta)], axis=0)


def tide_kernel(items, pairs, rows, lhs_ref, tab_ref, tide_ref, hi_ref, lo_ref):
    step = pl.program_id(0)

    @pl.when(step == 0)
    def _():
        hi_ref[...] = jnp.zeros_like(hi_ref)
        lo_ref[...] = jnp.zeros_like(lo_ref)

    field = jnp.dot(lhs_ref[...], tab_ref[...], preferred_element_type=jnp.float32)
    width = field.shape[1]
    product = (field.reshape(items, rows, width) * tide_ref[...][None, :, :]).reshape(
        items * rows, width
    )
    product_hi = product.astype(jnp.bfloat16)
    product_lo = (product - product_hi.astype(jnp.float32)).astype(jnp.bfloat16)
    last_dims = (((1,), (1,)), ((), ()))
    hi_ref[...] += lax.dot_general(
        product_hi, tab_ref[...], last_dims, preferred_element_type=jnp.float32
    )
    lo_ref[...] += lax.dot_general(
        product_lo, tab_ref[0:pairs, :], last_dims, preferred_element_type=jnp.float32
    )


def tide_term(div_real, div_imag, tide_rows, tables_upper, tables_lower):
    slots, items, lays, rows = div_real.shape
    nlon = tables_upper.shape[1]
    pairs = 2 * slots
    stacked = jnp.concatenate([div_real, -div_imag], axis=0).reshape(pairs, items * lays * rows)
    lhs = jnp.concatenate([stacked, stacked], axis=0).T
    tabs = jnp.concatenate([tables_upper, tables_lower], axis=0)
    block = 2048
    mixed = items * lays * rows
    hi_part, lo_part = pl.pallas_call(
        functools.partial(tide_kernel, items * lays, pairs, rows),
        out_shape=(
            jax.ShapeDtypeStruct((mixed, 2 * pairs), jnp.float32),
            jax.ShapeDtypeStruct((mixed, pairs), jnp.float32),
        ),
        grid=(nlon // block,),
        in_specs=[
            pl.BlockSpec((mixed, 2 * pairs), lambda k: (0, 0)),
            pl.BlockSpec((2 * pairs, block), lambda k: (0, k)),
            pl.BlockSpec((rows, block), lambda k: (0, k)),
        ],
        out_specs=(
            pl.BlockSpec((mixed, 2 * pairs), lambda k: (0, 0)),
            pl.BlockSpec((mixed, pairs), lambda k: (0, 0)),
        ),
        compiler_params=pltpu.CompilerParams(dimension_semantics=("arbitrary",)),
        cost_estimate=pl.CostEstimate(
            flops=2 * mixed * nlon * (2 * pairs + 3 * pairs),
            transcendentals=0,
            bytes_accessed=2 * pairs * nlon * 2 + rows * nlon * 4 + mixed * 4 * pairs * 3,
        ),
    )(lhs, tabs, tide_rows)
    folded = (hi_part[:, :pairs] + hi_part[:, pairs:] + lo_part) * (2.0 / nlon)
    folded = folded.T.reshape(pairs, items, lays, rows)
    return (folded[:slots], -folded[slots:])


def tendency(grid_values, advect, coriolis, depth_rows, tide_real, tide_imag):
    vort_re = grid_values[:, :, :, 0, :]
    vort_im = grid_values[:, :, :, 1, :]
    div_re = grid_values[:, :, :, 2, :]
    div_im = grid_values[:, :, :, 3, :]
    height_re = grid_values[:, :, :, 4, :]
    height_im = grid_values[:, :, :, 5, :]
    depth_b = depth_rows[None, None, :, :]
    parts = [
        advect * vort_im - coriolis * div_re,
        -advect * vort_re - coriolis * div_im,
        advect * div_im + coriolis * vort_re,
        -advect * div_re + coriolis * vort_im,
        advect * height_im - depth_b * div_re - tide_real,
        -advect * height_re - depth_b * div_im - tide_imag,
    ]
    return jnp.stack(parts, axis=3)


def implicit_step(explicit, wave_ids, mode_to_layer, layer_to_mode, mode_speed, ntrunc):
    degrees = wave_ids[:, None] + jnp.arange(explicit.shape[-1], dtype=jnp.int32)[None, :]
    degree_f = degrees.astype(jnp.float32)
    laplace = (degree_f * (degree_f + 1.0) / float(ntrunc * ntrunc))[:, None, None, None, :]
    speeds = mode_speed[None, None, :, None, None]
    div_modes = jnp.einsum(
        "pk,svkrj->svprj", layer_to_mode, explicit[:, :, :, 2:4, :], precision=HIGHEST_PRECISION
    )
    height_modes = jnp.einsum(
        "pk,svkrj->svprj", layer_to_mode, explicit[:, :, :, 4:6, :], precision=HIGHEST_PRECISION
    )
    div_new = (div_modes + laplace * speeds * height_modes) / (1.0 + laplace * speeds * speeds)
    height_new = height_modes - speeds * div_new
    div_layers = jnp.einsum("kp,svprj->svkrj", mode_to_layer, div_new, precision=HIGHEST_PRECISION)
    height_layers = jnp.einsum(
        "kp,svprj->svkrj", mode_to_layer, height_new, precision=HIGHEST_PRECISION
    )
    return jnp.concatenate([explicit[:, :, :, 0:2, :], div_layers, height_layers], axis=3)


def exchange_sum(parts, device_count):
    flat = jnp.concatenate([p.reshape(-1) for p in parts])
    rows = jnp.broadcast_to(flat[None, :], (device_count, flat.shape[0]))
    gathered = lax.all_to_all(rows, ("lat", "wave"), 0, 0, tiled=True)
    total = jnp.sum(gathered, axis=0)
    out, start = [], 0
    for p in parts:
        out.append(total[start:start + p.size].reshape(p.shape))
        start += p.size
    return tuple(out)


def to_bands(values, device_count, lanes=128):
    ls, vecs, lays, parts, nlat = values.shape
    band = nlat // device_count
    split = values.reshape(ls, vecs, lays, parts, device_count, band)
    split = jnp.transpose(split, (4, 0, 1, 2, 3, 5))
    return split.reshape(device_count, ls * vecs * lays * parts * band // lanes, lanes)


def on_device(
    arnoldi_block,
    legendre,
    wave_index,
    lat_index,
    quad_weight,
    zonal_flow,
    layer_depth,
    tide_height,
    mode_to_layer,
    layer_to_mode,
    mode_speed,
):
    local_slots = arnoldi_block.shape[0]
    vectors = arnoldi_block.shape[1]
    channels = arnoldi_block.shape[2]
    nlat = legendre.shape[1]
    ndeg = legendre.shape[2]
    ntrunc = ndeg - 1
    layers = mode_speed.shape[0]
    band_rows = tide_height.shape[0]
    device_count = lax.axis_size("lat") * lax.axis_size("wave")
    device_rank = lax.axis_index("lat") * lax.axis_size("wave") + lax.axis_index("wave")
    all_slots = wave_index.shape[0]
    axes = ("lat", "wave")
    local_waves = lax.dynamic_slice_in_dim(wave_index, device_rank * local_slots, local_slots)
    degrees = local_waves[:, None] + jnp.arange(ndeg, dtype=jnp.int32)[None, :]
    truncation = (degrees <= ntrunc).astype(jnp.float32)[:, None, None, :]
    basis = arnoldi_block * truncation
    tables = angle_tables(wave_index, tide_height.shape[1])
    tables_upper = tables.astype(jnp.bfloat16)
    tables_lower = (tables - tables_upper.astype(jnp.float32)).astype(jnp.bfloat16)
    coriolis = (2 * lat_index + 1).astype(jnp.float32) / nlat - 1.0
    advect = (
        local_waves.astype(jnp.float32)[:, None, None, None] * zonal_flow[None, None, :, :] / ntrunc
    )
    def synthesize(spectral):
        return jnp.einsum(
            "svcj,slj->svcl", spectral.astype(jnp.bfloat16), legendre,
            preferred_element_type=jnp.float32,
        ).astype(jnp.bfloat16)

    def advance(spectral, grid_b):
        grid_split = grid_b.reshape(local_slots, vectors, layers, 6, nlat)
        sent = to_bands(grid_split[:, :, :, 2:4, :], device_count)
        received = lax.all_to_all(sent, axes, 0, 0, tiled=True)
        band_div = received.reshape(all_slots, vectors, layers, 2, band_rows)
        tide_real, tide_imag = tide_term(
            band_div[:, :, :, 0, :],
            band_div[:, :, :, 1, :],
            tide_height,
            tables_upper,
            tables_lower,
        )
        tide_parts = jnp.stack([tide_real, tide_imag], axis=3)
        back = tide_parts.reshape(device_count, -1, 128)
        returned = lax.all_to_all(back, axes, 0, 0, tiled=True)
        returned = returned.reshape(device_count, local_slots, vectors, layers, 2, band_rows)
        tide_rows = jnp.transpose(returned, (1, 2, 3, 4, 0, 5)).reshape(
            local_slots, vectors, layers, 2, nlat
        )
        tendencies = tendency(
            grid_split.astype(jnp.float32),
            advect,
            coriolis,
            layer_depth,
            tide_rows[:, :, :, 0, :],
            tide_rows[:, :, :, 1, :],
        )
        weighted = (
            (quad_weight * tendencies)
            .astype(jnp.bfloat16)
            .reshape(local_slots, vectors, channels, nlat)
        )
        analysed = jnp.einsum(
            "svcl,slj->svcj", weighted, legendre, preferred_element_type=jnp.float32
        )
        analysed = analysed * truncation
        explicit = (spectral + analysed).reshape(local_slots, vectors, layers, 6, ndeg)
        spectral = (
            implicit_step(
                explicit, local_waves, mode_to_layer, layer_to_mode, mode_speed, ntrunc
            ).reshape(local_slots, vectors, channels, ndeg)
            * truncation
        )
        return spectral

    def rotated_step(step_index, carry):
        spectral = advance(*carry)
        return spectral, synthesize(spectral)

    carry = lax.fori_loop(0, STEPS - 1, rotated_step, (basis, synthesize(basis)))
    spectral = advance(*carry)
    entries = float(local_slots * device_count * channels * ndeg)
    local_proj = jnp.sum(basis[:, :, None] * spectral[:, None, :], axis=(0, 3, 4))
    local_self = jnp.sum(spectral * spectral, axis=(0, 2, 3))
    local_gram = jnp.sum(basis[:, :, None] * basis[:, None, :], axis=(0, 3, 4))
    projection, self_sum, gram = exchange_sum((local_proj, local_self, local_gram), device_count)
    hessenberg = projection / entries
    residual = spectral - jnp.einsum(
        "skcj,kv->svcj", basis, hessenberg, precision=HIGHEST_PRECISION
    )
    quadratic = jnp.einsum("kv,kq,qv->v", hessenberg, gram, hessenberg, precision=HIGHEST_PRECISION)
    norm_sq = (self_sum - 2.0 * jnp.sum(hessenberg * projection, axis=0) + quadratic) / entries
    subdiagonal = jnp.sqrt(norm_sq + 1e-06)
    return (residual / subdiagonal[None, :, None, None], hessenberg, subdiagonal)


def solution(mesh):
    return jax.shard_map(
        on_device,
        mesh=mesh,
        in_specs=(
            P(("lat", "wave"), None, None, None),
            P(("lat", "wave"), None, None),
            P(),
            P(),
            P(),
            P(),
            P(),
            P(("lat", "wave"), None),
            P(),
            P(),
            P(),
        ),
        out_specs=(P(("lat", "wave"), None, None, None), P(), P()),
        check_vma=False,
    )
```

```python
import functools
import math

import jax
import jax.numpy as jnp
from jax import lax
from jax.sharding import PartitionSpec as P
from jax.experimental import pallas as pl
from jax.experimental.pallas import tpu as pltpu

STEPS = 3


HIGHEST_PRECISION = lax.Precision.HIGHEST


def angle_tables(wave_ids, nlon):
    lon_steps = jnp.arange(nlon, dtype=jnp.int32)
    phase = wave_ids[:, None] * lon_steps[None, :] % nlon
    theta = phase.astype(jnp.float32) * (2.0 * math.pi / nlon)
    return jnp.concatenate([jnp.cos(theta), jnp.sin(theta)], axis=0)


def tide_kernel(items, pairs, rows, lhs_ref, tab_ref, tide_ref, hi_ref, lo_ref):
    step = pl.program_id(0)

    @pl.when(step == 0)
    def _():
        hi_ref[...] = jnp.zeros_like(hi_ref)
        lo_ref[...] = jnp.zeros_like(lo_ref)

    lhs = lhs_ref[...]
    field = jnp.dot(lhs, tab_ref[0:pairs, :], preferred_element_type=jnp.float32)
    field = field + jnp.dot(lhs, tab_ref[pairs:2 * pairs, :], preferred_element_type=jnp.float32)
    width = field.shape[1]
    product = (field.reshape(items, rows, width) * tide_ref[...][None, :, :]).reshape(
        items * rows, width
    )
    product_hi = product.astype(jnp.bfloat16)
    product_lo = (product - product_hi.astype(jnp.float32)).astype(jnp.bfloat16)
    last_dims = (((1,), (1,)), ((), ()))
    hi_ref[...] += lax.dot_general(
        product_hi, tab_ref[...], last_dims, preferred_element_type=jnp.float32
    )
    lo_ref[...] += lax.dot_general(
        product_lo, tab_ref[0:pairs, :], last_dims, preferred_element_type=jnp.float32
    )


def tide_term(div_real, div_imag, tide_rows, tables_upper, tables_lower):
    slots, items, lays, rows = div_real.shape
    nlon = tables_upper.shape[1]
    pairs = 2 * slots
    stacked = jnp.concatenate([div_real, -div_imag], axis=0).reshape(pairs, items * lays * rows)
    lhs = stacked.T
    tabs = jnp.concatenate([tables_upper, tables_lower], axis=0)
    block = 2048
    mixed = items * lays * rows
    hi_part, lo_part = pl.pallas_call(
        functools.partial(tide_kernel, items * lays, pairs, rows),
        out_shape=(
            jax.ShapeDtypeStruct((mixed, 2 * pairs), jnp.float32),
            jax.ShapeDtypeStruct((mixed, pairs), jnp.float32),
        ),
        grid=(nlon // block,),
        in_specs=[
            pl.BlockSpec((mixed, pairs), lambda k: (0, 0)),
            pl.BlockSpec((2 * pairs, block), lambda k: (0, k)),
            pl.BlockSpec((rows, block), lambda k: (0, k)),
        ],
        out_specs=(
            pl.BlockSpec((mixed, 2 * pairs), lambda k: (0, 0)),
            pl.BlockSpec((mixed, pairs), lambda k: (0, 0)),
        ),
        compiler_params=pltpu.CompilerParams(dimension_semantics=("arbitrary",)),
        cost_estimate=pl.CostEstimate(
            flops=2 * mixed * nlon * (2 * pairs + 3 * pairs),
            transcendentals=0,
            bytes_accessed=2 * pairs * nlon * 2 + rows * nlon * 4 + mixed * 4 * pairs * 3,
        ),
    )(lhs, tabs, tide_rows)
    folded = (hi_part[:, :pairs] + hi_part[:, pairs:] + lo_part) * (2.0 / nlon)
    folded = folded.T.reshape(pairs, items, lays, rows)
    return (folded[:slots], -folded[slots:])


def tendency(grid_values, advect, coriolis, depth_rows, tide_real, tide_imag):
    vort_re = grid_values[:, :, :, 0, :]
    vort_im = grid_values[:, :, :, 1, :]
    div_re = grid_values[:, :, :, 2, :]
    div_im = grid_values[:, :, :, 3, :]
    height_re = grid_values[:, :, :, 4, :]
    height_im = grid_values[:, :, :, 5, :]
    depth_b = depth_rows[None, None, :, :]
    parts = [
        advect * vort_im - coriolis * div_re,
        -advect * vort_re - coriolis * div_im,
        advect * div_im + coriolis * vort_re,
        -advect * div_re + coriolis * vort_im,
        advect * height_im - depth_b * div_re - tide_real,
        -advect * height_re - depth_b * div_im - tide_imag,
    ]
    return jnp.stack(parts, axis=3)


def implicit_step(explicit, wave_ids, mode_to_layer, layer_to_mode, mode_speed, ntrunc):
    degrees = wave_ids[:, None] + jnp.arange(explicit.shape[-1], dtype=jnp.int32)[None, :]
    degree_f = degrees.astype(jnp.float32)
    laplace = (degree_f * (degree_f + 1.0) / float(ntrunc * ntrunc))[:, None, None, None, :]
    speeds = mode_speed[None, None, :, None, None]
    div_modes = jnp.einsum(
        "pk,svkrj->svprj", layer_to_mode, explicit[:, :, :, 2:4, :], precision=HIGHEST_PRECISION
    )
    height_modes = jnp.einsum(
        "pk,svkrj->svprj", layer_to_mode, explicit[:, :, :, 4:6, :], precision=HIGHEST_PRECISION
    )
    div_new = (div_modes + laplace * speeds * height_modes) / (1.0 + laplace * speeds * speeds)
    height_new = height_modes - speeds * div_new
    div_layers = jnp.einsum("kp,svprj->svkrj", mode_to_layer, div_new, precision=HIGHEST_PRECISION)
    height_layers = jnp.einsum(
        "kp,svprj->svkrj", mode_to_layer, height_new, precision=HIGHEST_PRECISION
    )
    return jnp.concatenate([explicit[:, :, :, 0:2, :], div_layers, height_layers], axis=3)


def exchange_sum(parts, device_count):
    flat = jnp.concatenate([p.reshape(-1) for p in parts])
    rows = jnp.broadcast_to(flat[None, :], (device_count, flat.shape[0]))
    gathered = lax.all_to_all(rows, ("lat", "wave"), 0, 0, tiled=True)
    total = jnp.sum(gathered, axis=0)
    out, start = [], 0
    for p in parts:
        out.append(total[start:start + p.size].reshape(p.shape))
        start += p.size
    return tuple(out)


def to_bands(values, device_count, lanes=128):
    ls, vecs, lays, parts, nlat = values.shape
    band = nlat // device_count
    split = values.reshape(ls, vecs, lays, parts, device_count, band)
    split = jnp.transpose(split, (4, 0, 1, 2, 3, 5))
    return split.reshape(device_count, ls * vecs * lays * parts * band // lanes, lanes)


def on_device(
    arnoldi_block,
    legendre,
    wave_index,
    lat_index,
    quad_weight,
    zonal_flow,
    layer_depth,
    tide_height,
    mode_to_layer,
    layer_to_mode,
    mode_speed,
):
    local_slots = arnoldi_block.shape[0]
    vectors = arnoldi_block.shape[1]
    channels = arnoldi_block.shape[2]
    nlat = legendre.shape[1]
    ndeg = legendre.shape[2]
    ntrunc = ndeg - 1
    layers = mode_speed.shape[0]
    band_rows = tide_height.shape[0]
    device_count = lax.axis_size("lat") * lax.axis_size("wave")
    device_rank = lax.axis_index("lat") * lax.axis_size("wave") + lax.axis_index("wave")
    all_slots = wave_index.shape[0]
    axes = ("lat", "wave")
    local_waves = lax.dynamic_slice_in_dim(wave_index, device_rank * local_slots, local_slots)
    degrees = local_waves[:, None] + jnp.arange(ndeg, dtype=jnp.int32)[None, :]
    truncation = (degrees <= ntrunc).astype(jnp.float32)[:, None, None, :]
    basis = arnoldi_block * truncation
    tables = angle_tables(wave_index, tide_height.shape[1])
    tables_upper = tables.astype(jnp.bfloat16)
    tables_lower = (tables - tables_upper.astype(jnp.float32)).astype(jnp.bfloat16)
    coriolis = (2 * lat_index + 1).astype(jnp.float32) / nlat - 1.0
    advect = (
        local_waves.astype(jnp.float32)[:, None, None, None] * zonal_flow[None, None, :, :] / ntrunc
    )
    def one_step(step_index, spectral):
        spectral_b = spectral.astype(jnp.bfloat16)
        grid_b = jnp.einsum(
            "svcj,slj->svcl", spectral_b, legendre, preferred_element_type=jnp.float32
        ).astype(jnp.bfloat16)
        grid_split = grid_b.reshape(local_slots, vectors, layers, 6, nlat)
        sent = to_bands(grid_split[:, :, :, 2:4, :], device_count)
        received = lax.all_to_all(sent, axes, 0, 0, tiled=True)
        band_div = received.reshape(all_slots, vectors, layers, 2, band_rows)
        tide_real, tide_imag = tide_term(
            band_div[:, :, :, 0, :],
            band_div[:, :, :, 1, :],
            tide_height,
            tables_upper,
            tables_lower,
        )
        tide_parts = jnp.stack([tide_real, tide_imag], axis=3)
        back = tide_parts.reshape(device_count, -1, 128)
        returned = lax.all_to_all(back, axes, 0, 0, tiled=True)
        returned = returned.reshape(device_count, local_slots, vectors, layers, 2, band_rows)
        tide_rows = jnp.transpose(returned, (1, 2, 3, 4, 0, 5)).reshape(
            local_slots, vectors, layers, 2, nlat
        )
        tendencies = tendency(
            grid_split.astype(jnp.float32),
            advect,
            coriolis,
            layer_depth,
            tide_rows[:, :, :, 0, :],
            tide_rows[:, :, :, 1, :],
        )
        weighted = (
            (quad_weight * tendencies)
            .astype(jnp.bfloat16)
            .reshape(local_slots, vectors, channels, nlat)
        )
        analysed = jnp.einsum(
            "svcl,slj->svcj", weighted, legendre, preferred_element_type=jnp.float32
        )
        analysed = analysed * truncation
        explicit = (spectral + analysed).reshape(local_slots, vectors, layers, 6, ndeg)
        spectral = (
            implicit_step(
                explicit, local_waves, mode_to_layer, layer_to_mode, mode_speed, ntrunc
            ).reshape(local_slots, vectors, channels, ndeg)
            * truncation
        )
        return spectral

    spectral = lax.fori_loop(0, STEPS, one_step, basis)
    entries = float(local_slots * device_count * channels * ndeg)
    local_proj = jnp.sum(basis[:, :, None] * spectral[:, None, :], axis=(0, 3, 4))
    local_self = jnp.sum(spectral * spectral, axis=(0, 2, 3))
    local_gram = jnp.sum(basis[:, :, None] * basis[:, None, :], axis=(0, 3, 4))
    projection, self_sum, gram = exchange_sum((local_proj, local_self, local_gram), device_count)
    hessenberg = projection / entries
    residual = spectral - jnp.einsum(
        "skcj,kv->svcj", basis, hessenberg, precision=HIGHEST_PRECISION
    )
    quadratic = jnp.einsum("kv,kq,qv->v", hessenberg, gram, hessenberg, precision=HIGHEST_PRECISION)
    norm_sq = (self_sum - 2.0 * jnp.sum(hessenberg * projection, axis=0) + quadratic) / entries
    subdiagonal = jnp.sqrt(norm_sq + 1e-06)
    return (residual / subdiagonal[None, :, None, None], hessenberg, subdiagonal)


def solution(mesh):
    return jax.shard_map(
        on_device,
        mesh=mesh,
        in_specs=(
            P(("lat", "wave"), None, None, None),
            P(("lat", "wave"), None, None),
            P(),
            P(),
            P(),
            P(),
            P(),
            P(("lat", "wave"), None),
            P(),
            P(),
            P(),
        ),
        out_specs=(P(("lat", "wave"), None, None, None), P(), P()),
        check_vma=False,
    )
```

```python
import functools
import math

import jax
import jax.numpy as jnp
from jax import lax
from jax.sharding import PartitionSpec as P
from jax.experimental import pallas as pl
from jax.experimental.pallas import tpu as pltpu

STEPS = 3


HIGHEST_PRECISION = lax.Precision.HIGHEST


def angle_tables(wave_ids, nlon):
    lon_steps = jnp.arange(nlon, dtype=jnp.int32)
    phase = wave_ids[:, None] * lon_steps[None, :] % nlon
    theta = phase.astype(jnp.float32) * (2.0 * math.pi / nlon)
    return jnp.concatenate([jnp.cos(theta), jnp.sin(theta)], axis=0)


def tide_kernel(items, pairs, rows, lhs_ref, tab_ref, tide_ref, hi_ref, lo_ref):
    step = pl.program_id(0)

    @pl.when(step == 0)
    def _():
        hi_ref[...] = jnp.zeros_like(hi_ref)
        lo_ref[...] = jnp.zeros_like(lo_ref)

    field = jnp.dot(lhs_ref[...], tab_ref[...], preferred_element_type=jnp.float32)
    width = field.shape[1]
    product = (field.reshape(items, rows, width) * tide_ref[...][None, :, :]).reshape(
        items * rows, width
    )
    product_hi = product.astype(jnp.bfloat16)
    product_lo = (product - product_hi.astype(jnp.float32)).astype(jnp.bfloat16)
    last_dims = (((1,), (1,)), ((), ()))
    hi_ref[...] += lax.dot_general(
        product_hi, tab_ref[...], last_dims, preferred_element_type=jnp.float32
    )
    lo_ref[...] += lax.dot_general(
        product_lo, tab_ref[0:pairs, :], last_dims, preferred_element_type=jnp.float32
    )


def tide_term(div_real, div_imag, tide_rows, tables_upper, tables_lower):
    slots, items, lays, rows = div_real.shape
    nlon = tables_upper.shape[1]
    pairs = 2 * slots
    stacked = jnp.concatenate([div_real, -div_imag], axis=0).reshape(pairs, items * lays * rows)
    lhs = jnp.concatenate([stacked, stacked], axis=0).T
    tabs = jnp.concatenate([tables_upper, tables_lower], axis=0)
    block = 2048
    mixed = items * lays * rows
    hi_part, lo_part = pl.pallas_call(
        functools.partial(tide_kernel, items * lays, pairs, rows),
        out_shape=(
            jax.ShapeDtypeStruct((mixed, 2 * pairs), jnp.float32),
            jax.ShapeDtypeStruct((mixed, pairs), jnp.float32),
        ),
        grid=(nlon // block,),
        in_specs=[
            pl.BlockSpec((mixed, 2 * pairs), lambda k: (0, 0)),
            pl.BlockSpec((2 * pairs, block), lambda k: (0, k)),
            pl.BlockSpec((rows, block), lambda k: (0, k)),
        ],
        out_specs=(
            pl.BlockSpec((mixed, 2 * pairs), lambda k: (0, 0)),
            pl.BlockSpec((mixed, pairs), lambda k: (0, 0)),
        ),
        compiler_params=pltpu.CompilerParams(dimension_semantics=("arbitrary",)),
        cost_estimate=pl.CostEstimate(
            flops=2 * mixed * nlon * (2 * pairs + 3 * pairs),
            transcendentals=0,
            bytes_accessed=2 * pairs * nlon * 2 + rows * nlon * 4 + mixed * 4 * pairs * 3,
        ),
    )(lhs, tabs, tide_rows)
    folded = (hi_part[:, :pairs] + hi_part[:, pairs:] + lo_part) * (2.0 / nlon)
    folded = folded.T.reshape(pairs, items, lays, rows)
    return (folded[:slots], -folded[slots:])


def tendency(grid_values, advect, coriolis, depth_rows, tide_real, tide_imag):
    vort_re = grid_values[:, :, :, 0, :]
    vort_im = grid_values[:, :, :, 1, :]
    div_re = grid_values[:, :, :, 2, :]
    div_im = grid_values[:, :, :, 3, :]
    height_re = grid_values[:, :, :, 4, :]
    height_im = grid_values[:, :, :, 5, :]
    depth_b = depth_rows[None, None, :, :]
    parts = [
        advect * vort_im - coriolis * div_re,
        -advect * vort_re - coriolis * div_im,
        advect * div_im + coriolis * vort_re,
        -advect * div_re + coriolis * vort_im,
        advect * height_im - depth_b * div_re - tide_real,
        -advect * height_re - depth_b * div_im - tide_imag,
    ]
    return jnp.stack(parts, axis=3)


def implicit_step(explicit, wave_ids, mode_to_layer, layer_to_mode, mode_speed, ntrunc):
    degrees = wave_ids[:, None] + jnp.arange(explicit.shape[-1], dtype=jnp.int32)[None, :]
    degree_f = degrees.astype(jnp.float32)
    laplace = (degree_f * (degree_f + 1.0) / float(ntrunc * ntrunc))[:, None, None, None, :]
    speeds = mode_speed[None, None, :, None, None]
    div_modes = jnp.einsum(
        "pk,svkrj->svprj", layer_to_mode, explicit[:, :, :, 2:4, :], precision=lax.Precision.HIGH
    )
    height_modes = jnp.einsum(
        "pk,svkrj->svprj", layer_to_mode, explicit[:, :, :, 4:6, :], precision=lax.Precision.HIGH
    )
    div_new = (div_modes + laplace * speeds * height_modes) / (1.0 + laplace * speeds * speeds)
    height_new = height_modes - speeds * div_new
    div_layers = jnp.einsum("kp,svprj->svkrj", mode_to_layer, div_new, precision=lax.Precision.HIGH)
    height_layers = jnp.einsum(
        "kp,svprj->svkrj", mode_to_layer, height_new, precision=lax.Precision.HIGH
    )
    return jnp.concatenate([explicit[:, :, :, 0:2, :], div_layers, height_layers], axis=3)


def exchange_sum(parts, device_count):
    flat = jnp.concatenate([p.reshape(-1) for p in parts])
    rows = jnp.broadcast_to(flat[None, :], (device_count, flat.shape[0]))
    gathered = lax.all_to_all(rows, ("lat", "wave"), 0, 0, tiled=True)
    total = jnp.sum(gathered, axis=0)
    out, start = [], 0
    for p in parts:
        out.append(total[start:start + p.size].reshape(p.shape))
        start += p.size
    return tuple(out)


def to_bands(values, device_count, lanes=128):
    ls, vecs, lays, parts, nlat = values.shape
    band = nlat // device_count
    split = values.reshape(ls, vecs, lays, parts, device_count, band)
    split = jnp.transpose(split, (4, 0, 1, 2, 3, 5))
    return split.reshape(device_count, ls * vecs * lays * parts * band // lanes, lanes)


def on_device(
    arnoldi_block,
    legendre,
    wave_index,
    lat_index,
    quad_weight,
    zonal_flow,
    layer_depth,
    tide_height,
    mode_to_layer,
    layer_to_mode,
    mode_speed,
):
    local_slots = arnoldi_block.shape[0]
    vectors = arnoldi_block.shape[1]
    channels = arnoldi_block.shape[2]
    nlat = legendre.shape[1]
    ndeg = legendre.shape[2]
    ntrunc = ndeg - 1
    layers = mode_speed.shape[0]
    band_rows = tide_height.shape[0]
    device_count = lax.axis_size("lat") * lax.axis_size("wave")
    device_rank = lax.axis_index("lat") * lax.axis_size("wave") + lax.axis_index("wave")
    all_slots = wave_index.shape[0]
    axes = ("lat", "wave")
    local_waves = lax.dynamic_slice_in_dim(wave_index, device_rank * local_slots, local_slots)
    degrees = local_waves[:, None] + jnp.arange(ndeg, dtype=jnp.int32)[None, :]
    truncation = (degrees <= ntrunc).astype(jnp.float32)[:, None, None, :]
    basis = arnoldi_block * truncation
    tables = angle_tables(wave_index, tide_height.shape[1])
    tables_upper = tables.astype(jnp.bfloat16)
    tables_lower = (tables - tables_upper.astype(jnp.float32)).astype(jnp.bfloat16)
    coriolis = (2 * lat_index + 1).astype(jnp.float32) / nlat - 1.0
    advect = (
        local_waves.astype(jnp.float32)[:, None, None, None] * zonal_flow[None, None, :, :] / ntrunc
    )
    def one_step(step_index, spectral):
        spectral_b = spectral.astype(jnp.bfloat16)
        grid_b = jnp.einsum(
            "svcj,slj->svcl", spectral_b, legendre, preferred_element_type=jnp.float32
        ).astype(jnp.bfloat16)
        grid_split = grid_b.reshape(local_slots, vectors, layers, 6, nlat)
        sent = to_bands(grid_split[:, :, :, 2:4, :], device_count)
        received = lax.all_to_all(sent, axes, 0, 0, tiled=True)
        band_div = received.reshape(all_slots, vectors, layers, 2, band_rows)
        tide_real, tide_imag = tide_term(
            band_div[:, :, :, 0, :],
            band_div[:, :, :, 1, :],
            tide_height,
            tables_upper,
            tables_lower,
        )
        tide_parts = jnp.stack([tide_real, tide_imag], axis=3)
        back = tide_parts.reshape(device_count, -1, 128)
        returned = lax.all_to_all(back, axes, 0, 0, tiled=True)
        returned = returned.reshape(device_count, local_slots, vectors, layers, 2, band_rows)
        tide_rows = jnp.transpose(returned, (1, 2, 3, 4, 0, 5)).reshape(
            local_slots, vectors, layers, 2, nlat
        )
        tendencies = tendency(
            grid_split.astype(jnp.float32),
            advect,
            coriolis,
            layer_depth,
            tide_rows[:, :, :, 0, :],
            tide_rows[:, :, :, 1, :],
        )
        weighted = (
            (quad_weight * tendencies)
            .astype(jnp.bfloat16)
            .reshape(local_slots, vectors, channels, nlat)
        )
        analysed = jnp.einsum(
            "svcl,slj->svcj", weighted, legendre, preferred_element_type=jnp.float32
        )
        analysed = analysed * truncation
        explicit = (spectral + analysed).reshape(local_slots, vectors, layers, 6, ndeg)
        spectral = (
            implicit_step(
                explicit, local_waves, mode_to_layer, layer_to_mode, mode_speed, ntrunc
            ).reshape(local_slots, vectors, channels, ndeg)
            * truncation
        )
        return spectral

    spectral = lax.fori_loop(0, STEPS, one_step, basis)
    entries = float(local_slots * device_count * channels * ndeg)
    local_proj = jnp.sum(basis[:, :, None] * spectral[:, None, :], axis=(0, 3, 4))
    local_self = jnp.sum(spectral * spectral, axis=(0, 2, 3))
    local_gram = jnp.sum(basis[:, :, None] * basis[:, None, :], axis=(0, 3, 4))
    projection, self_sum, gram = exchange_sum((local_proj, local_self, local_gram), device_count)
    hessenberg = projection / entries
    residual = spectral - jnp.einsum(
        "skcj,kv->svcj", basis, hessenberg, precision=HIGHEST_PRECISION
    )
    quadratic = jnp.einsum("kv,kq,qv->v", hessenberg, gram, hessenberg, precision=HIGHEST_PRECISION)
    norm_sq = (self_sum - 2.0 * jnp.sum(hessenberg * projection, axis=0) + quadratic) / entries
    subdiagonal = jnp.sqrt(norm_sq + 1e-06)
    return (residual / subdiagonal[None, :, None, None], hessenberg, subdiagonal)


def solution(mesh):
    return jax.shard_map(
        on_device,
        mesh=mesh,
        in_specs=(
            P(("lat", "wave"), None, None, None),
            P(("lat", "wave"), None, None),
            P(),
            P(),
            P(),
            P(),
            P(),
            P(("lat", "wave"), None),
            P(),
            P(),
            P(),
        ),
        out_specs=(P(("lat", "wave"), None, None, None), P(), P()),
        check_vma=False,
    )
```

```python
import functools
import math

import jax
import jax.numpy as jnp
from jax import lax
from jax.sharding import PartitionSpec as P
from jax.experimental import pallas as pl
from jax.experimental.pallas import tpu as pltpu

STEPS = 3


HIGHEST_PRECISION = lax.Precision.HIGHEST


def angle_tables(wave_ids, nlon):
    lon_steps = jnp.arange(nlon, dtype=jnp.int32)
    phase = wave_ids[:, None] * lon_steps[None, :] % nlon
    theta = phase.astype(jnp.float32) * (2.0 * math.pi / nlon)
    return jnp.concatenate([jnp.cos(theta), jnp.sin(theta)], axis=0)


def tide_kernel(items, pairs, rows, lhs_ref, tab_ref, tide_ref, hi_ref, lo_ref):
    step = pl.program_id(0)

    @pl.when(step == 0)
    def _():
        hi_ref[...] = jnp.zeros_like(hi_ref)
        lo_ref[...] = jnp.zeros_like(lo_ref)

    field = jnp.dot(lhs_ref[...], tab_ref[...], preferred_element_type=jnp.float32)
    width = field.shape[1]
    product = (field.reshape(items, rows, width) * tide_ref[...][None, :, :]).reshape(
        items * rows, width
    )
    product_hi = product.astype(jnp.bfloat16)
    product_lo = (product - product_hi.astype(jnp.float32)).astype(jnp.bfloat16)
    last_dims = (((1,), (1,)), ((), ()))
    hi_ref[...] += lax.dot_general(
        product_hi, tab_ref[...], last_dims, preferred_element_type=jnp.float32
    )
    lo_ref[...] += lax.dot_general(
        product_lo, tab_ref[0:pairs, :], last_dims, preferred_element_type=jnp.float32
    )


def tide_term(div_real, div_imag, tide_rows, tables_upper, tables_lower):
    slots, items, lays, rows = div_real.shape
    nlon = tables_upper.shape[1]
    pairs = 2 * slots
    stacked = jnp.concatenate([div_real, -div_imag], axis=0).reshape(pairs, items * lays * rows)
    lhs = jnp.concatenate([stacked, stacked], axis=0).T
    tabs = jnp.concatenate([tables_upper, tables_lower], axis=0)
    block = 2048
    mixed = items * lays * rows
    hi_part, lo_part = pl.pallas_call(
        functools.partial(tide_kernel, items * lays, pairs, rows),
        out_shape=(
            jax.ShapeDtypeStruct((mixed, 2 * pairs), jnp.float32),
            jax.ShapeDtypeStruct((mixed, pairs), jnp.float32),
        ),
        grid=(nlon // block,),
        in_specs=[
            pl.BlockSpec((mixed, 2 * pairs), lambda k: (0, 0)),
            pl.BlockSpec((2 * pairs, block), lambda k: (0, k)),
            pl.BlockSpec((rows, block), lambda k: (0, k)),
        ],
        out_specs=(
            pl.BlockSpec((mixed, 2 * pairs), lambda k: (0, 0)),
            pl.BlockSpec((mixed, pairs), lambda k: (0, 0)),
        ),
        compiler_params=pltpu.CompilerParams(dimension_semantics=("arbitrary",)),
        cost_estimate=pl.CostEstimate(
            flops=2 * mixed * nlon * (2 * pairs + 3 * pairs),
            transcendentals=0,
            bytes_accessed=2 * pairs * nlon * 2 + rows * nlon * 4 + mixed * 4 * pairs * 3,
        ),
    )(lhs, tabs, tide_rows)
    folded = (hi_part[:, :pairs] + hi_part[:, pairs:] + lo_part) * (2.0 / nlon)
    folded = folded.T.reshape(pairs, items, lays, rows)
    return (folded[:slots], -folded[slots:])


def tendency(grid_values, advect, coriolis, depth_rows, tide_real, tide_imag):
    vort_re = grid_values[:, :, :, 0, :]
    vort_im = grid_values[:, :, :, 1, :]
    div_re = grid_values[:, :, :, 2, :]
    div_im = grid_values[:, :, :, 3, :]
    height_re = grid_values[:, :, :, 4, :]
    height_im = grid_values[:, :, :, 5, :]
    depth_b = depth_rows[None, None, :, :]
    parts = [
        advect * vort_im - coriolis * div_re,
        -advect * vort_re - coriolis * div_im,
        advect * div_im + coriolis * vort_re,
        -advect * div_re + coriolis * vort_im,
        advect * height_im - depth_b * div_re - tide_real,
        -advect * height_re - depth_b * div_im - tide_imag,
    ]
    return jnp.stack(parts, axis=3)


def implicit_step(explicit, wave_ids, mode_to_layer, layer_to_mode, mode_speed, ntrunc):
    degrees = wave_ids[:, None] + jnp.arange(explicit.shape[-1], dtype=jnp.int32)[None, :]
    degree_f = degrees.astype(jnp.float32)
    laplace = (degree_f * (degree_f + 1.0) / float(ntrunc * ntrunc))[:, None, None, None, :]
    speeds = mode_speed[None, None, :, None, None]
    div_modes = jnp.einsum(
        "pk,svkrj->svprj", layer_to_mode, explicit[:, :, :, 2:4, :], precision=lax.Precision.HIGH
    )
    height_modes = jnp.einsum(
        "pk,svkrj->svprj", layer_to_mode, explicit[:, :, :, 4:6, :], precision=lax.Precision.HIGH
    )
    div_new = (div_modes + laplace * speeds * height_modes) / (1.0 + laplace * speeds * speeds)
    height_new = height_modes - speeds * div_new
    div_layers = jnp.einsum("kp,svprj->svkrj", mode_to_layer, div_new, precision=lax.Precision.HIGH)
    height_layers = jnp.einsum(
        "kp,svprj->svkrj", mode_to_layer, height_new, precision=lax.Precision.HIGH
    )
    return jnp.concatenate([explicit[:, :, :, 0:2, :], div_layers, height_layers], axis=3)


def exchange_sum(parts, device_count):
    flat = jnp.concatenate([p.reshape(-1) for p in parts])
    rows = jnp.broadcast_to(flat[None, :], (device_count, flat.shape[0]))
    gathered = lax.all_to_all(rows, ("lat", "wave"), 0, 0, tiled=True)
    total = jnp.sum(gathered, axis=0)
    out, start = [], 0
    for p in parts:
        out.append(total[start:start + p.size].reshape(p.shape))
        start += p.size
    return tuple(out)


def to_bands(values, device_count, lanes=128):
    ls, vecs, lays, parts, nlat = values.shape
    band = nlat // device_count
    split = values.reshape(ls, vecs, lays, parts, device_count, band)
    split = jnp.transpose(split, (4, 0, 1, 2, 3, 5))
    return split.reshape(device_count, ls * vecs * lays * parts * band // lanes, lanes)


def on_device(
    arnoldi_block,
    legendre,
    wave_index,
    lat_index,
    quad_weight,
    zonal_flow,
    layer_depth,
    tide_height,
    mode_to_layer,
    layer_to_mode,
    mode_speed,
):
    local_slots = arnoldi_block.shape[0]
    vectors = arnoldi_block.shape[1]
    channels = arnoldi_block.shape[2]
    nlat = legendre.shape[1]
    ndeg = legendre.shape[2]
    ntrunc = ndeg - 1
    layers = mode_speed.shape[0]
    band_rows = tide_height.shape[0]
    device_count = lax.axis_size("lat") * lax.axis_size("wave")
    device_rank = lax.axis_index("lat") * lax.axis_size("wave") + lax.axis_index("wave")
    all_slots = wave_index.shape[0]
    axes = ("lat", "wave")
    local_waves = lax.dynamic_slice_in_dim(wave_index, device_rank * local_slots, local_slots)
    degrees = local_waves[:, None] + jnp.arange(ndeg, dtype=jnp.int32)[None, :]
    truncation = (degrees <= ntrunc).astype(jnp.float32)[:, None, None, :]
    basis = arnoldi_block * truncation
    coriolis = (2 * lat_index + 1).astype(jnp.float32) / nlat - 1.0
    advect = (
        local_waves.astype(jnp.float32)[:, None, None, None] * zonal_flow[None, None, :, :] / ntrunc
    )
    def one_step(step_index, spectral):
        step_waves, spectral = lax.optimization_barrier((wave_index, spectral))
        tables = angle_tables(step_waves, tide_height.shape[1])
        tables_upper = tables.astype(jnp.bfloat16)
        tables_lower = (tables - tables_upper.astype(jnp.float32)).astype(jnp.bfloat16)
        spectral_b = spectral.astype(jnp.bfloat16)
        grid_b = jnp.einsum(
            "svcj,slj->svcl", spectral_b, legendre, preferred_element_type=jnp.float32
        ).astype(jnp.bfloat16)
        grid_split = grid_b.reshape(local_slots, vectors, layers, 6, nlat)
        sent = to_bands(grid_split[:, :, :, 2:4, :], device_count)
        received = lax.all_to_all(sent, axes, 0, 0, tiled=True)
        band_div = received.reshape(all_slots, vectors, layers, 2, band_rows)
        tide_real, tide_imag = tide_term(
            band_div[:, :, :, 0, :],
            band_div[:, :, :, 1, :],
            tide_height,
            tables_upper,
            tables_lower,
        )
        tide_parts = jnp.stack([tide_real, tide_imag], axis=3)
        back = tide_parts.reshape(device_count, -1, 128)
        returned = lax.all_to_all(back, axes, 0, 0, tiled=True)
        returned = returned.reshape(device_count, local_slots, vectors, layers, 2, band_rows)
        tide_rows = jnp.transpose(returned, (1, 2, 3, 4, 0, 5)).reshape(
            local_slots, vectors, layers, 2, nlat
        )
        tendencies = tendency(
            grid_split.astype(jnp.float32),
            advect,
            coriolis,
            layer_depth,
            tide_rows[:, :, :, 0, :],
            tide_rows[:, :, :, 1, :],
        )
        weighted = (
            (quad_weight * tendencies)
            .astype(jnp.bfloat16)
            .reshape(local_slots, vectors, channels, nlat)
        )
        analysed = jnp.einsum(
            "svcl,slj->svcj", weighted, legendre, preferred_element_type=jnp.float32
        )
        analysed = analysed * truncation
        explicit = (spectral + analysed).reshape(local_slots, vectors, layers, 6, ndeg)
        spectral = (
            implicit_step(
                explicit, local_waves, mode_to_layer, layer_to_mode, mode_speed, ntrunc
            ).reshape(local_slots, vectors, channels, ndeg)
            * truncation
        )
        return spectral

    spectral = lax.fori_loop(0, STEPS, one_step, basis)
    entries = float(local_slots * device_count * channels * ndeg)
    local_proj = jnp.sum(basis[:, :, None] * spectral[:, None, :], axis=(0, 3, 4))
    local_self = jnp.sum(spectral * spectral, axis=(0, 2, 3))
    local_gram = jnp.sum(basis[:, :, None] * basis[:, None, :], axis=(0, 3, 4))
    projection, self_sum, gram = exchange_sum((local_proj, local_self, local_gram), device_count)
    hessenberg = projection / entries
    residual = spectral - jnp.einsum(
        "skcj,kv->svcj", basis, hessenberg, precision=HIGHEST_PRECISION
    )
    quadratic = jnp.einsum("kv,kq,qv->v", hessenberg, gram, hessenberg, precision=HIGHEST_PRECISION)
    norm_sq = (self_sum - 2.0 * jnp.sum(hessenberg * projection, axis=0) + quadratic) / entries
    subdiagonal = jnp.sqrt(norm_sq + 1e-06)
    return (residual / subdiagonal[None, :, None, None], hessenberg, subdiagonal)


def solution(mesh):
    return jax.shard_map(
        on_device,
        mesh=mesh,
        in_specs=(
            P(("lat", "wave"), None, None, None),
            P(("lat", "wave"), None, None),
            P(),
            P(),
            P(),
            P(),
            P(),
            P(("lat", "wave"), None),
            P(),
            P(),
            P(),
        ),
        out_specs=(P(("lat", "wave"), None, None, None), P(), P()),
        check_vma=False,
    )
```

```python
import functools
import math

import jax
import jax.numpy as jnp
from jax import lax
from jax.sharding import PartitionSpec as P
from jax.experimental import pallas as pl
from jax.experimental.pallas import tpu as pltpu

STEPS = 3


HIGHEST_PRECISION = lax.Precision.HIGHEST


def angle_tables(wave_ids, nlon):
    lon_steps = jnp.arange(nlon, dtype=jnp.int32)
    phase = wave_ids[:, None] * lon_steps[None, :] % nlon
    theta = phase.astype(jnp.float32) * (2.0 * math.pi / nlon)
    return jnp.concatenate([jnp.cos(theta), jnp.sin(theta)], axis=0)


def tide_kernel(items, pairs, rows, lhs_ref, tab_ref, tide_ref, hi_ref, lo_ref):
    step = pl.program_id(0)

    @pl.when(step == 0)
    def _():
        hi_ref[...] = jnp.zeros_like(hi_ref)
        lo_ref[...] = jnp.zeros_like(lo_ref)

    field = jnp.dot(lhs_ref[...], tab_ref[...], preferred_element_type=jnp.float32)
    width = field.shape[1]
    product = (field.reshape(items, rows, width) * tide_ref[...][None, :, :]).reshape(
        items * rows, width
    )
    product_hi = product.astype(jnp.bfloat16)
    product_lo = (product - product_hi.astype(jnp.float32)).astype(jnp.bfloat16)
    last_dims = (((1,), (1,)), ((), ()))
    hi_ref[...] += lax.dot_general(
        product_hi, tab_ref[...], last_dims, preferred_element_type=jnp.float32
    )
    lo_ref[...] += lax.dot_general(
        product_lo, tab_ref[0:pairs, :], last_dims, preferred_element_type=jnp.float32
    )


def tide_term(div_real, div_imag, tide_rows, tables_upper, tables_lower):
    slots, items, lays, rows = div_real.shape
    nlon = tables_upper.shape[1]
    pairs = 2 * slots
    stacked = jnp.concatenate([div_real, -div_imag], axis=0).reshape(pairs, items * lays * rows)
    lhs = jnp.concatenate([stacked, stacked], axis=0).T
    tabs = jnp.concatenate([tables_upper, tables_lower], axis=0)
    block = 2048
    mixed = items * lays * rows
    hi_part, lo_part = pl.pallas_call(
        functools.partial(tide_kernel, items * lays, pairs, rows),
        out_shape=(
            jax.ShapeDtypeStruct((mixed, 2 * pairs), jnp.float32),
            jax.ShapeDtypeStruct((mixed, pairs), jnp.float32),
        ),
        grid=(nlon // block,),
        in_specs=[
            pl.BlockSpec((mixed, 2 * pairs), lambda k: (0, 0)),
            pl.BlockSpec((2 * pairs, block), lambda k: (0, k)),
            pl.BlockSpec((rows, block), lambda k: (0, k)),
        ],
        out_specs=(
            pl.BlockSpec((mixed, 2 * pairs), lambda k: (0, 0)),
            pl.BlockSpec((mixed, pairs), lambda k: (0, 0)),
        ),
        compiler_params=pltpu.CompilerParams(dimension_semantics=("arbitrary",)),
        cost_estimate=pl.CostEstimate(
            flops=2 * mixed * nlon * (2 * pairs + 3 * pairs),
            transcendentals=0,
            bytes_accessed=2 * pairs * nlon * 2 + rows * nlon * 4 + mixed * 4 * pairs * 3,
        ),
    )(lhs, tabs, tide_rows)
    folded = (hi_part[:, :pairs] + hi_part[:, pairs:] + lo_part) * (2.0 / nlon)
    folded = folded.T.reshape(pairs, items, lays, rows)
    return (folded[:slots], -folded[slots:])


def tendency(grid_values, advect, coriolis, depth_rows, tide_real, tide_imag):
    vort_re = grid_values[:, :, :, 0, :]
    vort_im = grid_values[:, :, :, 1, :]
    div_re = grid_values[:, :, :, 2, :]
    div_im = grid_values[:, :, :, 3, :]
    height_re = grid_values[:, :, :, 4, :]
    height_im = grid_values[:, :, :, 5, :]
    depth_b = depth_rows[None, None, :, :]
    parts = [
        advect * vort_im - coriolis * div_re,
        -advect * vort_re - coriolis * div_im,
        advect * div_im + coriolis * vort_re,
        -advect * div_re + coriolis * vort_im,
        advect * height_im - depth_b * div_re - tide_real,
        -advect * height_re - depth_b * div_im - tide_imag,
    ]
    return jnp.stack(parts, axis=3)


def implicit_step(explicit, wave_ids, mode_to_layer, layer_to_mode, mode_speed, ntrunc):
    degrees = wave_ids[:, None] + jnp.arange(explicit.shape[-1], dtype=jnp.int32)[None, :]
    degree_f = degrees.astype(jnp.float32)
    laplace = (degree_f * (degree_f + 1.0) / float(ntrunc * ntrunc))[:, None, None, None, :]
    speeds = mode_speed[None, None, :, None, None]
    div_modes = jnp.einsum(
        "pk,svkrj->svprj", layer_to_mode, explicit[:, :, :, 2:4, :], precision=lax.Precision.HIGH
    )
    height_modes = jnp.einsum(
        "pk,svkrj->svprj", layer_to_mode, explicit[:, :, :, 4:6, :], precision=lax.Precision.HIGH
    )
    div_new = (div_modes + laplace * speeds * height_modes) / (1.0 + laplace * speeds * speeds)
    height_new = height_modes - speeds * div_new
    div_layers = jnp.einsum("kp,svprj->svkrj", mode_to_layer, div_new, precision=lax.Precision.HIGH)
    height_layers = jnp.einsum(
        "kp,svprj->svkrj", mode_to_layer, height_new, precision=lax.Precision.HIGH
    )
    return jnp.concatenate([explicit[:, :, :, 0:2, :], div_layers, height_layers], axis=3)


def exchange_sum(parts, device_count):
    flat = jnp.concatenate([p.reshape(-1) for p in parts])
    rows = jnp.broadcast_to(flat[None, :], (device_count, flat.shape[0]))
    gathered = lax.all_to_all(rows, ("lat", "wave"), 0, 0, tiled=True)
    total = jnp.sum(gathered, axis=0)
    out, start = [], 0
    for p in parts:
        out.append(total[start:start + p.size].reshape(p.shape))
        start += p.size
    return tuple(out)


def to_bands(values, device_count, lanes=128):
    ls, vecs, lays, parts, nlat = values.shape
    band = nlat // device_count
    split = values.reshape(ls, vecs, lays, parts, device_count, band)
    split = jnp.transpose(split, (4, 0, 1, 2, 3, 5))
    return split.reshape(device_count, ls * vecs * lays * parts * band // lanes, lanes)


def on_device(
    arnoldi_block,
    legendre,
    wave_index,
    lat_index,
    quad_weight,
    zonal_flow,
    layer_depth,
    tide_height,
    mode_to_layer,
    layer_to_mode,
    mode_speed,
):
    local_slots = arnoldi_block.shape[0]
    vectors = arnoldi_block.shape[1]
    channels = arnoldi_block.shape[2]
    nlat = legendre.shape[1]
    ndeg = legendre.shape[2]
    ntrunc = ndeg - 1
    layers = mode_speed.shape[0]
    band_rows = tide_height.shape[0]
    device_count = lax.axis_size("lat") * lax.axis_size("wave")
    device_rank = lax.axis_index("lat") * lax.axis_size("wave") + lax.axis_index("wave")
    all_slots = wave_index.shape[0]
    axes = ("lat", "wave")
    local_waves = lax.dynamic_slice_in_dim(wave_index, device_rank * local_slots, local_slots)
    degrees = local_waves[:, None] + jnp.arange(ndeg, dtype=jnp.int32)[None, :]
    truncation = (degrees <= ntrunc).astype(jnp.float32)[:, None, None, :]
    basis = arnoldi_block * truncation
    coriolis = (2 * lat_index + 1).astype(jnp.float32) / nlat - 1.0
    advect = (
        local_waves.astype(jnp.float32)[:, None, None, None] * zonal_flow[None, None, :, :] / ntrunc
    )
    def one_step(step_index, spectral):
        step_waves, spectral = lax.optimization_barrier((wave_index, spectral))
        tables = angle_tables(step_waves, tide_height.shape[1])
        tables_upper = tables.astype(jnp.bfloat16)
        tables_lower = (tables - tables_upper.astype(jnp.float32)).astype(jnp.bfloat16)
        spectral_b = spectral.astype(jnp.bfloat16)
        grid_b = jnp.einsum(
            "svcj,slj->svcl", spectral_b, legendre, preferred_element_type=jnp.float32
        ).astype(jnp.bfloat16)
        grid_split = grid_b.reshape(local_slots, vectors, layers, 6, nlat)
        sent = to_bands(grid_split[:, :, :, 2:4, :], device_count)
        received = lax.all_to_all(sent, axes, 0, 0, tiled=True)
        band_div = received.reshape(all_slots, vectors, layers, 2, band_rows)
        tide_real, tide_imag = tide_term(
            band_div[:, :, :, 0, :],
            band_div[:, :, :, 1, :],
            tide_height,
            tables_upper,
            tables_lower,
        )
        tide_parts = jnp.stack([tide_real, tide_imag], axis=3)
        back = tide_parts.reshape(device_count, -1, 128)
        returned = lax.all_to_all(back, axes, 0, 0, tiled=True)
        returned = returned.reshape(device_count, local_slots, vectors, layers, 2, band_rows)
        tide_rows = jnp.transpose(returned, (1, 2, 3, 4, 0, 5)).reshape(
            local_slots, vectors, layers, 2, nlat
        )
        tendencies = tendency(
            grid_split.astype(jnp.float32),
            advect,
            coriolis,
            layer_depth,
            tide_rows[:, :, :, 0, :],
            tide_rows[:, :, :, 1, :],
        )
        weighted = (
            (quad_weight * tendencies)
            .astype(jnp.bfloat16)
            .reshape(local_slots, vectors, channels, nlat)
        )
        analysed = jnp.einsum(
            "svcl,slj->svcj", weighted, legendre, preferred_element_type=jnp.float32
        )
        analysed = analysed * truncation
        explicit = (spectral + analysed).reshape(local_slots, vectors, layers, 6, ndeg)
        spectral = (
            implicit_step(
                explicit, local_waves, mode_to_layer, layer_to_mode, mode_speed, ntrunc
            ).reshape(local_slots, vectors, channels, ndeg)
            * truncation
        )
        return spectral

    spectral = lax.fori_loop(0, STEPS, one_step, basis)
    entries = float(local_slots * device_count * channels * ndeg)
    local_proj = jnp.sum(basis[:, :, None] * spectral[:, None, :], axis=(0, 3, 4))
    local_self = jnp.sum(spectral * spectral, axis=(0, 2, 3))
    local_gram = jnp.sum(basis[:, :, None] * basis[:, None, :], axis=(0, 3, 4))
    projection, self_sum, gram = exchange_sum((local_proj, local_self, local_gram), device_count)
    hessenberg = projection / entries
    residual = spectral - jnp.einsum(
        "skcj,kv->svcj", basis, hessenberg, precision=lax.Precision.HIGH
    )
    quadratic = jnp.einsum("kv,kq,qv->v", hessenberg, gram, hessenberg, precision=HIGHEST_PRECISION)
    norm_sq = (self_sum - 2.0 * jnp.sum(hessenberg * projection, axis=0) + quadratic) / entries
    subdiagonal = jnp.sqrt(norm_sq + 1e-06)
    return (residual / subdiagonal[None, :, None, None], hessenberg, subdiagonal)


def solution(mesh):
    return jax.shard_map(
        on_device,
        mesh=mesh,
        in_specs=(
            P(("lat", "wave"), None, None, None),
            P(("lat", "wave"), None, None),
            P(),
            P(),
            P(),
            P(),
            P(),
            P(("lat", "wave"), None),
            P(),
            P(),
            P(),
        ),
        out_specs=(P(("lat", "wave"), None, None, None), P(), P()),
        check_vma=False,
    )
```

```python
import functools
import math

import jax
import jax.numpy as jnp
from jax import lax
from jax.sharding import PartitionSpec as P
from jax.experimental import pallas as pl
from jax.experimental.pallas import tpu as pltpu

STEPS = 3


HIGHEST_PRECISION = lax.Precision.HIGHEST


def angle_tables(wave_ids, nlon):
    lon_steps = jnp.arange(nlon, dtype=jnp.int32)
    phase = wave_ids[:, None] * lon_steps[None, :] % nlon
    theta = phase.astype(jnp.float32) * (2.0 * math.pi / nlon)
    return jnp.concatenate([jnp.cos(theta), jnp.sin(theta)], axis=0)


def tide_kernel(items, pairs, rows, lhs_ref, tab_ref, tide_ref, hi_ref, lo_ref):
    step = pl.program_id(0)

    @pl.when(step == 0)
    def _():
        hi_ref[...] = jnp.zeros_like(hi_ref)
        lo_ref[...] = jnp.zeros_like(lo_ref)

    field = jnp.dot(lhs_ref[...], tab_ref[...], preferred_element_type=jnp.float32)
    width = field.shape[1]
    product = (field.reshape(items, rows, width) * tide_ref[...][None, :, :]).reshape(
        items * rows, width
    )
    product_hi = product.astype(jnp.bfloat16)
    product_lo = (product - product_hi.astype(jnp.float32)).astype(jnp.bfloat16)
    last_dims = (((1,), (1,)), ((), ()))
    hi_ref[...] += lax.dot_general(
        product_hi, tab_ref[...], last_dims, preferred_element_type=jnp.float32
    )
    lo_ref[...] += lax.dot_general(
        product_lo, tab_ref[0:pairs, :], last_dims, preferred_element_type=jnp.float32
    )


def tide_term(div_real, div_imag, tide_rows, tables_upper, tables_lower):
    slots, items, lays, rows = div_real.shape
    nlon = tables_upper.shape[1]
    pairs = 2 * slots
    stacked = jnp.concatenate([div_real, -div_imag], axis=0).reshape(pairs, items * lays * rows)
    lhs = jnp.concatenate([stacked, stacked], axis=0).T
    tabs = jnp.concatenate([tables_upper, tables_lower], axis=0)
    block = 2048
    mixed = items * lays * rows
    hi_part, lo_part = pl.pallas_call(
        functools.partial(tide_kernel, items * lays, pairs, rows),
        out_shape=(
            jax.ShapeDtypeStruct((mixed, 2 * pairs), jnp.float32),
            jax.ShapeDtypeStruct((mixed, pairs), jnp.float32),
        ),
        grid=(nlon // block,),
        in_specs=[
            pl.BlockSpec((mixed, 2 * pairs), lambda k: (0, 0)),
            pl.BlockSpec((2 * pairs, block), lambda k: (0, k)),
            pl.BlockSpec((rows, block), lambda k: (0, k)),
        ],
        out_specs=(
            pl.BlockSpec((mixed, 2 * pairs), lambda k: (0, 0)),
            pl.BlockSpec((mixed, pairs), lambda k: (0, 0)),
        ),
        compiler_params=pltpu.CompilerParams(dimension_semantics=("arbitrary",)),
        cost_estimate=pl.CostEstimate(
            flops=2 * mixed * nlon * (2 * pairs + 3 * pairs),
            transcendentals=0,
            bytes_accessed=2 * pairs * nlon * 2 + rows * nlon * 4 + mixed * 4 * pairs * 3,
        ),
    )(lhs, tabs, tide_rows)
    folded = (hi_part[:, :pairs] + hi_part[:, pairs:] + lo_part) * (2.0 / nlon)
    folded = folded.T.reshape(pairs, items, lays, rows)
    return (folded[:slots], -folded[slots:])


def tendency(grid_values, advect, coriolis, depth_rows, tide_real, tide_imag):
    vort_re = grid_values[:, :, :, 0, :]
    vort_im = grid_values[:, :, :, 1, :]
    div_re = grid_values[:, :, :, 2, :]
    div_im = grid_values[:, :, :, 3, :]
    height_re = grid_values[:, :, :, 4, :]
    height_im = grid_values[:, :, :, 5, :]
    depth_b = depth_rows[None, None, :, :]
    parts = [
        advect * vort_im - coriolis * div_re,
        -advect * vort_re - coriolis * div_im,
        advect * div_im + coriolis * vort_re,
        -advect * div_re + coriolis * vort_im,
        advect * height_im - depth_b * div_re - tide_real,
        -advect * height_re - depth_b * div_im - tide_imag,
    ]
    return jnp.stack(parts, axis=3)


def implicit_step(explicit, wave_ids, mode_to_layer, layer_to_mode, mode_speed, ntrunc):
    degrees = wave_ids[:, None] + jnp.arange(explicit.shape[-1], dtype=jnp.int32)[None, :]
    degree_f = degrees.astype(jnp.float32)
    laplace = (degree_f * (degree_f + 1.0) / float(ntrunc * ntrunc))[:, None, None, None, :]
    speeds = mode_speed[None, None, :, None, None]
    div_modes = jnp.einsum(
        "pk,svkrj->svprj", layer_to_mode, explicit[:, :, :, 2:4, :], precision=lax.Precision.HIGH
    )
    height_modes = jnp.einsum(
        "pk,svkrj->svprj", layer_to_mode, explicit[:, :, :, 4:6, :], precision=lax.Precision.HIGH
    )
    div_new = (div_modes + laplace * speeds * height_modes) / (1.0 + laplace * speeds * speeds)
    height_new = height_modes - speeds * div_new
    div_layers = jnp.einsum("kp,svprj->svkrj", mode_to_layer, div_new, precision=lax.Precision.HIGH)
    height_layers = jnp.einsum(
        "kp,svprj->svkrj", mode_to_layer, height_new, precision=lax.Precision.HIGH
    )
    return jnp.concatenate([explicit[:, :, :, 0:2, :], div_layers, height_layers], axis=3)


def exchange_sum(parts, device_count):
    flat = jnp.concatenate([p.reshape(-1) for p in parts])
    rows = jnp.broadcast_to(flat[None, :], (device_count, flat.shape[0]))
    gathered = lax.all_to_all(rows, ("lat", "wave"), 0, 0, tiled=True)
    total = jnp.sum(gathered, axis=0)
    out, start = [], 0
    for p in parts:
        out.append(total[start:start + p.size].reshape(p.shape))
        start += p.size
    return tuple(out)


def to_bands(values, device_count, lanes=128):
    ls, vecs, lays, parts, nlat = values.shape
    band = nlat // device_count
    split = values.reshape(ls, vecs, lays, parts, device_count, band)
    split = jnp.transpose(split, (4, 0, 1, 2, 3, 5))
    return split.reshape(device_count, ls * vecs * lays * parts * band // lanes, lanes)


def on_device(
    arnoldi_block,
    legendre,
    wave_index,
    lat_index,
    quad_weight,
    zonal_flow,
    layer_depth,
    tide_height,
    mode_to_layer,
    layer_to_mode,
    mode_speed,
):
    local_slots = arnoldi_block.shape[0]
    vectors = arnoldi_block.shape[1]
    channels = arnoldi_block.shape[2]
    nlat = legendre.shape[1]
    ndeg = legendre.shape[2]
    ntrunc = ndeg - 1
    layers = mode_speed.shape[0]
    band_rows = tide_height.shape[0]
    device_count = lax.axis_size("lat") * lax.axis_size("wave")
    device_rank = lax.axis_index("lat") * lax.axis_size("wave") + lax.axis_index("wave")
    all_slots = wave_index.shape[0]
    axes = ("lat", "wave")
    local_waves = lax.dynamic_slice_in_dim(wave_index, device_rank * local_slots, local_slots)
    degrees = local_waves[:, None] + jnp.arange(ndeg, dtype=jnp.int32)[None, :]
    truncation = (degrees <= ntrunc).astype(jnp.float32)[:, None, None, :]
    basis = arnoldi_block * truncation
    coriolis = (2 * lat_index + 1).astype(jnp.float32) / nlat - 1.0
    advect = (
        local_waves.astype(jnp.float32)[:, None, None, None] * zonal_flow[None, None, :, :] / ntrunc
    )
    def one_step(step_index, spectral):
        step_waves, spectral = lax.optimization_barrier((wave_index, spectral))
        tables = angle_tables(step_waves, tide_height.shape[1])
        tables_upper = tables.astype(jnp.bfloat16)
        tables_lower = (tables - tables_upper.astype(jnp.float32)).astype(jnp.bfloat16)
        spectral_b = spectral.astype(jnp.bfloat16)
        grid_b = jnp.einsum(
            "svcj,slj->svcl", spectral_b, legendre, preferred_element_type=jnp.float32
        ).astype(jnp.bfloat16)
        grid_split = grid_b.reshape(local_slots, vectors, layers, 6, nlat)
        sent = to_bands(grid_split[:, :, :, 2:4, :], device_count)
        received = lax.all_to_all(sent, axes, 0, 0, tiled=True)
        band_div = received.reshape(all_slots, vectors, layers, 2, band_rows)
        tide_real, tide_imag = tide_term(
            band_div[:, :, :, 0, :],
            band_div[:, :, :, 1, :],
            tide_height,
            tables_upper,
            tables_lower,
        )
        tide_parts = jnp.stack([tide_real, tide_imag], axis=3)
        back = tide_parts.reshape(device_count, -1, 128)
        returned = lax.all_to_all(back, axes, 0, 0, tiled=True)
        returned = returned.reshape(device_count, local_slots, vectors, layers, 2, band_rows)
        tide_rows = jnp.transpose(returned, (1, 2, 3, 4, 0, 5)).reshape(
            local_slots, vectors, layers, 2, nlat
        )
        tendencies = tendency(
            grid_split.astype(jnp.float32),
            advect,
            coriolis,
            layer_depth,
            tide_rows[:, :, :, 0, :],
            tide_rows[:, :, :, 1, :],
        )
        weighted = (
            (quad_weight * tendencies)
            .astype(jnp.bfloat16)
            .reshape(local_slots, vectors, channels, nlat)
        )
        analysed = jnp.einsum(
            "svcl,slj->svcj", weighted, legendre, preferred_element_type=jnp.float32
        )
        analysed = analysed * truncation
        explicit = (spectral + analysed).reshape(local_slots, vectors, layers, 6, ndeg)
        spectral = (
            implicit_step(
                explicit, local_waves, mode_to_layer, layer_to_mode, mode_speed, ntrunc
            ).reshape(local_slots, vectors, channels, ndeg)
            * truncation
        )
        return spectral

    spectral = lax.fori_loop(0, STEPS, one_step, basis)
    entries = float(local_slots * device_count * channels * ndeg)
    block_end, spectral = lax.optimization_barrier((arnoldi_block, spectral))
    basis = block_end * truncation
    local_proj = jnp.sum(basis[:, :, None] * spectral[:, None, :], axis=(0, 3, 4))
    local_self = jnp.sum(spectral * spectral, axis=(0, 2, 3))
    local_gram = jnp.sum(basis[:, :, None] * basis[:, None, :], axis=(0, 3, 4))
    projection, self_sum, gram = exchange_sum((local_proj, local_self, local_gram), device_count)
    hessenberg = projection / entries
    residual = spectral - jnp.einsum(
        "skcj,kv->svcj", basis, hessenberg, precision=HIGHEST_PRECISION
    )
    quadratic = jnp.einsum("kv,kq,qv->v", hessenberg, gram, hessenberg, precision=HIGHEST_PRECISION)
    norm_sq = (self_sum - 2.0 * jnp.sum(hessenberg * projection, axis=0) + quadratic) / entries
    subdiagonal = jnp.sqrt(norm_sq + 1e-06)
    return (residual / subdiagonal[None, :, None, None], hessenberg, subdiagonal)


def solution(mesh):
    return jax.shard_map(
        on_device,
        mesh=mesh,
        in_specs=(
            P(("lat", "wave"), None, None, None),
            P(("lat", "wave"), None, None),
            P(),
            P(),
            P(),
            P(),
            P(),
            P(("lat", "wave"), None),
            P(),
            P(),
            P(),
        ),
        out_specs=(P(("lat", "wave"), None, None, None), P(), P()),
        check_vma=False,
    )
```

```python
import functools
import math

import jax
import jax.numpy as jnp
from jax import lax
from jax.sharding import PartitionSpec as P
from jax.experimental import pallas as pl
from jax.experimental.pallas import tpu as pltpu

STEPS = 3


HIGHEST_PRECISION = lax.Precision.HIGHEST


def angle_tables(wave_ids, nlon):
    lon_steps = jnp.arange(nlon, dtype=jnp.int32)
    phase = wave_ids[:, None] * lon_steps[None, :] % nlon
    theta = phase.astype(jnp.float32) * (2.0 * math.pi / nlon)
    return jnp.concatenate([jnp.cos(theta), jnp.sin(theta)], axis=0)


def tide_kernel(items, pairs, rows, lhs_ref, tab_ref, tide_ref, hi_ref, lo_ref):
    step = pl.program_id(0)

    @pl.when(step == 0)
    def _():
        hi_ref[...] = jnp.zeros_like(hi_ref)
        lo_ref[...] = jnp.zeros_like(lo_ref)

    field = jnp.dot(lhs_ref[...], tab_ref[...], preferred_element_type=jnp.float32)
    width = field.shape[1]
    product = (field.reshape(items, rows, width) * tide_ref[...][None, :, :]).reshape(
        items * rows, width
    )
    product_hi = product.astype(jnp.bfloat16)
    product_lo = (product - product_hi.astype(jnp.float32)).astype(jnp.bfloat16)
    last_dims = (((1,), (1,)), ((), ()))
    hi_ref[...] += lax.dot_general(
        product_hi, tab_ref[...], last_dims, preferred_element_type=jnp.float32
    )
    lo_ref[...] += lax.dot_general(
        product_lo, tab_ref[0:pairs, :], last_dims, preferred_element_type=jnp.float32
    )


def tide_term(div_real, div_imag, tide_rows, tables_upper, tables_lower):
    slots, items, lays, rows = div_real.shape
    nlon = tables_upper.shape[1]
    pairs = 2 * slots
    stacked = jnp.concatenate([div_real, -div_imag], axis=0).reshape(pairs, items * lays * rows)
    lhs = jnp.concatenate([stacked, stacked], axis=0).T
    tabs = jnp.concatenate([tables_upper, tables_lower], axis=0)
    block = 2048
    mixed = items * lays * rows
    hi_part, lo_part = pl.pallas_call(
        functools.partial(tide_kernel, items * lays, pairs, rows),
        out_shape=(
            jax.ShapeDtypeStruct((mixed, 2 * pairs), jnp.float32),
            jax.ShapeDtypeStruct((mixed, pairs), jnp.float32),
        ),
        grid=(nlon // block,),
        in_specs=[
            pl.BlockSpec((mixed, 2 * pairs), lambda k: (0, 0)),
            pl.BlockSpec((2 * pairs, block), lambda k: (0, k)),
            pl.BlockSpec((rows, block), lambda k: (0, k)),
        ],
        out_specs=(
            pl.BlockSpec((mixed, 2 * pairs), lambda k: (0, 0)),
            pl.BlockSpec((mixed, pairs), lambda k: (0, 0)),
        ),
        compiler_params=pltpu.CompilerParams(dimension_semantics=("arbitrary",)),
        cost_estimate=pl.CostEstimate(
            flops=2 * mixed * nlon * (2 * pairs + 3 * pairs),
            transcendentals=0,
            bytes_accessed=2 * pairs * nlon * 2 + rows * nlon * 4 + mixed * 4 * pairs * 3,
        ),
    )(lhs, tabs, tide_rows)
    folded = (hi_part[:, :pairs] + hi_part[:, pairs:] + lo_part) * (2.0 / nlon)
    folded = folded.T.reshape(pairs, items, lays, rows)
    return (folded[:slots], -folded[slots:])


def tendency(grid_values, advect, coriolis, depth_rows, tide_real, tide_imag):
    vort_re = grid_values[:, :, :, 0, :]
    vort_im = grid_values[:, :, :, 1, :]
    div_re = grid_values[:, :, :, 2, :]
    div_im = grid_values[:, :, :, 3, :]
    height_re = grid_values[:, :, :, 4, :]
    height_im = grid_values[:, :, :, 5, :]
    depth_b = depth_rows[None, None, :, :]
    parts = [
        advect * vort_im - coriolis * div_re,
        -advect * vort_re - coriolis * div_im,
        advect * div_im + coriolis * vort_re,
        -advect * div_re + coriolis * vort_im,
        advect * height_im - depth_b * div_re - tide_real,
        -advect * height_re - depth_b * div_im - tide_imag,
    ]
    return jnp.stack(parts, axis=3)


def implicit_step(explicit, wave_ids, mode_to_layer, layer_to_mode, mode_speed, ntrunc):
    degrees = wave_ids[:, None] + jnp.arange(explicit.shape[-1], dtype=jnp.int32)[None, :]
    degree_f = degrees.astype(jnp.float32)
    laplace = (degree_f * (degree_f + 1.0) / float(ntrunc * ntrunc))[:, None, None, None, :]
    speeds = mode_speed[None, None, :, None, None]
    div_modes = jnp.einsum(
        "pk,svkrj->svprj", layer_to_mode, explicit[:, :, :, 2:4, :], precision=lax.Precision.HIGH
    )
    height_modes = jnp.einsum(
        "pk,svkrj->svprj", layer_to_mode, explicit[:, :, :, 4:6, :], precision=lax.Precision.HIGH
    )
    div_new = (div_modes + laplace * speeds * height_modes) / (1.0 + laplace * speeds * speeds)
    height_new = height_modes - speeds * div_new
    div_layers = jnp.einsum("kp,svprj->svkrj", mode_to_layer, div_new, precision=lax.Precision.HIGH)
    height_layers = jnp.einsum(
        "kp,svprj->svkrj", mode_to_layer, height_new, precision=lax.Precision.HIGH
    )
    return jnp.concatenate([explicit[:, :, :, 0:2, :], div_layers, height_layers], axis=3)


def exchange_sum(parts, device_count):
    flat = jnp.concatenate([p.reshape(-1) for p in parts])
    rows = jnp.broadcast_to(flat[None, :], (device_count, flat.shape[0]))
    gathered = lax.all_to_all(rows, ("lat", "wave"), 0, 0, tiled=True)
    total = jnp.sum(gathered, axis=0)
    out, start = [], 0
    for p in parts:
        out.append(total[start:start + p.size].reshape(p.shape))
        start += p.size
    return tuple(out)


def to_bands(values, device_count, lanes=128):
    ls, vecs, lays, parts, nlat = values.shape
    band = nlat // device_count
    split = values.reshape(ls, vecs, lays, parts, device_count, band)
    split = jnp.transpose(split, (4, 0, 1, 2, 3, 5))
    return split.reshape(device_count, ls * vecs * lays * parts * band // lanes, lanes)


def on_device(
    arnoldi_block,
    legendre,
    wave_index,
    lat_index,
    quad_weight,
    zonal_flow,
    layer_depth,
    tide_height,
    mode_to_layer,
    layer_to_mode,
    mode_speed,
):
    local_slots = arnoldi_block.shape[0]
    vectors = arnoldi_block.shape[1]
    channels = arnoldi_block.shape[2]
    nlat = legendre.shape[1]
    ndeg = legendre.shape[2]
    ntrunc = ndeg - 1
    layers = mode_speed.shape[0]
    band_rows = tide_height.shape[0]
    device_count = lax.axis_size("lat") * lax.axis_size("wave")
    device_rank = lax.axis_index("lat") * lax.axis_size("wave") + lax.axis_index("wave")
    all_slots = wave_index.shape[0]
    axes = ("lat", "wave")
    local_waves = lax.dynamic_slice_in_dim(wave_index, device_rank * local_slots, local_slots)
    degrees = local_waves[:, None] + jnp.arange(ndeg, dtype=jnp.int32)[None, :]
    truncation = (degrees <= ntrunc).astype(jnp.float32)[:, None, None, :]
    basis = arnoldi_block * truncation
    coriolis = (2 * lat_index + 1).astype(jnp.float32) / nlat - 1.0
    advect = (
        local_waves.astype(jnp.float32)[:, None, None, None] * zonal_flow[None, None, :, :] / ntrunc
    )
    def one_step(step_index, carry):
        spectral, _ = carry
        step_waves, step_basis, spectral = lax.optimization_barrier((wave_index, basis, spectral))
        step_gram = jnp.sum(step_basis[:, :, None] * step_basis[:, None, :], axis=(0, 3, 4))
        tables = angle_tables(step_waves, tide_height.shape[1])
        tables_upper = tables.astype(jnp.bfloat16)
        tables_lower = (tables - tables_upper.astype(jnp.float32)).astype(jnp.bfloat16)
        spectral_b = spectral.astype(jnp.bfloat16)
        grid_b = jnp.einsum(
            "svcj,slj->svcl", spectral_b, legendre, preferred_element_type=jnp.float32
        ).astype(jnp.bfloat16)
        grid_split = grid_b.reshape(local_slots, vectors, layers, 6, nlat)
        sent = to_bands(grid_split[:, :, :, 2:4, :], device_count)
        received = lax.all_to_all(sent, axes, 0, 0, tiled=True)
        band_div = received.reshape(all_slots, vectors, layers, 2, band_rows)
        tide_real, tide_imag = tide_term(
            band_div[:, :, :, 0, :],
            band_div[:, :, :, 1, :],
            tide_height,
            tables_upper,
            tables_lower,
        )
        tide_parts = jnp.stack([tide_real, tide_imag], axis=3)
        back = tide_parts.reshape(device_count, -1, 128)
        returned = lax.all_to_all(back, axes, 0, 0, tiled=True)
        returned = returned.reshape(device_count, local_slots, vectors, layers, 2, band_rows)
        tide_rows = jnp.transpose(returned, (1, 2, 3, 4, 0, 5)).reshape(
            local_slots, vectors, layers, 2, nlat
        )
        tendencies = tendency(
            grid_split.astype(jnp.float32),
            advect,
            coriolis,
            layer_depth,
            tide_rows[:, :, :, 0, :],
            tide_rows[:, :, :, 1, :],
        )
        weighted = (
            (quad_weight * tendencies)
            .astype(jnp.bfloat16)
            .reshape(local_slots, vectors, channels, nlat)
        )
        analysed = jnp.einsum(
            "svcl,slj->svcj", weighted, legendre, preferred_element_type=jnp.float32
        )
        analysed = analysed * truncation
        explicit = (spectral + analysed).reshape(local_slots, vectors, layers, 6, ndeg)
        spectral = (
            implicit_step(
                explicit, local_waves, mode_to_layer, layer_to_mode, mode_speed, ntrunc
            ).reshape(local_slots, vectors, channels, ndeg)
            * truncation
        )
        return spectral, step_gram

    gram_shape = jnp.zeros((vectors, vectors), jnp.float32)
    spectral, local_gram = lax.fori_loop(0, STEPS, one_step, (basis, gram_shape))
    entries = float(local_slots * device_count * channels * ndeg)
    local_proj = jnp.sum(basis[:, :, None] * spectral[:, None, :], axis=(0, 3, 4))
    local_self = jnp.sum(spectral * spectral, axis=(0, 2, 3))
    projection, self_sum, gram = exchange_sum((local_proj, local_self, local_gram), device_count)
    hessenberg = projection / entries
    residual = spectral - jnp.einsum(
        "skcj,kv->svcj", basis, hessenberg, precision=HIGHEST_PRECISION
    )
    quadratic = jnp.einsum("kv,kq,qv->v", hessenberg, gram, hessenberg, precision=HIGHEST_PRECISION)
    norm_sq = (self_sum - 2.0 * jnp.sum(hessenberg * projection, axis=0) + quadratic) / entries
    subdiagonal = jnp.sqrt(norm_sq + 1e-06)
    return (residual / subdiagonal[None, :, None, None], hessenberg, subdiagonal)


def solution(mesh):
    return jax.shard_map(
        on_device,
        mesh=mesh,
        in_specs=(
            P(("lat", "wave"), None, None, None),
            P(("lat", "wave"), None, None),
            P(),
            P(),
            P(),
            P(),
            P(),
            P(("lat", "wave"), None),
            P(),
            P(),
            P(),
        ),
        out_specs=(P(("lat", "wave"), None, None, None), P(), P()),
        check_vma=False,
    )
```
